32 devices in a mesh: section: 4 (over y, x), rep: 8 (over z, core).
Axes of the slice: x: 2, y: 2, z: 4, core: 2. Of those that a mesh axis runs over, the one named last changes fastest.
Arguments:
- clean_latents: bfloat16 [4, 1024, 320], P(None, 'rep'), may hold values from -40 to 40
- target_noise: bfloat16 [4, 1024, 320], P(None, 'rep'), may hold values from -6 to 6
- timesteps: int32 [8, 4], P('rep'), may hold values from 0 to 999
- layer_counts: int32 [4], P('section'), may hold values from 1 to 7, as said below
- section_weights: bfloat16 [4, 2560, 320], P('section'), may hold values from -0.3125 to 0.3125
Outputs:
- weight_grads: float32 [4, 2560, 320], P('section', 'rep')
The draws below stay inside these ranges and needn't reach their ends.
Inputs may be any that keep to these rules, and one draw needn't show every extreme that they name: `layer_counts`: the number of layer slots that section runs, from its first slot on; in every draw some section runs all 7 and some only one.
All inputs are finite; a program needn't handle non-finite values.
Results may differ from the reference program's by a relative error of at most 0.0012.
Values may be sent and summed in bfloat16 or wider, within the bound.
No kernel may reach another device: no remote copies, remote signals or barrier semaphores. Data moves between devices by JAX's collectives and lax.ppermute only.
A program may use at most 128 MiB of HBM per device.

```python
import math
import jax
import jax.numpy as jnp
from jax import lax

C = 320
SLOTS = 7
MB = 4
SECTIONS = 4
REPLICAS = 8
ROWS = 1024


def draw_clean_latents(key, part):
    key_base, key_rows, key_cols = jax.random.split(key, 3)
    row_level = jax.random.uniform(key_rows, (MB, ROWS, 1), jnp.float32, 0.0, math.log(10.0))
    col_level = jax.random.uniform(key_cols, (1, 1, C), jnp.float32, 0.0, math.log(10.0))
    magnitude = jnp.exp(0.5 * (row_level + col_level))
    result = jnp.clip(jax.random.normal(key_base, (MB, ROWS, C), jnp.float32), -4.0, 4.0) * magnitude
    return result.astype(jnp.bfloat16)


def draw_layer_counts(key, part):
    key_draw, key_order = jax.random.split(key)
    counts = jax.random.randint(key_draw, (SECTIONS,), 1, SLOTS + 1)
    ranking = jax.random.permutation(key_order, SECTIONS)
    counts = counts.at[ranking[0]].set(SLOTS)
    counts = counts.at[ranking[1]].set(1)
    return counts.astype(jnp.int32)


def touch_ends(entries, key, smallest, largest):
    dims = entries.shape
    index_at = [jax.random.randint(jax.random.fold_in(key, axis), (), 0, dims[axis]) for axis in range(len(dims))]
    entries = entries.at[tuple(index_at)].set(smallest)
    longest = dims.index(max(dims))
    index_at[longest] = (index_at[longest] + 1) % dims[longest]
    return entries.at[tuple(index_at)].set(largest)


def steps_of(rng, dims, cuts, low, largest):
    gain = 1.0
    for axis_at, parts in cuts:
        steps = jax.random.uniform(jax.random.fold_in(jax.random.fold_in(rng, 6), axis_at), (parts,), jnp.float32, low / len(cuts), largest / len(cuts))
        gain = gain * jnp.repeat(jnp.exp(steps), dims[axis_at] // parts).reshape((-1,) + (1,) * (len(dims) - 1 - axis_at))
    return gain


def scatter_about(key, dims, spread, most, pieces=(), kind=jnp.bfloat16):
    level = steps_of(key, dims, pieces, -0.22, 0.18) if pieces else 1.0
    entries = jax.random.normal(key, dims, jnp.float32) * spread * level
    return jnp.minimum(jnp.maximum(entries, -most), most).astype(kind)


def setup_inputs(seed: int = 0) -> dict:
    key_of = jax.random.split(jax.random.key(seed), 6)
    return {
        "clean_latents": draw_clean_latents(jax.random.fold_in(key_of[5], 71), 0),
        "target_noise": scatter_about(key_of[1], (MB, ROWS, C), 1.0, 6.0, ((1, 8),)),
        "timesteps": touch_ends(jax.random.randint(key_of[2], (REPLICAS, MB), 0, 1000), jax.random.fold_in(key_of[2], 1), 0, 999).astype(jnp.int32),
        "layer_counts": draw_layer_counts(jax.random.fold_in(key_of[5], 71), 0),
        "section_weights": scatter_about(key_of[4], (SECTIONS, (SLOTS + 1) * C, C), C ** -0.5, 0.3125, ((0, 4),)),
    }


EPSILON = 1e-06

def noise_level(step_values):
    phase = (step_values.astype(jnp.float32) / 1000.0 + 0.008) / 1.008 * (math.pi / 2.0)
    return jnp.cos(phase) ** 2

def time_features(step_values, channels):
    half_width = channels // 2
    ladder = jnp.exp(-math.log(10000.0) * jnp.arange(half_width, dtype=jnp.float32) / half_width)
    angles = step_values.astype(jnp.float32)[..., None] * ladder
    return jnp.concatenate([jnp.sin(angles), jnp.cos(angles)], axis=-1)

def pair_product(left, right):
    return jnp.einsum('brc,brd->cd', left.astype(jnp.float32), right.astype(jnp.float32), precision=lax.Precision.HIGHEST)

def times_transpose(left, weight):
    return lax.dot_general(left, weight, (((left.ndim - 1,), (1,)), ((), ())), preferred_element_type=jnp.float32)

def layer_forward(hidden, time_embed, weight):
    inverse_rms = lax.rsqrt(lax.optimization_barrier(jnp.mean(hidden * hidden, axis=-1, keepdims=True)) + EPSILON)
    activated = jax.nn.silu(hidden * inverse_rms + time_embed).astype(jnp.bfloat16)
    return hidden + jnp.dot(activated, weight, preferred_element_type=jnp.float32)

def layer_backward(hidden, time_embed, weight, grad_hidden):
    inverse_rms = lax.rsqrt(lax.optimization_barrier(jnp.mean(hidden * hidden, axis=-1, keepdims=True)) + EPSILON)
    normed = hidden * inverse_rms
    preact = normed + time_embed
    activated = jax.nn.silu(preact).astype(jnp.bfloat16)
    grad_low = grad_hidden.astype(jnp.bfloat16)
    weight_grad = pair_product(activated, grad_low)
    grad_act = times_transpose(grad_low, weight)
    sigmoid_val = jax.nn.sigmoid(preact)
    grad_pre = grad_act * sigmoid_val * (1.0 + preact * (1.0 - sigmoid_val))
    grad_in = grad_hidden + inverse_rms * (grad_pre - normed * lax.optimization_barrier(jnp.mean(grad_pre * normed, axis=-1, keepdims=True)))
    return (grad_in, weight_grad)

def apply_slot(hidden, time_embed, weight, enabled):

    def run_layer(current):
        return layer_forward(current, time_embed, weight)

    def keep_current(current):
        return current
    return lax.cond(enabled, run_layer, keep_current, hidden)

def slot_backward(hidden, time_embed, weight, grad_hidden, enabled):

    def run_back(operands):
        return layer_backward(operands[0], time_embed, weight, operands[1])

    def pass_back(operands):
        return (operands[1], jnp.zeros((weight.shape[0], weight.shape[1]), jnp.float32))
    return lax.cond(enabled, run_back, pass_back, (hidden, grad_hidden))

def section_hidden(section_in, skip_in, weights, time_embed, layer_count, channels, slot_count):
    side_weight = weights[slot_count * channels:]
    hidden = section_in.astype(jnp.float32)
    if skip_in is not None:
        hidden = hidden + jnp.dot(skip_in, side_weight, preferred_element_type=jnp.float32)
    layer_inputs = []
    for slot_index in range(slot_count):
        layer_inputs.append(hidden)
        weight = weights[slot_index * channels:(slot_index + 1) * channels]
        hidden = apply_slot(hidden, time_embed, weight, slot_index < layer_count)
    return (hidden, layer_inputs)

def section_backward(section_in, skip_in, weights, time_embed, layer_count, channels, slot_count, grad_out, grad_skip):
    hidden, layer_inputs = section_hidden(section_in, skip_in, weights, time_embed, layer_count, channels, slot_count)
    side_weight = weights[slot_count * channels:]
    section_out = hidden.astype(jnp.bfloat16)
    grad_hidden = grad_out.astype(jnp.float32)
    side_grad = None
    if grad_skip is not None:
        grad_hidden = grad_hidden + times_transpose(grad_skip, side_weight)
        side_grad = pair_product(section_out, grad_skip)
    slot_grads = [None] * slot_count
    for slot_index in reversed(range(slot_count)):
        weight = weights[slot_index * channels:(slot_index + 1) * channels]
        grad_hidden, slot_grads[slot_index] = slot_backward(layer_inputs[slot_index], time_embed, weight, grad_hidden, slot_index < layer_count)
    grad_low = grad_hidden.astype(jnp.bfloat16)
    grad_skip_in = None
    if skip_in is not None:
        side_grad = pair_product(skip_in, grad_low)
        grad_skip_in = times_transpose(grad_low, side_weight).astype(jnp.bfloat16)
    return (grad_low, grad_skip_in, jnp.concatenate(slot_grads + [side_grad], axis=0))

def reference(clean_latents, target_noise, timesteps, layer_counts, section_weights):
    micro_count, total_rows, channels = clean_latents.shape
    replica_count = timesteps.shape[0]
    row_count = total_rows // replica_count
    section_count = section_weights.shape[0]
    half_count = section_count // 2
    slot_count = section_weights.shape[1] // channels - 1
    batch_size = micro_count * replica_count
    clean = clean_latents.reshape(batch_size, row_count, channels)
    target = target_noise.reshape(batch_size, row_count, channels)
    step_values = timesteps.T.reshape(batch_size)
    signal_level = noise_level(step_values)[:, None, None]
    noisy_input = (jnp.sqrt(signal_level) * clean.astype(jnp.float32) + jnp.sqrt(1.0 - signal_level) * target.astype(jnp.float32)).astype(jnp.bfloat16)
    time_embed = time_features(step_values, channels)[:, None, :]
    section_inputs = []
    skip_outs = {}
    current = noisy_input
    for section in range(section_count):
        skip_in = skip_outs[section_count - 1 - section] if section >= half_count else None
        section_inputs.append(current)
        hidden, unused_inputs = section_hidden(current, skip_in, section_weights[section], time_embed, layer_counts[section], channels, slot_count)
        current = hidden.astype(jnp.bfloat16)
        if section < half_count:
            side_weight = section_weights[section][slot_count * channels:]
            skip_outs[section] = jnp.dot(current, side_weight, preferred_element_type=jnp.float32).astype(jnp.bfloat16)
    grad_out = ((current.astype(jnp.float32) - target.astype(jnp.float32)) / (micro_count * row_count)).astype(jnp.bfloat16)
    grad_skips = {}
    grad_rows = [None] * section_count
    for section in reversed(range(section_count)):
        is_decoder = section >= half_count
        skip_in = skip_outs[section_count - 1 - section] if is_decoder else None
        grad_skip = None if is_decoder else grad_skips[section_count - 1 - section]
        grad_out, grad_skip_in, section_grad = section_backward(section_inputs[section], skip_in, section_weights[section], time_embed, layer_counts[section], channels, slot_count, grad_out, grad_skip)
        if is_decoder:
            grad_skips[section] = grad_skip_in
        grad_rows[section] = section_grad
    return jnp.stack(grad_rows)
```

```python
import math

import jax
import jax.numpy as jnp
from jax import lax
from jax.sharding import PartitionSpec as P

EPSILON = 1e-06


def noise_level(step_values):
    phase = (step_values.astype(jnp.float32) / 1000.0 + 0.008) / 1.008 * (math.pi / 2.0)
    return jnp.cos(phase) ** 2


def time_features(step_values, channels):
    half_width = channels // 2
    ladder = jnp.exp(-math.log(10000.0) * jnp.arange(half_width, dtype=jnp.float32) / half_width)
    angles = step_values.astype(jnp.float32)[..., None] * ladder
    return jnp.concatenate([jnp.sin(angles), jnp.cos(angles)], axis=-1)


def pair_product(left, right):
    return lax.dot_general(
        left, right, (((0, 1), (0, 1)), ((), ())), preferred_element_type=jnp.float32
    )


def times_transpose(left, weight):
    return lax.dot_general(
        left, weight, (((left.ndim - 1,), (1,)), ((), ())), preferred_element_type=jnp.float32
    )


def layer_forward(hidden, time_embed, weight):
    inverse_rms = lax.rsqrt(jnp.mean(hidden * hidden, axis=-1, keepdims=True) + EPSILON)
    activated = jax.nn.silu(hidden * inverse_rms + time_embed).astype(jnp.bfloat16)
    return hidden + jnp.dot(activated, weight, preferred_element_type=jnp.float32)


def layer_backward(hidden, time_embed, weight, grad_hidden):
    inverse_rms = lax.rsqrt(jnp.mean(hidden * hidden, axis=-1, keepdims=True) + EPSILON)
    normed = hidden * inverse_rms
    preact = normed + time_embed
    activated = jax.nn.silu(preact).astype(jnp.bfloat16)
    grad_low = grad_hidden.astype(jnp.bfloat16)
    weight_grad = pair_product(activated, grad_low)
    grad_act = times_transpose(grad_low, weight)
    sigmoid_val = jax.nn.sigmoid(preact)
    grad_pre = grad_act * sigmoid_val * (1.0 + preact * (1.0 - sigmoid_val))
    grad_in = grad_hidden + inverse_rms * (
        grad_pre - normed * jnp.mean(grad_pre * normed, axis=-1, keepdims=True)
    )
    return (grad_in, weight_grad)


def section_hidden(section_in, skip_in, weights, time_embed, layer_count, slot_count, channels):
    side_weight = weights[slot_count * channels :]
    hidden = section_in.astype(jnp.float32)
    if skip_in is not None:
        hidden = hidden + jnp.dot(skip_in, side_weight, preferred_element_type=jnp.float32)
    layer_inputs = []
    for slot_index in range(slot_count):
        layer_inputs.append(hidden)
        weight = weights[slot_index * channels : (slot_index + 1) * channels]
        stepped = layer_forward(hidden, time_embed, weight)
        hidden = jnp.where(slot_index < layer_count, stepped, hidden)
    return (hidden, layer_inputs)


def section_forward(section_in, skip_in, weights, time_embed, layer_count, slot_count, channels):
    hidden, unused_inputs = section_hidden(
        section_in, skip_in, weights, time_embed, layer_count, slot_count, channels
    )
    section_out = hidden.astype(jnp.bfloat16)
    skip_out = None
    if skip_in is None:
        side_weight = weights[slot_count * channels :]
        skip_out = jnp.dot(section_out, side_weight, preferred_element_type=jnp.float32).astype(
            jnp.bfloat16
        )
    return (section_out, skip_out)


def section_backward(
    section_in, skip_in, weights, time_embed, layer_count, grad_out, grad_skip, slot_count, channels
):
    hidden, layer_inputs = section_hidden(
        section_in, skip_in, weights, time_embed, layer_count, slot_count, channels
    )
    side_weight = weights[slot_count * channels :]
    section_out = hidden.astype(jnp.bfloat16)
    grad_hidden = grad_out.astype(jnp.float32)
    side_grad = None
    if grad_skip is not None:
        grad_hidden = grad_hidden + times_transpose(grad_skip, side_weight)
        side_grad = pair_product(section_out, grad_skip)
    slot_grads = [None] * slot_count
    for slot_index in reversed(range(slot_count)):
        weight = weights[slot_index * channels : (slot_index + 1) * channels]
        stepped, weight_grad = layer_backward(
            layer_inputs[slot_index], time_embed, weight, grad_hidden
        )
        enabled = slot_index < layer_count
        grad_hidden = jnp.where(enabled, stepped, grad_hidden)
        slot_grads[slot_index] = jnp.where(enabled, weight_grad, jnp.zeros_like(weight_grad))
    grad_low = grad_hidden.astype(jnp.bfloat16)
    grad_skip_in = None
    if skip_in is not None:
        side_grad = pair_product(skip_in, grad_low)
        grad_skip_in = times_transpose(grad_low, side_weight).astype(jnp.bfloat16)
    return (grad_low, grad_skip_in, jnp.concatenate(slot_grads + [side_grad], axis=0))


def on_device(clean_latents, target_noise, timesteps, layer_counts, section_weights):
    section_count = lax.axis_size("section")
    half_count = section_count // 2
    section_index = lax.axis_index("section")
    micro_count, row_count, channels = clean_latents.shape
    weights = section_weights[0]
    slot_count = weights.shape[0] // channels - 1
    layer_count = layer_counts[0]
    step_values = timesteps[0]
    signal_level = noise_level(step_values)[:, None, None]
    noisy_input = (
        jnp.sqrt(signal_level) * clean_latents.astype(jnp.float32)
        + jnp.sqrt(1.0 - signal_level) * target_noise.astype(jnp.float32)
    ).astype(jnp.bfloat16)
    time_embed = time_features(step_values, channels)[:, None, :]
    mirror_pairs_fwd = [(i, section_count - 1 - i) for i in range(half_count)]
    mirror_pairs_bwd = [(section_count - 1 - i, i) for i in range(half_count)]

    current = noisy_input
    saved_in = noisy_input
    my_skip = jnp.zeros_like(noisy_input)
    skip_box = None
    final_out = None
    for stage in range(section_count):
        is_decoder = stage >= half_count
        section_out, skip_out = section_forward(
            current,
            skip_box if is_decoder else None,
            weights,
            time_embed,
            layer_count,
            slot_count,
            channels,
        )
        if not is_decoder:
            my_skip = jnp.where(section_index == stage, skip_out, my_skip)
        if stage == half_count - 1:
            skip_box = lax.ppermute(my_skip, "section", mirror_pairs_fwd)
        if stage < section_count - 1:
            current = lax.ppermute(section_out, "section", [(stage, stage + 1)])
            saved_in = jnp.where(section_index == stage + 1, current, saved_in)
        else:
            final_out = section_out

    grad_current = (
        (final_out.astype(jnp.float32) - target_noise.astype(jnp.float32))
        / (micro_count * row_count)
    ).astype(jnp.bfloat16)
    my_e = jnp.zeros_like(noisy_input)
    e_box = None
    weight_grads = None
    for stage in reversed(range(section_count)):
        is_decoder = stage >= half_count
        grad_low, grad_skip_in, section_grad = section_backward(
            saved_in,
            skip_box if is_decoder else None,
            weights,
            time_embed,
            layer_count,
            grad_current,
            None if is_decoder else e_box,
            slot_count,
            channels,
        )
        if weight_grads is None:
            weight_grads = section_grad
        else:
            weight_grads = jnp.where(section_index == stage, section_grad, weight_grads)
        if is_decoder:
            my_e = jnp.where(section_index == stage, grad_skip_in, my_e)
        if stage == half_count:
            e_box = lax.ppermute(my_e, "section", mirror_pairs_bwd)
        if stage > 0:
            grad_current = lax.ppermute(grad_low, "section", [(stage, stage - 1)])

    reduced = lax.psum_scatter(weight_grads, "rep", scatter_dimension=0, tiled=True)
    return reduced[None]


def solution(mesh):
    placed = (
        P(None, "rep", None),
        P(None, "rep", None),
        P("rep", None),
        P("section"),
        P("section", None, None),
    )
    return jax.shard_map(
        on_device, mesh=mesh, in_specs=placed, out_specs=P("section", "rep", None), check_vma=False
    )
```

```python
import functools
import math

import jax
import jax.numpy as jnp
from jax import lax
from jax.experimental import pallas as pl
from jax.experimental.pallas import tpu as pltpu
from jax.sharding import PartitionSpec as P

EPSILON = 1e-06
F32 = jnp.float32
BF16 = jnp.bfloat16


def noise_level(step_values):
    phase = (step_values.astype(jnp.float32) / 1000.0 + 0.008) / 1.008 * (math.pi / 2.0)
    return jnp.cos(phase) ** 2


def time_features(step_values, channels):
    half_width = channels // 2
    ladder = jnp.exp(-math.log(10000.0) * jnp.arange(half_width, dtype=jnp.float32) / half_width)
    angles = step_values.astype(jnp.float32)[..., None] * ladder
    return jnp.concatenate([jnp.sin(angles), jnp.cos(angles)], axis=-1)


def contract_rows(left, right):
    return lax.dot_general(left, right, (((0,), (0,)), ((), ())), preferred_element_type=F32)


def contract_cols(left, right):
    return lax.dot_general(left, right, (((1,), (1,)), ((), ())), preferred_element_type=F32)


def plain_product(left, right):
    return lax.dot_general(left, right, (((1,), (0,)), ((), ())), preferred_element_type=F32)


def sigmoid(value):
    return 1.0 / (1.0 + jnp.exp(-value))


def inverse_rms_of(hidden):
    return lax.rsqrt(jnp.mean(hidden * hidden, axis=-1, keepdims=True) + EPSILON)


def run_forward_slots(h_ref, te, w_ref, count, slot_count, channels, store_ref=None):
    for slot_index in range(slot_count):

        @pl.when(slot_index < count)
        def _():
            hidden = h_ref[...]
            if store_ref is not None:
                store_ref[slot_index] = hidden
            preact = hidden * inverse_rms_of(hidden) + te
            activated = (preact * sigmoid(preact)).astype(BF16)
            weight = w_ref[slot_index * channels : (slot_index + 1) * channels, :]
            h_ref[...] = hidden + plain_product(activated, weight)


def forward_kernel(
    flags_ref, a_ref, te_ref, w_ref, skip_ref, skip_acc_ref, out_ref, skip_out_ref,
    h_ref, skip_scr, sem, *, decoder, slot_count, channels
):
    count = flags_ref[0]
    active = flags_ref[1]

    @pl.when(active == 1)
    def _():
        side = w_ref[slot_count * channels :, :]
        hidden = a_ref[...].astype(F32)
        if decoder:
            hidden = hidden + plain_product(skip_ref[...], side)
        h_ref[...] = hidden
        run_forward_slots(h_ref, te_ref[...], w_ref, count, slot_count, channels)
        section_out = h_ref[...].astype(BF16)
        out_ref[...] = section_out
        if not decoder:
            skip_scr[...] = plain_product(section_out, side).astype(BF16)
            copy = pltpu.make_async_copy(skip_scr, skip_out_ref, sem)
            copy.start()
            copy.wait()


def backward_kernel(
    flags_ref, a_ref, te_ref, w_ref, skip_ref, g_ref, e_ref, e_acc_ref, grads_acc_ref,
    gprev_ref, e_out_ref, grads_out_ref,
    h_ref, hs_ref, gh_ref, grads_scr, e_scr, sems, *, decoder, slot_count, channels
):
    count = flags_ref[0]
    active = flags_ref[1]

    @pl.when(active == 1)
    def _():
        side = w_ref[slot_count * channels :, :]
        te = te_ref[...]
        hidden = a_ref[...].astype(F32)
        if decoder:
            hidden = hidden + plain_product(skip_ref[...], side)
        h_ref[...] = hidden
        run_forward_slots(h_ref, te, w_ref, count, slot_count, channels, store_ref=hs_ref)
        grad_hidden = g_ref[...].astype(F32)
        if not decoder:
            grad_skip = e_ref[...]
            grad_hidden = grad_hidden + contract_cols(grad_skip, side)
            section_out = h_ref[...].astype(BF16)
            grads_scr[slot_count * channels :, :] = contract_rows(section_out, grad_skip)
        gh_ref[...] = grad_hidden
        for slot_index in reversed(range(slot_count)):
            rows = slice(slot_index * channels, (slot_index + 1) * channels)

            @pl.when(slot_index < count)
            def _():
                hidden = hs_ref[slot_index]
                inverse_rms = inverse_rms_of(hidden)
                normed = hidden * inverse_rms
                preact = normed + te
                sigmoid_val = sigmoid(preact)
                activated = (preact * sigmoid_val).astype(BF16)
                grad_hidden = gh_ref[...]
                grad_low = grad_hidden.astype(BF16)
                grads_scr[rows, :] = contract_rows(activated, grad_low)
                grad_act = contract_cols(grad_low, w_ref[rows, :])
                grad_pre = grad_act * sigmoid_val * (1.0 + preact * (1.0 - sigmoid_val))
                gh_ref[...] = grad_hidden + inverse_rms * (
                    grad_pre - normed * jnp.mean(grad_pre * normed, axis=-1, keepdims=True)
                )

            @pl.when(slot_index >= count)
            def _():
                grads_scr[rows, :] = jnp.zeros((channels, channels), F32)

        grad_low = gh_ref[...].astype(BF16)
        gprev_ref[...] = grad_low
        if decoder:
            grads_scr[slot_count * channels :, :] = contract_rows(skip_ref[...], grad_low)
            e_scr[...] = contract_cols(grad_low, side).astype(BF16)
            e_copy = pltpu.make_async_copy(e_scr, e_out_ref, sems.at[1])
            e_copy.start()
        grads_copy = pltpu.make_async_copy(grads_scr, grads_out_ref, sems.at[0])
        grads_copy.start()
        grads_copy.wait()
        if decoder:
            e_copy.wait()


VMEM_SPEC = pl.BlockSpec(memory_space=pltpu.VMEM)
SMEM_SPEC = pl.BlockSpec(memory_space=pltpu.SMEM)
ANY_SPEC = pl.BlockSpec(memory_space=pl.ANY)
PARAMS = pltpu.CompilerParams(vmem_limit_bytes=48 * 1024 * 1024)


def stage_forward(flags, a, te, weights, skip_in, skip_acc, decoder, slot_count, channels):
    rows = a.shape[0]
    kernel = functools.partial(
        forward_kernel, decoder=decoder, slot_count=slot_count, channels=channels
    )
    return pl.pallas_call(
        kernel,
        out_shape=(
            jax.ShapeDtypeStruct((rows, channels), BF16),
            jax.ShapeDtypeStruct((rows, channels), BF16),
        ),
        in_specs=[SMEM_SPEC, VMEM_SPEC, VMEM_SPEC, VMEM_SPEC, VMEM_SPEC, ANY_SPEC],
        out_specs=(VMEM_SPEC, ANY_SPEC),
        scratch_shapes=[
            pltpu.VMEM((rows, channels), F32),
            pltpu.VMEM((rows, channels), BF16),
            pltpu.SemaphoreType.DMA(()),
        ],
        input_output_aliases={5: 1},
        compiler_params=PARAMS,
    )(flags, a, te, weights, skip_in, skip_acc)


def stage_backward(
    flags, a, te, weights, skip_in, grad_out, grad_skip, e_acc, grads_acc, decoder,
    slot_count, channels
):
    rows = a.shape[0]
    kernel = functools.partial(
        backward_kernel, decoder=decoder, slot_count=slot_count, channels=channels
    )
    return pl.pallas_call(
        kernel,
        out_shape=(
            jax.ShapeDtypeStruct((rows, channels), BF16),
            jax.ShapeDtypeStruct((rows, channels), BF16),
            jax.ShapeDtypeStruct(grads_acc.shape, F32),
        ),
        in_specs=[SMEM_SPEC] + [VMEM_SPEC] * 6 + [ANY_SPEC, ANY_SPEC],
        out_specs=(VMEM_SPEC, ANY_SPEC, ANY_SPEC),
        scratch_shapes=[
            pltpu.VMEM((rows, channels), F32),
            pltpu.VMEM((slot_count, rows, channels), F32),
            pltpu.VMEM((rows, channels), F32),
            pltpu.VMEM(grads_acc.shape, F32),
            pltpu.VMEM((rows, channels), BF16),
            pltpu.SemaphoreType.DMA((2,)),
        ],
        input_output_aliases={7: 1, 8: 2},
        compiler_params=PARAMS,
    )(flags, a, te, weights, skip_in, grad_out, grad_skip, e_acc, grads_acc)


def on_device(clean_latents, target_noise, timesteps, layer_counts, section_weights):
    section_count = lax.axis_size("section")
    half_count = section_count // 2
    section_index = lax.axis_index("section")
    micro_count, row_count, channels = clean_latents.shape
    rows = micro_count * row_count
    weights = section_weights[0]
    slot_count = weights.shape[0] // channels - 1
    layer_count = layer_counts[0]
    step_values = timesteps[0]
    signal_level = noise_level(step_values)[:, None, None]
    noisy_input = (
        jnp.sqrt(signal_level) * clean_latents.astype(jnp.float32)
        + jnp.sqrt(1.0 - signal_level) * target_noise.astype(jnp.float32)
    ).astype(BF16).reshape(rows, channels)
    target_rows = target_noise.reshape(rows, channels)
    time_embed = jnp.broadcast_to(
        time_features(step_values, channels)[:, None, :], (micro_count, row_count, channels)
    ).reshape(rows, channels)
    mirror_pairs_fwd = [(i, section_count - 1 - i) for i in range(half_count)]
    mirror_pairs_bwd = [(section_count - 1 - i, i) for i in range(half_count)]

    def flags_at(stage):
        active = (section_index == stage).astype(jnp.int32)
        return jnp.stack([layer_count, active])

    blank = jnp.zeros((rows, channels), BF16)
    current = noisy_input
    saved_in = noisy_input
    my_skip = blank
    skip_box = blank
    final_out = None
    for stage in range(section_count):
        is_decoder = stage >= half_count
        section_out, my_skip = stage_forward(
            flags_at(stage), current, time_embed, weights, skip_box, my_skip,
            is_decoder, slot_count, channels,
        )
        if stage == half_count - 1:
            skip_box = lax.ppermute(my_skip, "section", mirror_pairs_fwd)
        if stage < section_count - 1:
            current = lax.ppermute(section_out, "section", [(stage, stage + 1)])
            saved_in = jnp.where(section_index == stage + 1, current, saved_in)
        else:
            final_out = section_out

    grad_current = (
        (final_out.astype(jnp.float32) - target_rows.astype(jnp.float32)) / rows
    ).astype(BF16)
    my_e = blank
    e_box = blank
    weight_grads = jnp.zeros(((slot_count + 1) * channels, channels), F32)
    for stage in reversed(range(section_count)):
        is_decoder = stage >= half_count
        grad_low, my_e, weight_grads = stage_backward(
            flags_at(stage), saved_in, time_embed, weights, skip_box, grad_current, e_box,
            my_e, weight_grads, is_decoder, slot_count, channels,
        )
        if stage == half_count:
            e_box = lax.ppermute(my_e, "section", mirror_pairs_bwd)
        if stage > 0:
            grad_current = lax.ppermute(grad_low, "section", [(stage, stage - 1)])

    reduced = lax.psum_scatter(weight_grads, "rep", scatter_dimension=0, tiled=True)
    return reduced[None]


def solution(mesh):
    placed = (
        P(None, "rep", None),
        P(None, "rep", None),
        P("rep", None),
        P("section"),
        P("section", None, None),
    )
    return jax.shard_map(
        on_device, mesh=mesh, in_specs=placed, out_specs=P("section", "rep", None), check_vma=False
    )
```

```python
import functools
import math

import jax
import jax.numpy as jnp
from jax import lax
from jax.experimental import pallas as pl
from jax.experimental.pallas import tpu as pltpu
from jax.sharding import PartitionSpec as P

EPSILON = 1e-06
F32 = jnp.float32
BF16 = jnp.bfloat16


def noise_level(step_values):
    phase = (step_values.astype(jnp.float32) / 1000.0 + 0.008) / 1.008 * (math.pi / 2.0)
    return jnp.cos(phase) ** 2


def time_features(step_values, channels):
    half_width = channels // 2
    ladder = jnp.exp(-math.log(10000.0) * jnp.arange(half_width, dtype=jnp.float32) / half_width)
    angles = step_values.astype(jnp.float32)[..., None] * ladder
    return jnp.concatenate([jnp.sin(angles), jnp.cos(angles)], axis=-1)


def contract_rows(left, right):
    return lax.dot_general(left, right, (((0,), (0,)), ((), ())), preferred_element_type=F32)


def contract_cols(left, right):
    return lax.dot_general(left, right, (((1,), (1,)), ((), ())), preferred_element_type=F32)


def plain_product(left, right):
    return lax.dot_general(left, right, (((1,), (0,)), ((), ())), preferred_element_type=F32)


def sigmoid(value):
    return 1.0 / (1.0 + jnp.exp(-value))


def inverse_rms_of(hidden):
    return lax.rsqrt(jnp.mean(hidden * hidden, axis=-1, keepdims=True) + EPSILON)


def run_forward_slots(h_ref, te, w_ref, count, slot_count, channels, store_ref=None):
    for slot_index in range(slot_count):

        @pl.when(slot_index < count)
        def _():
            hidden = h_ref[...]
            if store_ref is not None:
                store_ref[slot_index] = hidden
            preact = hidden * inverse_rms_of(hidden) + te
            activated = (preact * sigmoid(preact)).astype(BF16)
            weight = w_ref[slot_index * channels : (slot_index + 1) * channels, :]
            h_ref[...] = hidden + plain_product(activated, weight)


def forward_kernel(
    flags_ref, a_ref, te_ref, w_ref, skip_ref, skip_acc_ref, out_ref, skip_out_ref,
    h_ref, skip_scr, sem, *, decoder, slot_count, channels
):
    count = flags_ref[0]
    active = flags_ref[1]

    @pl.when(active == 1)
    def _():
        side = w_ref[slot_count * channels :, :]
        hidden = a_ref[...].astype(F32)
        if decoder:
            hidden = hidden + plain_product(skip_ref[...], side)
        h_ref[...] = hidden
        run_forward_slots(h_ref, te_ref[...], w_ref, count, slot_count, channels)
        section_out = h_ref[...].astype(BF16)
        out_ref[...] = section_out
        if not decoder:
            skip_scr[...] = plain_product(section_out, side).astype(BF16)
            copy = pltpu.make_async_copy(skip_scr, skip_out_ref, sem)
            copy.start()
            copy.wait()


def backward_kernel(
    flags_ref, a_ref, te_ref, w_ref, skip_ref, g_ref, e_ref, e_acc_ref, grads_acc_ref,
    gprev_ref, e_out_ref, grads_out_ref,
    h_ref, hs_ref, gh_ref, grads_scr, e_scr, sems, *, decoder, slot_count, channels
):
    count = flags_ref[0]
    active = flags_ref[1]

    @pl.when(active == 1)
    def _():
        side = w_ref[slot_count * channels :, :]
        te = te_ref[...]
        hidden = a_ref[...].astype(F32)
        if decoder:
            hidden = hidden + plain_product(skip_ref[...], side)
        h_ref[...] = hidden
        run_forward_slots(h_ref, te, w_ref, count, slot_count, channels, store_ref=hs_ref)
        grad_hidden = g_ref[...].astype(F32)
        if not decoder:
            grad_skip = e_ref[...]
            grad_hidden = grad_hidden + contract_cols(grad_skip, side)
            section_out = h_ref[...].astype(BF16)
            grads_scr[slot_count * channels :, :] = contract_rows(section_out, grad_skip)
        gh_ref[...] = grad_hidden
        for slot_index in reversed(range(slot_count)):
            rows = slice(slot_index * channels, (slot_index + 1) * channels)

            @pl.when(slot_index < count)
            def _():
                hidden = hs_ref[slot_index]
                inverse_rms = inverse_rms_of(hidden)
                normed = hidden * inverse_rms
                preact = normed + te
                sigmoid_val = sigmoid(preact)
                activated = (preact * sigmoid_val).astype(BF16)
                grad_hidden = gh_ref[...]
                grad_low = grad_hidden.astype(BF16)
                grads_scr[rows, :] = contract_rows(activated, grad_low)
                grad_act = contract_cols(grad_low, w_ref[rows, :])
                grad_pre = grad_act * sigmoid_val * (1.0 + preact * (1.0 - sigmoid_val))
                gh_ref[...] = grad_hidden + inverse_rms * (
                    grad_pre - normed * jnp.mean(grad_pre * normed, axis=-1, keepdims=True)
                )

            @pl.when(slot_index >= count)
            def _():
                grads_scr[rows, :] = jnp.zeros((channels, channels), F32)

        grad_low = gh_ref[...].astype(BF16)
        gprev_ref[...] = grad_low
        if decoder:
            grads_scr[slot_count * channels :, :] = contract_rows(skip_ref[...], grad_low)
            e_scr[...] = contract_cols(grad_low, side).astype(BF16)
            e_copy = pltpu.make_async_copy(e_scr, e_out_ref, sems.at[1])
            e_copy.start()
        grads_copy = pltpu.make_async_copy(grads_scr, grads_out_ref, sems.at[0])
        grads_copy.start()
        grads_copy.wait()
        if decoder:
            e_copy.wait()


VMEM_SPEC = pl.BlockSpec(memory_space=pltpu.VMEM)
SMEM_SPEC = pl.BlockSpec(memory_space=pltpu.SMEM)
ANY_SPEC = pl.BlockSpec(memory_space=pl.ANY)
PARAMS = pltpu.CompilerParams(vmem_limit_bytes=48 * 1024 * 1024)


def stage_forward(flags, a, te, weights, skip_in, skip_acc, decoder, slot_count, channels):
    rows = a.shape[0]
    kernel = functools.partial(
        forward_kernel, decoder=decoder, slot_count=slot_count, channels=channels
    )
    return pl.pallas_call(
        kernel,
        out_shape=(
            jax.ShapeDtypeStruct((rows, channels), BF16),
            jax.ShapeDtypeStruct((rows, channels), BF16),
        ),
        in_specs=[SMEM_SPEC, VMEM_SPEC, VMEM_SPEC, VMEM_SPEC, VMEM_SPEC, ANY_SPEC],
        out_specs=(VMEM_SPEC, ANY_SPEC),
        scratch_shapes=[
            pltpu.VMEM((rows, channels), F32),
            pltpu.VMEM((rows, channels), BF16),
            pltpu.SemaphoreType.DMA(()),
        ],
        input_output_aliases={5: 1},
        compiler_params=PARAMS,
    )(flags, a, te, weights, skip_in, skip_acc)


def stage_backward(
    flags, a, te, weights, skip_in, grad_out, grad_skip, e_acc, grads_acc, decoder,
    slot_count, channels
):
    rows = a.shape[0]
    kernel = functools.partial(
        backward_kernel, decoder=decoder, slot_count=slot_count, channels=channels
    )
    return pl.pallas_call(
        kernel,
        out_shape=(
            jax.ShapeDtypeStruct((rows, channels), BF16),
            jax.ShapeDtypeStruct((rows, channels), BF16),
            jax.ShapeDtypeStruct(grads_acc.shape, F32),
        ),
        in_specs=[SMEM_SPEC] + [VMEM_SPEC] * 6 + [ANY_SPEC, ANY_SPEC],
        out_specs=(VMEM_SPEC, ANY_SPEC, ANY_SPEC),
        scratch_shapes=[
            pltpu.VMEM((rows, channels), F32),
            pltpu.VMEM((slot_count, rows, channels), F32),
            pltpu.VMEM((rows, channels), F32),
            pltpu.VMEM(grads_acc.shape, F32),
            pltpu.VMEM((rows, channels), BF16),
            pltpu.SemaphoreType.DMA((2,)),
        ],
        input_output_aliases={7: 1, 8: 2},
        compiler_params=PARAMS,
    )(flags, a, te, weights, skip_in, grad_out, grad_skip, e_acc, grads_acc)


def on_device(clean_latents, target_noise, timesteps, layer_counts, section_weights):
    section_count = lax.axis_size("section")
    half_count = section_count // 2
    section_index = lax.axis_index("section")
    micro_count, row_count, channels = clean_latents.shape
    rows = micro_count * row_count
    weights = section_weights[0]
    slot_count = weights.shape[0] // channels - 1
    layer_count = layer_counts[0]
    step_values = timesteps[0]
    signal_level = noise_level(step_values)[:, None, None]
    noisy_input = (
        jnp.sqrt(signal_level) * clean_latents.astype(jnp.float32)
        + jnp.sqrt(1.0 - signal_level) * target_noise.astype(jnp.float32)
    ).astype(BF16).reshape(rows, channels)
    target_rows = target_noise.reshape(rows, channels)
    time_embed = jnp.broadcast_to(
        time_features(step_values, channels)[:, None, :], (micro_count, row_count, channels)
    ).reshape(rows, channels)
    mirror_pairs_fwd = [(i, section_count - 1 - i) for i in range(half_count)]
    mirror_pairs_bwd = [(section_count - 1 - i, i) for i in range(half_count)]

    def flags_at(stage):
        active = (section_index == stage).astype(jnp.int32)
        return jnp.stack([layer_count, active])

    blank = jnp.zeros((rows, channels), BF16)
    current = noisy_input
    saved_in = noisy_input
    my_skip = blank
    skip_box = blank
    final_out = None
    for stage in range(section_count):
        is_decoder = stage >= half_count
        section_out, my_skip = stage_forward(
            flags_at(stage), current, time_embed, weights, skip_box, my_skip,
            is_decoder, slot_count, channels,
        )
        if stage == half_count - 1:
            skip_box = lax.ppermute(my_skip, "section", mirror_pairs_fwd)
        if stage < section_count - 1:
            current = lax.ppermute(section_out, "section", [(stage, stage + 1)])
            saved_in = jnp.where(section_index == stage + 1, current, saved_in)
        else:
            final_out = section_out

    grad_current = (
        (final_out.astype(jnp.float32) - target_rows.astype(jnp.float32)) / rows
    ).astype(BF16)
    my_e = blank
    e_box = blank
    weight_grads = jnp.zeros(((slot_count + 1) * channels, channels), F32)
    for stage in reversed(range(section_count)):
        is_decoder = stage >= half_count
        grad_low, my_e, weight_grads = stage_backward(
            flags_at(stage), saved_in, time_embed, weights, skip_box, grad_current, e_box,
            my_e, weight_grads, is_decoder, slot_count, channels,
        )
        if stage == half_count:
            e_box = lax.ppermute(my_e, "section", mirror_pairs_bwd)
        if stage > 0:
            grad_current = lax.ppermute(grad_low, "section", [(stage, stage - 1)])

    return two_level_scatter(weight_grads)[None]


def two_level_scatter(grads):
    rep_count = lax.axis_size("rep")
    if rep_count % 2:
        return lax.psum_scatter(grads, "rep", scatter_dimension=0, tiled=True)
    pair_count = rep_count // 2
    chunk = grads.shape[0] // rep_count
    reordered = (
        grads.reshape(pair_count, 2, chunk, grads.shape[1])
        .transpose(1, 0, 2, 3)
        .reshape(grads.shape)
    )
    within_chip = [[2 * i, 2 * i + 1] for i in range(pair_count)]
    across_chips = [[core + 2 * i for i in range(pair_count)] for core in range(2)]
    halves = lax.psum_scatter(
        reordered, "rep", scatter_dimension=0, axis_index_groups=within_chip, tiled=True
    )
    return lax.psum_scatter(
        halves, "rep", scatter_dimension=0, axis_index_groups=across_chips, tiled=True
    )


def solution(mesh):
    placed = (
        P(None, "rep", None),
        P(None, "rep", None),
        P("rep", None),
        P("section"),
        P("section", None, None),
    )
    return jax.shard_map(
        on_device, mesh=mesh, in_specs=placed, out_specs=P("section", "rep", None), check_vma=False
    )
```

```python
import functools
import math

import jax
import jax.numpy as jnp
from jax import lax
from jax.experimental import pallas as pl
from jax.experimental.pallas import tpu as pltpu
from jax.sharding import PartitionSpec as P

EPSILON = 1e-06
F32 = jnp.float32
BF16 = jnp.bfloat16


def noise_level(step_values):
    phase = (step_values.astype(jnp.float32) / 1000.0 + 0.008) / 1.008 * (math.pi / 2.0)
    return jnp.cos(phase) ** 2


def time_features(step_values, channels):
    half_width = channels // 2
    ladder = jnp.exp(-math.log(10000.0) * jnp.arange(half_width, dtype=jnp.float32) / half_width)
    angles = step_values.astype(jnp.float32)[..., None] * ladder
    return jnp.concatenate([jnp.sin(angles), jnp.cos(angles)], axis=-1)


def contract_rows(left, right):
    return lax.dot_general(left, right, (((0,), (0,)), ((), ())), preferred_element_type=F32)


def contract_cols(left, right):
    return lax.dot_general(left, right, (((1,), (1,)), ((), ())), preferred_element_type=F32)


def plain_product(left, right):
    return lax.dot_general(left, right, (((1,), (0,)), ((), ())), preferred_element_type=F32)


def sigmoid(value):
    return 1.0 / (1.0 + jnp.exp(-value))


def inverse_rms_of(hidden):
    return lax.rsqrt(jnp.mean(hidden * hidden, axis=-1, keepdims=True) + EPSILON)


def run_forward_slots(h_ref, te, w_ref, count, slot_count, channels, store_ref=None):
    for slot_index in range(slot_count):

        @pl.when(slot_index < count)
        def _():
            hidden = h_ref[...]
            if store_ref is not None:
                store_ref[slot_index] = hidden
            preact = hidden * inverse_rms_of(hidden) + te
            activated = (preact * sigmoid(preact)).astype(BF16)
            weight = w_ref[slot_index * channels : (slot_index + 1) * channels, :]
            h_ref[...] = hidden + plain_product(activated, weight)


def forward_kernel(
    flags_ref, a_ref, te_ref, w_ref, skip_ref, out_ref, skip_out_ref, h_ref,
    *, decoder, slot_count, channels
):
    count = flags_ref[0]
    side = w_ref[slot_count * channels :, :]
    hidden = a_ref[...].astype(F32)
    if decoder:
        hidden = hidden + plain_product(skip_ref[...], side)
    h_ref[...] = hidden
    run_forward_slots(h_ref, te_ref[...], w_ref, count, slot_count, channels)
    section_out = h_ref[...].astype(BF16)
    out_ref[...] = section_out
    if not decoder:
        skip_out_ref[...] = plain_product(section_out, side).astype(BF16)


def backward_kernel(
    flags_ref, a_ref, te_ref, w_ref, skip_ref, g_ref, e_ref, grads_acc_ref,
    gprev_ref, e_out_ref, grads_out_ref,
    h_ref, hs_ref, gh_ref, grads_scr, sem, *, decoder, slot_count, channels
):
    count = flags_ref[0]
    owned = flags_ref[1] == 1
    side = w_ref[slot_count * channels :, :]
    te = te_ref[...]
    hidden = a_ref[...].astype(F32)
    if decoder:
        hidden = hidden + plain_product(skip_ref[...], side)
    h_ref[...] = hidden
    run_forward_slots(h_ref, te, w_ref, count, slot_count, channels, store_ref=hs_ref)
    grad_hidden = g_ref[...].astype(F32)
    if not decoder:
        grad_skip = e_ref[...]
        grad_hidden = grad_hidden + contract_cols(grad_skip, side)
        section_out = h_ref[...].astype(BF16)
        grads_scr[slot_count * channels :, :] = contract_rows(section_out, grad_skip)

    gh_ref[...] = grad_hidden
    for slot_index in reversed(range(slot_count)):
        rows = slice(slot_index * channels, (slot_index + 1) * channels)

        @pl.when(slot_index < count)
        def _():
            hidden = hs_ref[slot_index]
            inverse_rms = inverse_rms_of(hidden)
            normed = hidden * inverse_rms
            preact = normed + te
            sigmoid_val = sigmoid(preact)
            grad_hidden = gh_ref[...]
            grad_low = grad_hidden.astype(BF16)
            activated = (preact * sigmoid_val).astype(BF16)
            grads_scr[rows, :] = contract_rows(activated, grad_low)
            grad_act = contract_cols(grad_low, w_ref[rows, :])
            grad_pre = grad_act * sigmoid_val * (1.0 + preact * (1.0 - sigmoid_val))
            gh_ref[...] = grad_hidden + inverse_rms * (
                grad_pre - normed * jnp.mean(grad_pre * normed, axis=-1, keepdims=True)
            )

        @pl.when(slot_index >= count)
        def _():
            grads_scr[rows, :] = jnp.zeros((channels, channels), F32)

    grad_low = gh_ref[...].astype(BF16)
    gprev_ref[...] = grad_low
    if decoder:
        e_out_ref[...] = contract_cols(grad_low, side).astype(BF16)
        grads_scr[slot_count * channels :, :] = contract_rows(skip_ref[...], grad_low)

    @pl.when(owned)
    def _():
        grads_copy = pltpu.make_async_copy(grads_scr, grads_out_ref, sem)
        grads_copy.start()
        grads_copy.wait()


PARAMS = pltpu.CompilerParams(vmem_limit_bytes=48 * 1024 * 1024)


VMEM_SPEC = pl.BlockSpec(memory_space=pltpu.VMEM)
SMEM_SPEC = pl.BlockSpec(memory_space=pltpu.SMEM)
ANY_SPEC = pl.BlockSpec(memory_space=pl.ANY)


def stage_forward(flags, a, te, weights, skip_in, decoder, slot_count, channels):
    rows = a.shape[0]
    kernel = functools.partial(
        forward_kernel, decoder=decoder, slot_count=slot_count, channels=channels
    )
    return pl.pallas_call(
        kernel,
        out_shape=(
            jax.ShapeDtypeStruct((rows, channels), BF16),
            jax.ShapeDtypeStruct((rows, channels), BF16),
        ),
        in_specs=[SMEM_SPEC] + [VMEM_SPEC] * 4,
        out_specs=(VMEM_SPEC, VMEM_SPEC),
        scratch_shapes=[pltpu.VMEM((rows, channels), F32)],
        compiler_params=PARAMS,
    )(flags, a, te, weights, skip_in)


def stage_backward(
    flags, a, te, weights, skip_in, grad_out, grad_skip, grads_acc, decoder,
    slot_count, channels
):
    rows = a.shape[0]
    kernel = functools.partial(
        backward_kernel, decoder=decoder, slot_count=slot_count, channels=channels
    )
    return pl.pallas_call(
        kernel,
        out_shape=(
            jax.ShapeDtypeStruct((rows, channels), BF16),
            jax.ShapeDtypeStruct((rows, channels), BF16),
            jax.ShapeDtypeStruct(grads_acc.shape, F32),
        ),
        in_specs=[SMEM_SPEC] + [VMEM_SPEC] * 6 + [ANY_SPEC],
        out_specs=(VMEM_SPEC, VMEM_SPEC, ANY_SPEC),
        scratch_shapes=[
            pltpu.VMEM((rows, channels), F32),
            pltpu.VMEM((slot_count, rows, channels), F32),
            pltpu.VMEM((rows, channels), F32),
            pltpu.VMEM(grads_acc.shape, F32),
            pltpu.SemaphoreType.DMA(()),
        ],
        input_output_aliases={7: 2},
        compiler_params=PARAMS,
    )(flags, a, te, weights, skip_in, grad_out, grad_skip, grads_acc)


def on_device(clean_latents, target_noise, timesteps, layer_counts, section_weights):
    section_count = lax.axis_size("section")
    half_count = section_count // 2
    section_index = lax.axis_index("section")
    micro_count, row_count, channels = clean_latents.shape
    rows = micro_count * row_count
    weights = section_weights[0]
    slot_count = weights.shape[0] // channels - 1
    step_values = timesteps[0]

    held_weights = [weights]
    held_counts = [layer_counts]
    for shift in range(1, section_count):
        pairs = [(i, (i + shift) % section_count) for i in range(section_count)]
        held_weights.append(lax.ppermute(weights, "section", pairs))
        held_counts.append(lax.ppermute(layer_counts, "section", pairs))
    stacked = jnp.stack(held_weights)
    counts_by_shift = jnp.concatenate(held_counts)

    signal_level = noise_level(step_values)[:, None, None]
    noisy_input = (
        jnp.sqrt(signal_level) * clean_latents.astype(jnp.float32)
        + jnp.sqrt(1.0 - signal_level) * target_noise.astype(jnp.float32)
    ).astype(BF16).reshape(rows, channels)
    target_rows = target_noise.reshape(rows, channels)
    time_embed = jnp.broadcast_to(
        time_features(step_values, channels)[:, None, :], (micro_count, row_count, channels)
    ).reshape(rows, channels)

    def flags_at(stage):
        shift = (section_index - stage) % section_count
        owned = (section_index == stage).astype(jnp.int32)
        return jnp.stack([counts_by_shift[shift], owned, shift])

    def weights_at(stage):
        shift = (section_index - stage) % section_count
        return lax.dynamic_index_in_dim(stacked, shift, 0, keepdims=False)

    blank = jnp.zeros((rows, channels), BF16)
    current = noisy_input
    section_inputs = []
    skips = {}
    for stage in range(section_count):
        is_decoder = stage >= half_count
        section_inputs.append(current)
        skip_in = skips[section_count - 1 - stage] if is_decoder else blank
        current, skip_out = stage_forward(
            flags_at(stage), current, time_embed, weights_at(stage), skip_in,
            is_decoder, slot_count, channels,
        )
        if not is_decoder:
            skips[stage] = skip_out

    grad_current = (
        (current.astype(jnp.float32) - target_rows.astype(jnp.float32)) / rows
    ).astype(BF16)
    grad_skips = {}
    weight_grads = jnp.zeros(((slot_count + 1) * channels, channels), F32)
    for stage in reversed(range(section_count)):
        is_decoder = stage >= half_count
        skip_in = skips[section_count - 1 - stage] if is_decoder else blank
        grad_skip = blank if is_decoder else grad_skips[section_count - 1 - stage]
        grad_current, e_out, weight_grads = stage_backward(
            flags_at(stage), section_inputs[stage], time_embed, weights_at(stage), skip_in,
            grad_current, grad_skip, weight_grads, is_decoder, slot_count, channels,
        )
        if is_decoder:
            grad_skips[stage] = e_out

    return lax.psum_scatter(weight_grads, "rep", scatter_dimension=0, tiled=True)[None]


def solution(mesh):
    placed = (
        P(None, "rep", None),
        P(None, "rep", None),
        P("rep", None),
        P("section"),
        P("section", None, None),
    )
    return jax.shard_map(
        on_device, mesh=mesh, in_specs=placed, out_specs=P("section", "rep", None), check_vma=False
    )
```

```python
import functools
import math

import jax
import jax.numpy as jnp
from jax import lax
from jax.experimental import pallas as pl
from jax.experimental.pallas import tpu as pltpu
from jax.sharding import PartitionSpec as P

EPSILON = 1e-06
F32 = jnp.float32
BF16 = jnp.bfloat16


def noise_level(step_values):
    phase = (step_values.astype(jnp.float32) / 1000.0 + 0.008) / 1.008 * (math.pi / 2.0)
    return jnp.cos(phase) ** 2


def time_features(step_values, channels):
    half_width = channels // 2
    ladder = jnp.exp(-math.log(10000.0) * jnp.arange(half_width, dtype=jnp.float32) / half_width)
    angles = step_values.astype(jnp.float32)[..., None] * ladder
    return jnp.concatenate([jnp.sin(angles), jnp.cos(angles)], axis=-1)


def contract_rows(left, right):
    return lax.dot_general(left, right, (((0,), (0,)), ((), ())), preferred_element_type=F32)


def contract_cols(left, right):
    return lax.dot_general(left, right, (((1,), (1,)), ((), ())), preferred_element_type=F32)


def plain_product(left, right):
    return lax.dot_general(left, right, (((1,), (0,)), ((), ())), preferred_element_type=F32)


def sigmoid(value):
    return 1.0 / (1.0 + jnp.exp(-value))


def inverse_rms_of(hidden):
    return lax.rsqrt(jnp.mean(hidden * hidden, axis=-1, keepdims=True) + EPSILON)


def run_forward_slots(h_ref, te, w_ref, count, slot_count, channels, store_ref=None):
    for slot_index in range(slot_count):

        @pl.when(slot_index < count)
        def _():
            hidden = h_ref[...]
            if store_ref is not None:
                store_ref[slot_index] = hidden
            preact = hidden * inverse_rms_of(hidden) + te
            activated = (preact * sigmoid(preact)).astype(BF16)
            weight = w_ref[slot_index * channels : (slot_index + 1) * channels, :]
            h_ref[...] = hidden + plain_product(activated, weight)


def forward_kernel(
    flags_ref, a_ref, te_ref, w_ref, skip_ref, out_ref, skip_out_ref, h_ref,
    *, decoder, slot_count, channels
):
    count = flags_ref[0]
    side = w_ref[slot_count * channels :, :]
    hidden = a_ref[...].astype(F32)
    if decoder:
        hidden = hidden + plain_product(skip_ref[...], side)
    h_ref[...] = hidden
    run_forward_slots(h_ref, te_ref[...], w_ref, count, slot_count, channels)
    section_out = h_ref[...].astype(BF16)
    out_ref[...] = section_out
    if not decoder:
        skip_out_ref[...] = plain_product(section_out, side).astype(BF16)


def backward_kernel(
    flags_ref, a_ref, te_ref, w_ref, skip_ref, g_ref, e_ref, grads_acc_ref,
    gprev_ref, e_out_ref, grads_out_ref,
    h_ref, hs_ref, gh_ref, grads_scr, sem, *, decoder, slot_count, channels
):
    count = flags_ref[0]
    owned = flags_ref[1] == 1
    side = w_ref[slot_count * channels :, :]
    te = te_ref[...]
    hidden = a_ref[...].astype(F32)
    if decoder:
        hidden = hidden + plain_product(skip_ref[...], side)
    h_ref[...] = hidden
    run_forward_slots(h_ref, te, w_ref, count, slot_count, channels, store_ref=hs_ref)
    grad_hidden = g_ref[...].astype(F32)
    if not decoder:
        grad_skip = e_ref[...]
        grad_hidden = grad_hidden + contract_cols(grad_skip, side)
        section_out = h_ref[...].astype(BF16)
        grads_scr[slot_count * channels :, :] = contract_rows(section_out, grad_skip)

    gh_ref[...] = grad_hidden
    for slot_index in reversed(range(slot_count)):
        rows = slice(slot_index * channels, (slot_index + 1) * channels)

        @pl.when(slot_index < count)
        def _():
            hidden = hs_ref[slot_index]
            inverse_rms = inverse_rms_of(hidden)
            normed = hidden * inverse_rms
            preact = normed + te
            sigmoid_val = sigmoid(preact)
            grad_hidden = gh_ref[...]
            grad_low = grad_hidden.astype(BF16)
            activated = (preact * sigmoid_val).astype(BF16)
            grads_scr[rows, :] = contract_rows(activated, grad_low)
            grad_act = contract_cols(grad_low, w_ref[rows, :])
            grad_pre = grad_act * sigmoid_val * (1.0 + preact * (1.0 - sigmoid_val))
            gh_ref[...] = grad_hidden + inverse_rms * (
                grad_pre - normed * jnp.mean(grad_pre * normed, axis=-1, keepdims=True)
            )

        @pl.when(slot_index >= count)
        def _():
            grads_scr[rows, :] = jnp.zeros((channels, channels), F32)

    grad_low = gh_ref[...].astype(BF16)
    gprev_ref[...] = grad_low
    if decoder:
        e_out_ref[...] = contract_cols(grad_low, side).astype(BF16)
        grads_scr[slot_count * channels :, :] = contract_rows(skip_ref[...], grad_low)

    @pl.when(owned)
    def _():
        grads_copy = pltpu.make_async_copy(grads_scr, grads_out_ref, sem)
        grads_copy.start()
        grads_copy.wait()


PARAMS = pltpu.CompilerParams(vmem_limit_bytes=48 * 1024 * 1024)


VMEM_SPEC = pl.BlockSpec(memory_space=pltpu.VMEM)
SMEM_SPEC = pl.BlockSpec(memory_space=pltpu.SMEM)
ANY_SPEC = pl.BlockSpec(memory_space=pl.ANY)


def stage_forward(flags, a, te, weights, skip_in, decoder, slot_count, channels):
    rows = a.shape[0]
    kernel = functools.partial(
        forward_kernel, decoder=decoder, slot_count=slot_count, channels=channels
    )
    return pl.pallas_call(
        kernel,
        out_shape=(
            jax.ShapeDtypeStruct((rows, channels), BF16),
            jax.ShapeDtypeStruct((rows, channels), BF16),
        ),
        in_specs=[SMEM_SPEC] + [VMEM_SPEC] * 4,
        out_specs=(VMEM_SPEC, VMEM_SPEC),
        scratch_shapes=[pltpu.VMEM((rows, channels), F32)],
        compiler_params=PARAMS,
    )(flags, a, te, weights, skip_in)


def stage_backward(
    flags, a, te, weights, skip_in, grad_out, grad_skip, grads_acc, decoder,
    slot_count, channels
):
    rows = a.shape[0]
    kernel = functools.partial(
        backward_kernel, decoder=decoder, slot_count=slot_count, channels=channels
    )
    return pl.pallas_call(
        kernel,
        out_shape=(
            jax.ShapeDtypeStruct((rows, channels), BF16),
            jax.ShapeDtypeStruct((rows, channels), BF16),
            jax.ShapeDtypeStruct(grads_acc.shape, F32),
        ),
        in_specs=[SMEM_SPEC] + [VMEM_SPEC] * 6 + [ANY_SPEC],
        out_specs=(VMEM_SPEC, VMEM_SPEC, ANY_SPEC),
        scratch_shapes=[
            pltpu.VMEM((rows, channels), F32),
            pltpu.VMEM((slot_count, rows, channels), F32),
            pltpu.VMEM((rows, channels), F32),
            pltpu.VMEM(grads_acc.shape, F32),
            pltpu.SemaphoreType.DMA(()),
        ],
        input_output_aliases={7: 2},
        compiler_params=PARAMS,
    )(flags, a, te, weights, skip_in, grad_out, grad_skip, grads_acc)


def on_device(clean_latents, target_noise, timesteps, layer_counts, section_weights):
    section_count = lax.axis_size("section")
    half_count = section_count // 2
    section_index = lax.axis_index("section")
    micro_count, row_count, channels = clean_latents.shape
    rows = micro_count * row_count
    weights = section_weights[0]
    slot_count = weights.shape[0] // channels - 1
    step_values = timesteps[0]

    all_weights = lax.all_gather(weights, "section")
    all_counts = lax.all_gather(layer_counts, "section", tiled=True)

    signal_level = noise_level(step_values)[:, None, None]
    noisy_input = (
        jnp.sqrt(signal_level) * clean_latents.astype(jnp.float32)
        + jnp.sqrt(1.0 - signal_level) * target_noise.astype(jnp.float32)
    ).astype(BF16).reshape(rows, channels)
    target_rows = target_noise.reshape(rows, channels)
    time_embed = jnp.broadcast_to(
        time_features(step_values, channels)[:, None, :], (micro_count, row_count, channels)
    ).reshape(rows, channels)

    def flags_at(stage):
        owned = (section_index == stage).astype(jnp.int32)
        return jnp.stack([all_counts[stage], owned])

    def weights_at(stage):
        return all_weights[stage]

    blank = jnp.zeros((rows, channels), BF16)
    current = noisy_input
    section_inputs = []
    skips = {}
    for stage in range(section_count):
        is_decoder = stage >= half_count
        section_inputs.append(current)
        skip_in = skips[section_count - 1 - stage] if is_decoder else blank
        current, skip_out = stage_forward(
            flags_at(stage), current, time_embed, weights_at(stage), skip_in,
            is_decoder, slot_count, channels,
        )
        if not is_decoder:
            skips[stage] = skip_out

    grad_current = (
        (current.astype(jnp.float32) - target_rows.astype(jnp.float32)) / rows
    ).astype(BF16)
    grad_skips = {}
    weight_grads = jnp.zeros(((slot_count + 1) * channels, channels), F32)
    for stage in reversed(range(section_count)):
        is_decoder = stage >= half_count
        skip_in = skips[section_count - 1 - stage] if is_decoder else blank
        grad_skip = blank if is_decoder else grad_skips[section_count - 1 - stage]
        grad_current, e_out, weight_grads = stage_backward(
            flags_at(stage), section_inputs[stage], time_embed, weights_at(stage), skip_in,
            grad_current, grad_skip, weight_grads, is_decoder, slot_count, channels,
        )
        if is_decoder:
            grad_skips[stage] = e_out

    return lax.psum_scatter(weight_grads, "rep", scatter_dimension=0, tiled=True)[None]


def solution(mesh):
    placed = (
        P(None, "rep", None),
        P(None, "rep", None),
        P("rep", None),
        P("section"),
        P("section", None, None),
    )
    return jax.shard_map(
        on_device, mesh=mesh, in_specs=placed, out_specs=P("section", "rep", None), check_vma=False
    )
```

```python
import functools
import math

import jax
import jax.numpy as jnp
from jax import lax
from jax.experimental import pallas as pl
from jax.experimental.pallas import tpu as pltpu
from jax.sharding import PartitionSpec as P

EPSILON = 1e-06
F32 = jnp.float32
BF16 = jnp.bfloat16


def noise_level(step_values):
    phase = (step_values.astype(jnp.float32) / 1000.0 + 0.008) / 1.008 * (math.pi / 2.0)
    return jnp.cos(phase) ** 2


def time_features(step_values, channels):
    half_width = channels // 2
    ladder = jnp.exp(-math.log(10000.0) * jnp.arange(half_width, dtype=jnp.float32) / half_width)
    angles = step_values.astype(jnp.float32)[..., None] * ladder
    return jnp.concatenate([jnp.sin(angles), jnp.cos(angles)], axis=-1)


def contract_rows(left, right):
    return lax.dot_general(left, right, (((0,), (0,)), ((), ())), preferred_element_type=F32)


def contract_cols(left, right):
    return lax.dot_general(left, right, (((1,), (1,)), ((), ())), preferred_element_type=F32)


def plain_product(left, right):
    return lax.dot_general(left, right, (((1,), (0,)), ((), ())), preferred_element_type=F32)


def sigmoid(value):
    return 1.0 / (1.0 + jnp.exp(-value))


def inverse_rms_of(hidden):
    return lax.rsqrt(jnp.mean(hidden * hidden, axis=-1, keepdims=True) + EPSILON)


def run_forward_slots(h_ref, te, w_ref, count, slot_count, channels, store_ref=None):
    for slot_index in range(slot_count):

        @pl.when(slot_index < count)
        def _():
            hidden = h_ref[...]
            if store_ref is not None:
                store_ref[slot_index] = hidden
            preact = hidden * inverse_rms_of(hidden) + te
            activated = (preact * sigmoid(preact)).astype(BF16)
            weight = w_ref[slot_index * channels : (slot_index + 1) * channels, :]
            h_ref[...] = hidden + plain_product(activated, weight)


def load_weights(w_hbm, w_ref, sems, stage):
    half_rows = w_hbm.shape[2]
    copies = [
        pltpu.make_async_copy(
            w_hbm.at[core, stage], w_ref.at[pl.ds(core * half_rows, half_rows)], sems.at[core]
        )
        for core in range(2)
    ]
    for copy in copies:
        copy.start()
    for copy in copies:
        copy.wait()


def forward_kernel(
    flags_ref, a_ref, te_ref, w_hbm, skip_ref, out_ref, skip_out_ref, h_ref, w_ref, w_sems,
    *, decoder, slot_count, channels, stage
):
    load_weights(w_hbm, w_ref, w_sems, stage)
    count = flags_ref[0]
    side = w_ref[slot_count * channels :, :]
    hidden = a_ref[...].astype(F32)
    if decoder:
        hidden = hidden + plain_product(skip_ref[...], side)
    h_ref[...] = hidden
    run_forward_slots(h_ref, te_ref[...], w_ref, count, slot_count, channels)
    section_out = h_ref[...].astype(BF16)
    out_ref[...] = section_out
    if not decoder:
        skip_out_ref[...] = plain_product(section_out, side).astype(BF16)


def backward_kernel(
    flags_ref, a_ref, te_ref, w_hbm, skip_ref, g_ref, e_ref, grads_acc_ref,
    gprev_ref, e_out_ref, grads_out_ref,
    h_ref, hs_ref, gh_ref, grads_scr, sem, w_ref, w_sems, *, decoder, slot_count, channels, stage
):
    load_weights(w_hbm, w_ref, w_sems, stage)
    count = flags_ref[0]
    owned = flags_ref[1] == 1
    side = w_ref[slot_count * channels :, :]
    te = te_ref[...]
    hidden = a_ref[...].astype(F32)
    if decoder:
        hidden = hidden + plain_product(skip_ref[...], side)
    h_ref[...] = hidden
    run_forward_slots(h_ref, te, w_ref, count, slot_count, channels, store_ref=hs_ref)
    grad_hidden = g_ref[...].astype(F32)
    if not decoder:
        grad_skip = e_ref[...]
        grad_hidden = grad_hidden + contract_cols(grad_skip, side)
        section_out = h_ref[...].astype(BF16)
        grads_scr[slot_count * channels :, :] = contract_rows(section_out, grad_skip)

    gh_ref[...] = grad_hidden
    for slot_index in reversed(range(slot_count)):
        rows = slice(slot_index * channels, (slot_index + 1) * channels)

        @pl.when(slot_index < count)
        def _():
            hidden = hs_ref[slot_index]
            inverse_rms = inverse_rms_of(hidden)
            normed = hidden * inverse_rms
            preact = normed + te
            sigmoid_val = sigmoid(preact)
            grad_hidden = gh_ref[...]
            grad_low = grad_hidden.astype(BF16)
            activated = (preact * sigmoid_val).astype(BF16)
            grads_scr[rows, :] = contract_rows(activated, grad_low)
            grad_act = contract_cols(grad_low, w_ref[rows, :])
            grad_pre = grad_act * sigmoid_val * (1.0 + preact * (1.0 - sigmoid_val))
            gh_ref[...] = grad_hidden + inverse_rms * (
                grad_pre - normed * jnp.mean(grad_pre * normed, axis=-1, keepdims=True)
            )

        @pl.when(slot_index >= count)
        def _():
            grads_scr[rows, :] = jnp.zeros((channels, channels), F32)

    grad_low = gh_ref[...].astype(BF16)
    gprev_ref[...] = grad_low
    if decoder:
        e_out_ref[...] = contract_cols(grad_low, side).astype(BF16)
        grads_scr[slot_count * channels :, :] = contract_rows(skip_ref[...], grad_low)

    @pl.when(owned)
    def _():
        grads_copy = pltpu.make_async_copy(grads_scr, grads_out_ref, sem)
        grads_copy.start()
        grads_copy.wait()


PARAMS = pltpu.CompilerParams(vmem_limit_bytes=48 * 1024 * 1024)


VMEM_SPEC = pl.BlockSpec(memory_space=pltpu.VMEM)
SMEM_SPEC = pl.BlockSpec(memory_space=pltpu.SMEM)
ANY_SPEC = pl.BlockSpec(memory_space=pl.ANY)


def stage_forward(flags, a, te, weights, skip_in, decoder, slot_count, channels, stage):
    rows = a.shape[0]
    kernel = functools.partial(
        forward_kernel, decoder=decoder, slot_count=slot_count, channels=channels, stage=stage
    )
    return pl.pallas_call(
        kernel,
        out_shape=(
            jax.ShapeDtypeStruct((rows, channels), BF16),
            jax.ShapeDtypeStruct((rows, channels), BF16),
        ),
        in_specs=[SMEM_SPEC, VMEM_SPEC, VMEM_SPEC, ANY_SPEC, VMEM_SPEC],
        out_specs=(VMEM_SPEC, VMEM_SPEC),
        scratch_shapes=[
            pltpu.VMEM((rows, channels), F32),
            pltpu.VMEM(((slot_count + 1) * channels, channels), BF16),
            pltpu.SemaphoreType.DMA((2,)),
        ],
        compiler_params=PARAMS,
    )(flags, a, te, weights, skip_in)


def stage_backward(
    flags, a, te, weights, skip_in, grad_out, grad_skip, grads_acc, decoder,
    slot_count, channels, stage
):
    rows = a.shape[0]
    kernel = functools.partial(
        backward_kernel, decoder=decoder, slot_count=slot_count, channels=channels, stage=stage
    )
    return pl.pallas_call(
        kernel,
        out_shape=(
            jax.ShapeDtypeStruct((rows, channels), BF16),
            jax.ShapeDtypeStruct((rows, channels), BF16),
            jax.ShapeDtypeStruct(grads_acc.shape, F32),
        ),
        in_specs=[SMEM_SPEC, VMEM_SPEC, VMEM_SPEC, ANY_SPEC] + [VMEM_SPEC] * 3 + [ANY_SPEC],
        out_specs=(VMEM_SPEC, VMEM_SPEC, ANY_SPEC),
        scratch_shapes=[
            pltpu.VMEM((rows, channels), F32),
            pltpu.VMEM((slot_count, rows, channels), F32),
            pltpu.VMEM((rows, channels), F32),
            pltpu.VMEM(grads_acc.shape, F32),
            pltpu.SemaphoreType.DMA(()),
            pltpu.VMEM(((slot_count + 1) * channels, channels), BF16),
            pltpu.SemaphoreType.DMA((2,)),
        ],
        input_output_aliases={7: 2},
        compiler_params=PARAMS,
    )(flags, a, te, weights, skip_in, grad_out, grad_skip, grads_acc)


def on_device(clean_latents, target_noise, timesteps, layer_counts, section_weights):
    section_count = lax.axis_size("section")
    half_count = section_count // 2
    section_index = lax.axis_index("section")
    micro_count, row_count, channels = clean_latents.shape
    rows = micro_count * row_count
    weights = section_weights[0]
    slot_count = weights.shape[0] // channels - 1
    step_values = timesteps[0]

    rep_count = lax.axis_size("rep")
    core_index = lax.axis_index("rep") % 2
    my_half = lax.dynamic_index_in_dim(
        weights.reshape(2, weights.shape[0] // 2, channels), core_index, 0, keepdims=False
    )
    halves_by_section = lax.all_gather(my_half, "section")
    chip_pairs = [[2 * i, 2 * i + 1] for i in range(rep_count // 2)]
    all_weights = lax.all_gather(halves_by_section, "rep", axis_index_groups=chip_pairs)
    all_counts = lax.all_gather(layer_counts, "section", tiled=True)

    signal_level = noise_level(step_values)[:, None, None]
    noisy_input = (
        jnp.sqrt(signal_level) * clean_latents.astype(jnp.float32)
        + jnp.sqrt(1.0 - signal_level) * target_noise.astype(jnp.float32)
    ).astype(BF16).reshape(rows, channels)
    target_rows = target_noise.reshape(rows, channels)
    time_embed = jnp.broadcast_to(
        time_features(step_values, channels)[:, None, :], (micro_count, row_count, channels)
    ).reshape(rows, channels)

    def flags_at(stage):
        owned = (section_index == stage).astype(jnp.int32)
        return jnp.stack([all_counts[stage], owned])


    blank = jnp.zeros((rows, channels), BF16)
    current = noisy_input
    section_inputs = []
    skips = {}
    for stage in range(section_count):
        is_decoder = stage >= half_count
        section_inputs.append(current)
        skip_in = skips[section_count - 1 - stage] if is_decoder else blank
        current, skip_out = stage_forward(
            flags_at(stage), current, time_embed, all_weights, skip_in,
            is_decoder, slot_count, channels, stage,
        )
        if not is_decoder:
            skips[stage] = skip_out

    grad_current = (
        (current.astype(jnp.float32) - target_rows.astype(jnp.float32)) / rows
    ).astype(BF16)
    grad_skips = {}
    weight_grads = jnp.zeros(((slot_count + 1) * channels, channels), F32)
    for stage in reversed(range(section_count)):
        is_decoder = stage >= half_count
        skip_in = skips[section_count - 1 - stage] if is_decoder else blank
        grad_skip = blank if is_decoder else grad_skips[section_count - 1 - stage]
        grad_current, e_out, weight_grads = stage_backward(
            flags_at(stage), section_inputs[stage], time_embed, all_weights, skip_in,
            grad_current, grad_skip, weight_grads, is_decoder, slot_count, channels, stage,
        )
        if is_decoder:
            grad_skips[stage] = e_out

    return lax.psum_scatter(weight_grads, "rep", scatter_dimension=0, tiled=True)[None]


def solution(mesh):
    placed = (
        P(None, "rep", None),
        P(None, "rep", None),
        P("rep", None),
        P("section"),
        P("section", None, None),
    )
    return jax.shard_map(
        on_device, mesh=mesh, in_specs=placed, out_specs=P("section", "rep", None), check_vma=False
    )
```

```python
import functools
import math

import jax
import jax.numpy as jnp
from jax import lax
from jax.experimental import pallas as pl
from jax.experimental.pallas import tpu as pltpu
from jax.sharding import PartitionSpec as P

EPSILON = 1e-06
F32 = jnp.float32
BF16 = jnp.bfloat16


def noise_level(step_values):
    phase = (step_values.astype(jnp.float32) / 1000.0 + 0.008) / 1.008 * (math.pi / 2.0)
    return jnp.cos(phase) ** 2


def time_features(step_values, channels):
    half_width = channels // 2
    ladder = jnp.exp(-math.log(10000.0) * jnp.arange(half_width, dtype=jnp.float32) / half_width)
    angles = step_values.astype(jnp.float32)[..., None] * ladder
    return jnp.concatenate([jnp.sin(angles), jnp.cos(angles)], axis=-1)


def contract_rows(left, right):
    return lax.dot_general(left, right, (((0,), (0,)), ((), ())), preferred_element_type=F32)


def contract_cols(left, right):
    return lax.dot_general(left, right, (((1,), (1,)), ((), ())), preferred_element_type=F32)


def plain_product(left, right):
    return lax.dot_general(left, right, (((1,), (0,)), ((), ())), preferred_element_type=F32)


def sigmoid(value):
    return 1.0 / (1.0 + jnp.exp(-value))


def inverse_rms_of(hidden):
    return lax.rsqrt(jnp.mean(hidden * hidden, axis=-1, keepdims=True) + EPSILON)


def run_forward_slots(h_ref, te, w_ref, count, slot_count, channels, store_ref=None):
    for slot_index in range(slot_count):

        @pl.when(slot_index < count)
        def _():
            hidden = h_ref[...]
            if store_ref is not None:
                store_ref[slot_index] = hidden
            preact = hidden * inverse_rms_of(hidden) + te
            activated = (preact * sigmoid(preact)).astype(BF16)
            weight = w_ref[slot_index * channels : (slot_index + 1) * channels, :]
            h_ref[...] = hidden + plain_product(activated, weight)


def load_weights(mine_hbm, sibling_hbm, w_ref, sems, core, stage):
    half_rows = w_ref.shape[0] // 2
    mine_at = pl.multiple_of(core * half_rows, 16)
    sibling_at = pl.multiple_of((1 - core) * half_rows, 16)
    copies = [
        pltpu.make_async_copy(
            mine_hbm.at[stage, pl.ds(0, half_rows)], w_ref.at[pl.ds(mine_at, half_rows)],
            sems.at[0],
        ),
        pltpu.make_async_copy(
            sibling_hbm.at[stage, pl.ds(0, half_rows)], w_ref.at[pl.ds(sibling_at, half_rows)],
            sems.at[1],
        ),
    ]
    for copy in copies:
        copy.start()
    for copy in copies:
        copy.wait()


def forward_kernel(
    flags_ref, a_ref, te_ref, mine_hbm, sibling_hbm, skip_ref, out_ref, skip_out_ref, h_ref,
    w_ref, w_sems, *, decoder, slot_count, channels, stage
):
    load_weights(mine_hbm, sibling_hbm, w_ref, w_sems, flags_ref[2], stage)
    count = flags_ref[0]
    side = w_ref[slot_count * channels :, :]
    hidden = a_ref[...].astype(F32)
    if decoder:
        hidden = hidden + plain_product(skip_ref[...], side)
    h_ref[...] = hidden
    run_forward_slots(h_ref, te_ref[...], w_ref, count, slot_count, channels)
    section_out = h_ref[...].astype(BF16)
    out_ref[...] = section_out
    if not decoder:
        skip_out_ref[...] = plain_product(section_out, side).astype(BF16)


def backward_kernel(
    flags_ref, a_ref, te_ref, mine_hbm, sibling_hbm, skip_ref, g_ref, e_ref, grads_acc_ref,
    gprev_ref, e_out_ref, grads_out_ref,
    h_ref, hs_ref, gh_ref, grads_scr, sem, w_ref, w_sems, *, decoder, slot_count, channels, stage
):
    load_weights(mine_hbm, sibling_hbm, w_ref, w_sems, flags_ref[2], stage)
    count = flags_ref[0]
    owned = flags_ref[1] == 1
    side = w_ref[slot_count * channels :, :]
    te = te_ref[...]
    hidden = a_ref[...].astype(F32)
    if decoder:
        hidden = hidden + plain_product(skip_ref[...], side)
    h_ref[...] = hidden
    run_forward_slots(h_ref, te, w_ref, count, slot_count, channels, store_ref=hs_ref)
    grad_hidden = g_ref[...].astype(F32)
    if not decoder:
        grad_skip = e_ref[...]
        grad_hidden = grad_hidden + contract_cols(grad_skip, side)
        section_out = h_ref[...].astype(BF16)
        grads_scr[slot_count * channels :, :] = contract_rows(section_out, grad_skip)

    gh_ref[...] = grad_hidden
    for slot_index in reversed(range(slot_count)):
        rows = slice(slot_index * channels, (slot_index + 1) * channels)

        @pl.when(slot_index < count)
        def _():
            hidden = hs_ref[slot_index]
            inverse_rms = inverse_rms_of(hidden)
            normed = hidden * inverse_rms
            preact = normed + te
            sigmoid_val = sigmoid(preact)
            grad_hidden = gh_ref[...]
            grad_low = grad_hidden.astype(BF16)
            activated = (preact * sigmoid_val).astype(BF16)
            grads_scr[rows, :] = contract_rows(activated, grad_low)
            grad_act = contract_cols(grad_low, w_ref[rows, :])
            grad_pre = grad_act * sigmoid_val * (1.0 + preact * (1.0 - sigmoid_val))
            gh_ref[...] = grad_hidden + inverse_rms * (
                grad_pre - normed * jnp.mean(grad_pre * normed, axis=-1, keepdims=True)
            )

        @pl.when(slot_index >= count)
        def _():
            grads_scr[rows, :] = jnp.zeros((channels, channels), F32)

    grad_low = gh_ref[...].astype(BF16)
    gprev_ref[...] = grad_low
    if decoder:
        e_out_ref[...] = contract_cols(grad_low, side).astype(BF16)
        grads_scr[slot_count * channels :, :] = contract_rows(skip_ref[...], grad_low)

    @pl.when(owned)
    def _():
        grads_copy = pltpu.make_async_copy(grads_scr, grads_out_ref, sem)
        grads_copy.start()
        grads_copy.wait()


PARAMS = pltpu.CompilerParams(vmem_limit_bytes=48 * 1024 * 1024)


VMEM_SPEC = pl.BlockSpec(memory_space=pltpu.VMEM)
SMEM_SPEC = pl.BlockSpec(memory_space=pltpu.SMEM)
ANY_SPEC = pl.BlockSpec(memory_space=pl.ANY)


def stage_forward(flags, a, te, weights, skip_in, decoder, slot_count, channels, stage):
    mine, sibling = weights
    rows = a.shape[0]
    kernel = functools.partial(
        forward_kernel, decoder=decoder, slot_count=slot_count, channels=channels, stage=stage
    )
    return pl.pallas_call(
        kernel,
        out_shape=(
            jax.ShapeDtypeStruct((rows, channels), BF16),
            jax.ShapeDtypeStruct((rows, channels), BF16),
        ),
        in_specs=[SMEM_SPEC, VMEM_SPEC, VMEM_SPEC, ANY_SPEC, ANY_SPEC, VMEM_SPEC],
        out_specs=(VMEM_SPEC, VMEM_SPEC),
        scratch_shapes=[
            pltpu.VMEM((rows, channels), F32),
            pltpu.VMEM(((slot_count + 1) * channels, channels), BF16),
            pltpu.SemaphoreType.DMA((2,)),
        ],
        compiler_params=PARAMS,
    )(flags, a, te, mine, sibling, skip_in)


def stage_backward(
    flags, a, te, weights, skip_in, grad_out, grad_skip, grads_acc, decoder,
    slot_count, channels, stage
):
    mine, sibling = weights
    rows = a.shape[0]
    kernel = functools.partial(
        backward_kernel, decoder=decoder, slot_count=slot_count, channels=channels, stage=stage
    )
    return pl.pallas_call(
        kernel,
        out_shape=(
            jax.ShapeDtypeStruct((rows, channels), BF16),
            jax.ShapeDtypeStruct((rows, channels), BF16),
            jax.ShapeDtypeStruct(grads_acc.shape, F32),
        ),
        in_specs=[SMEM_SPEC, VMEM_SPEC, VMEM_SPEC, ANY_SPEC, ANY_SPEC] + [VMEM_SPEC] * 3
        + [ANY_SPEC],
        out_specs=(VMEM_SPEC, VMEM_SPEC, ANY_SPEC),
        scratch_shapes=[
            pltpu.VMEM((rows, channels), F32),
            pltpu.VMEM((slot_count, rows, channels), F32),
            pltpu.VMEM((rows, channels), F32),
            pltpu.VMEM(grads_acc.shape, F32),
            pltpu.SemaphoreType.DMA(()),
            pltpu.VMEM(((slot_count + 1) * channels, channels), BF16),
            pltpu.SemaphoreType.DMA((2,)),
        ],
        input_output_aliases={8: 2},
        compiler_params=PARAMS,
    )(flags, a, te, mine, sibling, skip_in, grad_out, grad_skip, grads_acc)


def on_device(clean_latents, target_noise, timesteps, layer_counts, section_weights):
    section_count = lax.axis_size("section")
    half_count = section_count // 2
    section_index = lax.axis_index("section")
    micro_count, row_count, channels = clean_latents.shape
    rows = micro_count * row_count
    weights = section_weights[0]
    slot_count = weights.shape[0] // channels - 1
    step_values = timesteps[0]

    rep_count = lax.axis_size("rep")
    core_index = lax.axis_index("rep") % 2
    half_rows = weights.shape[0] // 2
    my_half = lax.dynamic_slice_in_dim(weights, core_index * half_rows, half_rows, 0)
    count_rows = jnp.zeros((16, channels), BF16).at[0, 0].set(layer_counts[0].astype(BF16))
    halves_by_section = lax.all_gather(jnp.concatenate([my_half, count_rows]), "section")
    all_counts = halves_by_section[:, half_rows, 0].astype(jnp.int32)
    chip_swap = [(i, i ^ 1) for i in range(rep_count)]
    sibling_halves = lax.ppermute(halves_by_section, "rep", chip_swap)
    all_weights = (halves_by_section, sibling_halves)

    signal_level = noise_level(step_values)[:, None, None]
    noisy_input = (
        jnp.sqrt(signal_level) * clean_latents.astype(jnp.float32)
        + jnp.sqrt(1.0 - signal_level) * target_noise.astype(jnp.float32)
    ).astype(BF16).reshape(rows, channels)
    target_rows = target_noise.reshape(rows, channels)
    time_embed = jnp.broadcast_to(
        time_features(step_values, channels)[:, None, :], (micro_count, row_count, channels)
    ).reshape(rows, channels)

    def flags_at(stage):
        owned = (section_index == stage).astype(jnp.int32)
        return jnp.stack([all_counts[stage], owned, core_index])


    blank = jnp.zeros((rows, channels), BF16)
    current = noisy_input
    section_inputs = []
    skips = {}
    for stage in range(section_count):
        is_decoder = stage >= half_count
        section_inputs.append(current)
        skip_in = skips[section_count - 1 - stage] if is_decoder else blank
        current, skip_out = stage_forward(
            flags_at(stage), current, time_embed, all_weights, skip_in,
            is_decoder, slot_count, channels, stage,
        )
        if not is_decoder:
            skips[stage] = skip_out

    grad_current = (
        (current.astype(jnp.float32) - target_rows.astype(jnp.float32)) / rows
    ).astype(BF16)
    grad_skips = {}
    weight_grads = jnp.zeros(((slot_count + 1) * channels, channels), F32)
    for stage in reversed(range(section_count)):
        is_decoder = stage >= half_count
        skip_in = skips[section_count - 1 - stage] if is_decoder else blank
        grad_skip = blank if is_decoder else grad_skips[section_count - 1 - stage]
        grad_current, e_out, weight_grads = stage_backward(
            flags_at(stage), section_inputs[stage], time_embed, all_weights, skip_in,
            grad_current, grad_skip, weight_grads, is_decoder, slot_count, channels, stage,
        )
        if is_decoder:
            grad_skips[stage] = e_out

    return lax.psum_scatter(weight_grads, "rep", scatter_dimension=0, tiled=True)[None]


def solution(mesh):
    placed = (
        P(None, "rep", None),
        P(None, "rep", None),
        P("rep", None),
        P("section"),
        P("section", None, None),
    )
    return jax.shard_map(
        on_device, mesh=mesh, in_specs=placed, out_specs=P("section", "rep", None), check_vma=False
    )
```

```python
import functools
import math

import jax
import jax.numpy as jnp
from jax import lax
from jax.experimental import pallas as pl
from jax.experimental.pallas import tpu as pltpu
from jax.sharding import PartitionSpec as P

EPSILON = 1e-06
F32 = jnp.float32
BF16 = jnp.bfloat16


def noise_level(step_values):
    phase = (step_values.astype(jnp.float32) / 1000.0 + 0.008) / 1.008 * (math.pi / 2.0)
    return jnp.cos(phase) ** 2


def time_features(step_values, channels):
    half_width = channels // 2
    ladder = jnp.exp(-math.log(10000.0) * jnp.arange(half_width, dtype=jnp.float32) / half_width)
    angles = step_values.astype(jnp.float32)[..., None] * ladder
    return jnp.concatenate([jnp.sin(angles), jnp.cos(angles)], axis=-1)


def contract_rows(left, right):
    return lax.dot_general(left, right, (((0,), (0,)), ((), ())), preferred_element_type=F32)


def contract_cols(left, right):
    return lax.dot_general(left, right, (((1,), (1,)), ((), ())), preferred_element_type=F32)


def plain_product(left, right):
    return lax.dot_general(left, right, (((1,), (0,)), ((), ())), preferred_element_type=F32)


def sigmoid(value):
    return 1.0 / (1.0 + jnp.exp(-value))


def inverse_rms_of(hidden):
    return lax.rsqrt(jnp.mean(hidden * hidden, axis=-1, keepdims=True) + EPSILON)


def run_forward_slots(h_ref, te, w_ref, count, slot_count, channels, store_ref=None):
    for slot_index in range(slot_count):

        @pl.when(slot_index < count)
        def _():
            hidden = h_ref[...]
            if store_ref is not None:
                store_ref[slot_index] = hidden
            preact = hidden * inverse_rms_of(hidden) + te
            activated = (preact * sigmoid(preact)).astype(BF16)
            weight = w_ref[slot_index * channels : (slot_index + 1) * channels, :]
            h_ref[...] = hidden + plain_product(activated, weight)


def load_weights(own_hbm, fetched, w_ref, sems, core, shift):
    half_rows = w_ref.shape[0] // 2
    mine_at = pl.multiple_of(core * half_rows, 16)
    sibling_at = pl.multiple_of((1 - core) * half_rows, 16)

    @pl.when(shift == 0)
    def _():
        copy = pltpu.make_async_copy(own_hbm, w_ref, sems.at[0])
        copy.start()
        copy.wait()

    for index, (mine_hbm, sibling_hbm) in enumerate(fetched):

        @pl.when(shift == index + 1)
        def _():
            copies = [
                pltpu.make_async_copy(
                    mine_hbm.at[pl.ds(0, half_rows)], w_ref.at[pl.ds(mine_at, half_rows)],
                    sems.at[0],
                ),
                pltpu.make_async_copy(
                    sibling_hbm.at[pl.ds(0, half_rows)], w_ref.at[pl.ds(sibling_at, half_rows)],
                    sems.at[1],
                ),
            ]
            for copy in copies:
                copy.start()
            for copy in copies:
                copy.wait()


def split_weight_refs(refs, fetched_count):
    own_hbm = refs[0]
    fetched = [
        (refs[1 + 2 * index], refs[2 + 2 * index]) for index in range(fetched_count)
    ]
    return own_hbm, fetched, refs[1 + 2 * fetched_count :]


def forward_kernel(flags_ref, a_ref, te_ref, *refs, decoder, slot_count, channels, fetched_count):
    own_hbm, fetched, refs = split_weight_refs(refs, fetched_count)
    skip_ref, out_ref, skip_out_ref, h_ref, w_ref, w_sems = refs
    load_weights(own_hbm, fetched, w_ref, w_sems, flags_ref[2], flags_ref[3])
    count = flags_ref[0]
    side = w_ref[slot_count * channels :, :]
    hidden = a_ref[...].astype(F32)
    if decoder:
        hidden = hidden + plain_product(skip_ref[...], side)
    h_ref[...] = hidden
    run_forward_slots(h_ref, te_ref[...], w_ref, count, slot_count, channels)
    section_out = h_ref[...].astype(BF16)
    out_ref[...] = section_out
    if not decoder:
        skip_out_ref[...] = plain_product(section_out, side).astype(BF16)


def backward_kernel(flags_ref, a_ref, te_ref, *refs, decoder, slot_count, channels, fetched_count):
    own_hbm, fetched, refs = split_weight_refs(refs, fetched_count)
    (skip_ref, g_ref, e_ref, grads_acc_ref, gprev_ref, e_out_ref, grads_out_ref,
     h_ref, hs_ref, gh_ref, grads_scr, sem, w_ref, w_sems) = refs
    load_weights(own_hbm, fetched, w_ref, w_sems, flags_ref[2], flags_ref[3])
    count = flags_ref[0]
    owned = flags_ref[1] == 1
    side = w_ref[slot_count * channels :, :]
    te = te_ref[...]
    hidden = a_ref[...].astype(F32)
    if decoder:
        hidden = hidden + plain_product(skip_ref[...], side)
    h_ref[...] = hidden
    run_forward_slots(h_ref, te, w_ref, count, slot_count, channels, store_ref=hs_ref)
    grad_hidden = g_ref[...].astype(F32)
    if not decoder:
        grad_skip = e_ref[...]
        grad_hidden = grad_hidden + contract_cols(grad_skip, side)
        section_out = h_ref[...].astype(BF16)
        grads_scr[slot_count * channels :, :] = contract_rows(section_out, grad_skip)

    gh_ref[...] = grad_hidden
    for slot_index in reversed(range(slot_count)):
        rows = slice(slot_index * channels, (slot_index + 1) * channels)

        @pl.when(slot_index < count)
        def _():
            hidden = hs_ref[slot_index]
            inverse_rms = inverse_rms_of(hidden)
            normed = hidden * inverse_rms
            preact = normed + te
            sigmoid_val = sigmoid(preact)
            grad_hidden = gh_ref[...]
            grad_low = grad_hidden.astype(BF16)
            activated = (preact * sigmoid_val).astype(BF16)
            grads_scr[rows, :] = contract_rows(activated, grad_low)
            grad_act = contract_cols(grad_low, w_ref[rows, :])
            grad_pre = grad_act * sigmoid_val * (1.0 + preact * (1.0 - sigmoid_val))
            gh_ref[...] = grad_hidden + inverse_rms * (
                grad_pre - normed * jnp.mean(grad_pre * normed, axis=-1, keepdims=True)
            )

        @pl.when(slot_index >= count)
        def _():
            grads_scr[rows, :] = jnp.zeros((channels, channels), F32)

    grad_low = gh_ref[...].astype(BF16)
    gprev_ref[...] = grad_low
    if decoder:
        e_out_ref[...] = contract_cols(grad_low, side).astype(BF16)
        grads_scr[slot_count * channels :, :] = contract_rows(skip_ref[...], grad_low)

    @pl.when(owned)
    def _():
        grads_copy = pltpu.make_async_copy(grads_scr, grads_out_ref, sem)
        grads_copy.start()
        grads_copy.wait()


PARAMS = pltpu.CompilerParams(vmem_limit_bytes=48 * 1024 * 1024)


VMEM_SPEC = pl.BlockSpec(memory_space=pltpu.VMEM)
SMEM_SPEC = pl.BlockSpec(memory_space=pltpu.SMEM)
ANY_SPEC = pl.BlockSpec(memory_space=pl.ANY)


def weight_operands(weights):
    own, fetched = weights
    flat = [own]
    for pair in fetched:
        flat.extend(pair)
    return flat, len(fetched)


def stage_forward(flags, a, te, weights, skip_in, decoder, slot_count, channels):
    rows = a.shape[0]
    flat, fetched_count = weight_operands(weights)
    kernel = functools.partial(
        forward_kernel, decoder=decoder, slot_count=slot_count, channels=channels,
        fetched_count=fetched_count,
    )
    return pl.pallas_call(
        kernel,
        out_shape=(
            jax.ShapeDtypeStruct((rows, channels), BF16),
            jax.ShapeDtypeStruct((rows, channels), BF16),
        ),
        in_specs=[SMEM_SPEC, VMEM_SPEC, VMEM_SPEC] + [ANY_SPEC] * len(flat) + [VMEM_SPEC],
        out_specs=(VMEM_SPEC, VMEM_SPEC),
        scratch_shapes=[
            pltpu.VMEM((rows, channels), F32),
            pltpu.VMEM(((slot_count + 1) * channels, channels), BF16),
            pltpu.SemaphoreType.DMA((2,)),
        ],
        compiler_params=PARAMS,
    )(flags, a, te, *flat, skip_in)


def stage_backward(
    flags, a, te, weights, skip_in, grad_out, grad_skip, grads_acc, decoder,
    slot_count, channels
):
    rows = a.shape[0]
    flat, fetched_count = weight_operands(weights)
    kernel = functools.partial(
        backward_kernel, decoder=decoder, slot_count=slot_count, channels=channels,
        fetched_count=fetched_count,
    )
    return pl.pallas_call(
        kernel,
        out_shape=(
            jax.ShapeDtypeStruct((rows, channels), BF16),
            jax.ShapeDtypeStruct((rows, channels), BF16),
            jax.ShapeDtypeStruct(grads_acc.shape, F32),
        ),
        in_specs=[SMEM_SPEC, VMEM_SPEC, VMEM_SPEC] + [ANY_SPEC] * len(flat)
        + [VMEM_SPEC] * 3 + [ANY_SPEC],
        out_specs=(VMEM_SPEC, VMEM_SPEC, ANY_SPEC),
        scratch_shapes=[
            pltpu.VMEM((rows, channels), F32),
            pltpu.VMEM((slot_count, rows, channels), F32),
            pltpu.VMEM((rows, channels), F32),
            pltpu.VMEM(grads_acc.shape, F32),
            pltpu.SemaphoreType.DMA(()),
            pltpu.VMEM(((slot_count + 1) * channels, channels), BF16),
            pltpu.SemaphoreType.DMA((2,)),
        ],
        input_output_aliases={3 + len(flat) + 3: 2},
        compiler_params=PARAMS,
    )(flags, a, te, *flat, skip_in, grad_out, grad_skip, grads_acc)


def on_device(clean_latents, target_noise, timesteps, layer_counts, section_weights):
    section_count = lax.axis_size("section")
    half_count = section_count // 2
    section_index = lax.axis_index("section")
    micro_count, row_count, channels = clean_latents.shape
    rows = micro_count * row_count
    weights = section_weights[0]
    slot_count = weights.shape[0] // channels - 1
    step_values = timesteps[0]

    rep_count = lax.axis_size("rep")
    core_index = lax.axis_index("rep") % 2
    half_rows = weights.shape[0] // 2
    my_half = lax.dynamic_slice_in_dim(weights, core_index * half_rows, half_rows, 0)
    count_rows = jnp.broadcast_to(layer_counts[0].astype(BF16), (16, channels))
    my_block = jnp.concatenate([my_half, count_rows])
    chip_swap = [(i, i ^ 1) for i in range(rep_count)]
    fetched = []
    counts_by_shift = [layer_counts[0]]
    for shift in range(1, section_count):
        pairs = [(i, (i + shift) % section_count) for i in range(section_count)]
        mine = lax.ppermute(my_block, "section", pairs)
        sibling = lax.ppermute(mine, "rep", chip_swap)
        fetched.append((mine, sibling))
        counts_by_shift.append(jnp.max(mine[half_rows:]).astype(jnp.int32))
    counts_by_shift = jnp.stack(counts_by_shift)
    all_weights = (weights, fetched)

    signal_level = noise_level(step_values)[:, None, None]
    noisy_input = (
        jnp.sqrt(signal_level) * clean_latents.astype(jnp.float32)
        + jnp.sqrt(1.0 - signal_level) * target_noise.astype(jnp.float32)
    ).astype(BF16).reshape(rows, channels)
    target_rows = target_noise.reshape(rows, channels)
    time_embed = jnp.broadcast_to(
        time_features(step_values, channels)[:, None, :], (micro_count, row_count, channels)
    ).reshape(rows, channels)

    def flags_at(stage):
        owned = (section_index == stage).astype(jnp.int32)
        shift = (section_index - stage) % section_count
        return jnp.stack([counts_by_shift[shift], owned, core_index, shift])


    blank = jnp.zeros((rows, channels), BF16)
    current = noisy_input
    section_inputs = []
    skips = {}
    for stage in range(section_count):
        is_decoder = stage >= half_count
        section_inputs.append(current)
        skip_in = skips[section_count - 1 - stage] if is_decoder else blank
        current, skip_out = stage_forward(
            flags_at(stage), current, time_embed, all_weights, skip_in,
            is_decoder, slot_count, channels,
        )
        if not is_decoder:
            skips[stage] = skip_out

    grad_current = (
        (current.astype(jnp.float32) - target_rows.astype(jnp.float32)) / rows
    ).astype(BF16)
    grad_skips = {}
    weight_grads = jnp.zeros(((slot_count + 1) * channels, channels), F32)
    for stage in reversed(range(section_count)):
        is_decoder = stage >= half_count
        skip_in = skips[section_count - 1 - stage] if is_decoder else blank
        grad_skip = blank if is_decoder else grad_skips[section_count - 1 - stage]
        grad_current, e_out, weight_grads = stage_backward(
            flags_at(stage), section_inputs[stage], time_embed, all_weights, skip_in,
            grad_current, grad_skip, weight_grads, is_decoder, slot_count, channels,
        )
        if is_decoder:
            grad_skips[stage] = e_out

    return lax.psum_scatter(weight_grads, "rep", scatter_dimension=0, tiled=True)[None]


def solution(mesh):
    placed = (
        P(None, "rep", None),
        P(None, "rep", None),
        P("rep", None),
        P("section"),
        P("section", None, None),
    )
    return jax.shard_map(
        on_device, mesh=mesh, in_specs=placed, out_specs=P("section", "rep", None), check_vma=False
    )
```

```python
import functools
import math

import jax
import jax.numpy as jnp
from jax import lax
from jax.experimental import pallas as pl
from jax.experimental.pallas import tpu as pltpu
from jax.sharding import PartitionSpec as P

EPSILON = 1e-06
F32 = jnp.float32
BF16 = jnp.bfloat16


def noise_level(step_values):
    phase = (step_values.astype(jnp.float32) / 1000.0 + 0.008) / 1.008 * (math.pi / 2.0)
    return jnp.cos(phase) ** 2


def time_features(step_values, channels):
    half_width = channels // 2
    ladder = jnp.exp(-math.log(10000.0) * jnp.arange(half_width, dtype=jnp.float32) / half_width)
    angles = step_values.astype(jnp.float32)[..., None] * ladder
    return jnp.concatenate([jnp.sin(angles), jnp.cos(angles)], axis=-1)


def contract_rows(left, right):
    return lax.dot_general(left, right, (((0,), (0,)), ((), ())), preferred_element_type=F32)


def contract_cols(left, right):
    return lax.dot_general(left, right, (((1,), (1,)), ((), ())), preferred_element_type=F32)


def plain_product(left, right):
    return lax.dot_general(left, right, (((1,), (0,)), ((), ())), preferred_element_type=F32)


def sigmoid(value):
    return 1.0 / (1.0 + jnp.exp(-value))


def inverse_rms_of(hidden):
    return lax.rsqrt(jnp.mean(hidden * hidden, axis=-1, keepdims=True) + EPSILON)


def run_forward_slots(h_ref, te, w_ref, count, slot_count, channels, store_ref=None):
    for slot_index in range(slot_count):

        @pl.when(slot_index < count)
        def _():
            hidden = h_ref[...]
            if store_ref is not None:
                store_ref[slot_index] = hidden
            preact = hidden * inverse_rms_of(hidden) + te
            activated = (preact * sigmoid(preact)).astype(BF16)
            weight = w_ref[slot_index * channels : (slot_index + 1) * channels, :]
            h_ref[...] = hidden + plain_product(activated, weight)


def load_weights(own_hbm, fetched, w_ref, sems, core, shift):
    half_rows = w_ref.shape[0] // 2
    mine_at = pl.multiple_of(core * half_rows, 16)
    sibling_at = pl.multiple_of((1 - core) * half_rows, 16)

    @pl.when(shift == 0)
    def _():
        copy = pltpu.make_async_copy(own_hbm, w_ref, sems.at[0])
        copy.start()
        copy.wait()

    for index, (mine_hbm, sibling_hbm) in enumerate(fetched):

        @pl.when(shift == index + 1)
        def _():
            copies = [
                pltpu.make_async_copy(
                    mine_hbm.at[pl.ds(0, half_rows)], w_ref.at[pl.ds(mine_at, half_rows)],
                    sems.at[0],
                ),
                pltpu.make_async_copy(
                    sibling_hbm.at[pl.ds(0, half_rows)], w_ref.at[pl.ds(sibling_at, half_rows)],
                    sems.at[1],
                ),
            ]
            for copy in copies:
                copy.start()
            for copy in copies:
                copy.wait()


def split_weight_refs(refs, fetched_count):
    own_hbm = refs[0]
    fetched = [
        (refs[1 + 2 * index], refs[2 + 2 * index]) for index in range(fetched_count)
    ]
    return own_hbm, fetched, refs[1 + 2 * fetched_count :]


def forward_kernel(flags_ref, a_ref, te_ref, *refs, decoder, slot_count, channels, fetched_count):
    own_hbm, fetched, refs = split_weight_refs(refs, fetched_count)
    skip_ref, out_ref, skip_out_ref, h_ref, w_ref, w_sems = refs
    load_weights(own_hbm, fetched, w_ref, w_sems, flags_ref[2], flags_ref[3])
    count = flags_ref[0]
    side = w_ref[slot_count * channels :, :]
    hidden = a_ref[...].astype(F32)
    if decoder:
        hidden = hidden + plain_product(skip_ref[...], side)
    h_ref[...] = hidden
    run_forward_slots(h_ref, te_ref[...], w_ref, count, slot_count, channels)
    section_out = h_ref[...].astype(BF16)
    out_ref[...] = section_out
    if not decoder:
        skip_out_ref[...] = plain_product(section_out, side).astype(BF16)


def backward_kernel(flags_ref, a_ref, te_ref, *refs, decoder, slot_count, channels, fetched_count):
    own_hbm, fetched, refs = split_weight_refs(refs, fetched_count)
    (skip_ref, g_ref, e_ref, grads_acc_ref, gprev_ref, e_out_ref, grads_out_ref,
     h_ref, hs_ref, gh_ref, grads_scr, sem, w_ref, w_sems) = refs
    load_weights(own_hbm, fetched, w_ref, w_sems, flags_ref[2], flags_ref[3])
    count = flags_ref[0]
    owned = flags_ref[1] == 1
    side = w_ref[slot_count * channels :, :]
    te = te_ref[...]
    hidden = a_ref[...].astype(F32)
    if decoder:
        hidden = hidden + plain_product(skip_ref[...], side)
    h_ref[...] = hidden
    run_forward_slots(h_ref, te, w_ref, count, slot_count, channels, store_ref=hs_ref)
    grad_hidden = g_ref[...].astype(F32)
    if not decoder:
        grad_skip = e_ref[...]
        grad_hidden = grad_hidden + contract_cols(grad_skip, side)
        section_out = h_ref[...].astype(BF16)
        grads_scr[slot_count * channels :, :] = contract_rows(section_out, grad_skip)

    gh_ref[...] = grad_hidden
    for slot_index in reversed(range(slot_count)):
        rows = slice(slot_index * channels, (slot_index + 1) * channels)

        @pl.when(slot_index < count)
        def _():
            hidden = hs_ref[slot_index]
            inverse_rms = inverse_rms_of(hidden)
            normed = hidden * inverse_rms
            preact = normed + te
            sigmoid_val = sigmoid(preact)
            grad_hidden = gh_ref[...]
            grad_low = grad_hidden.astype(BF16)
            activated = (preact * sigmoid_val).astype(BF16)
            grads_scr[rows, :] = contract_rows(activated, grad_low)
            grad_act = contract_cols(grad_low, w_ref[rows, :])
            grad_pre = grad_act * sigmoid_val * (1.0 + preact * (1.0 - sigmoid_val))
            gh_ref[...] = grad_hidden + inverse_rms * (
                grad_pre - normed * jnp.mean(grad_pre * normed, axis=-1, keepdims=True)
            )

        @pl.when(slot_index >= count)
        def _():
            grads_scr[rows, :] = jnp.zeros((channels, channels), F32)

    grad_low = gh_ref[...].astype(BF16)
    gprev_ref[...] = grad_low
    if decoder:
        e_out_ref[...] = contract_cols(grad_low, side).astype(BF16)
        grads_scr[slot_count * channels :, :] = contract_rows(skip_ref[...], grad_low)

    @pl.when(owned)
    def _():
        grads_copy = pltpu.make_async_copy(grads_scr, grads_out_ref, sem)
        grads_copy.start()
        grads_copy.wait()


PARAMS = pltpu.CompilerParams(vmem_limit_bytes=48 * 1024 * 1024)


VMEM_SPEC = pl.BlockSpec(memory_space=pltpu.VMEM)
SMEM_SPEC = pl.BlockSpec(memory_space=pltpu.SMEM)
ANY_SPEC = pl.BlockSpec(memory_space=pl.ANY)


def weight_operands(weights):
    own, fetched = weights
    flat = [own]
    for pair in fetched:
        flat.extend(pair)
    return flat, len(fetched)


def stage_forward(flags, a, te, weights, skip_in, decoder, slot_count, channels):
    rows = a.shape[0]
    flat, fetched_count = weight_operands(weights)
    kernel = functools.partial(
        forward_kernel, decoder=decoder, slot_count=slot_count, channels=channels,
        fetched_count=fetched_count,
    )
    return pl.pallas_call(
        kernel,
        out_shape=(
            jax.ShapeDtypeStruct((rows, channels), BF16),
            jax.ShapeDtypeStruct((rows, channels), BF16),
        ),
        in_specs=[SMEM_SPEC, VMEM_SPEC, VMEM_SPEC] + [ANY_SPEC] * len(flat) + [VMEM_SPEC],
        out_specs=(VMEM_SPEC, VMEM_SPEC),
        scratch_shapes=[
            pltpu.VMEM((rows, channels), F32),
            pltpu.VMEM(((slot_count + 1) * channels, channels), BF16),
            pltpu.SemaphoreType.DMA((2,)),
        ],
        compiler_params=PARAMS,
    )(flags, a, te, *flat, skip_in)


def stage_backward(
    flags, a, te, weights, skip_in, grad_out, grad_skip, grads_acc, decoder,
    slot_count, channels
):
    rows = a.shape[0]
    flat, fetched_count = weight_operands(weights)
    kernel = functools.partial(
        backward_kernel, decoder=decoder, slot_count=slot_count, channels=channels,
        fetched_count=fetched_count,
    )
    return pl.pallas_call(
        kernel,
        out_shape=(
            jax.ShapeDtypeStruct((rows, channels), BF16),
            jax.ShapeDtypeStruct((rows, channels), BF16),
            jax.ShapeDtypeStruct(grads_acc.shape, F32),
        ),
        in_specs=[SMEM_SPEC, VMEM_SPEC, VMEM_SPEC] + [ANY_SPEC] * len(flat)
        + [VMEM_SPEC] * 3 + [ANY_SPEC],
        out_specs=(VMEM_SPEC, VMEM_SPEC, ANY_SPEC),
        scratch_shapes=[
            pltpu.VMEM((rows, channels), F32),
            pltpu.VMEM((slot_count, rows, channels), F32),
            pltpu.VMEM((rows, channels), F32),
            pltpu.VMEM(grads_acc.shape, F32),
            pltpu.SemaphoreType.DMA(()),
            pltpu.VMEM(((slot_count + 1) * channels, channels), BF16),
            pltpu.SemaphoreType.DMA((2,)),
        ],
        input_output_aliases={3 + len(flat) + 3: 2},
        compiler_params=PARAMS,
    )(flags, a, te, *flat, skip_in, grad_out, grad_skip, grads_acc)


def on_device(clean_latents, target_noise, timesteps, layer_counts, section_weights):
    section_count = lax.axis_size("section")
    half_count = section_count // 2
    section_index = lax.axis_index("section")
    micro_count, row_count, channels = clean_latents.shape
    rows = micro_count * row_count
    weights = section_weights[0]
    slot_count = weights.shape[0] // channels - 1
    step_values = timesteps[0]

    rep_count = lax.axis_size("rep")
    core_index = lax.axis_index("rep") % 2
    half_rows = weights.shape[0] // 2
    my_half = lax.dynamic_slice_in_dim(weights, core_index * half_rows, half_rows, 0)
    count_rows = jnp.broadcast_to(layer_counts[0].astype(BF16), (16, channels))
    block_rows = half_rows + 16

    def tiles_of(value):
        return value.reshape(block_rows // 16, 16, channels)

    def rows_of(value):
        return value.reshape(block_rows, channels)

    my_block = tiles_of(jnp.concatenate([my_half, count_rows]))
    chip_swap = [(i, i ^ 1) for i in range(rep_count)]
    fetched = []
    counts_by_shift = [layer_counts]
    for shift in range(1, section_count):
        pairs = [(i, (i + shift) % section_count) for i in range(section_count)]
        mine = lax.ppermute(my_block, "section", pairs)
        sibling = lax.ppermute(mine, "rep", chip_swap)
        fetched.append((rows_of(mine), rows_of(sibling)))
        counts_by_shift.append(lax.ppermute(layer_counts, "section", pairs))
    counts_by_shift = jnp.concatenate(counts_by_shift)
    all_weights = (weights, fetched)

    signal_level = noise_level(step_values)[:, None, None]
    noisy_input = (
        jnp.sqrt(signal_level) * clean_latents.astype(jnp.float32)
        + jnp.sqrt(1.0 - signal_level) * target_noise.astype(jnp.float32)
    ).astype(BF16).reshape(rows, channels)
    target_rows = target_noise.reshape(rows, channels)
    time_embed = jnp.broadcast_to(
        time_features(step_values, channels)[:, None, :], (micro_count, row_count, channels)
    ).reshape(rows, channels)

    def flags_at(stage):
        owned = (section_index == stage).astype(jnp.int32)
        shift = (section_index - stage) % section_count
        return jnp.stack([counts_by_shift[shift], owned, core_index, shift])


    blank = jnp.zeros((rows, channels), BF16)
    current = noisy_input
    section_inputs = []
    skips = {}
    for stage in range(section_count):
        is_decoder = stage >= half_count
        section_inputs.append(current)
        skip_in = skips[section_count - 1 - stage] if is_decoder else blank
        current, skip_out = stage_forward(
            flags_at(stage), current, time_embed, all_weights, skip_in,
            is_decoder, slot_count, channels,
        )
        if not is_decoder:
            skips[stage] = skip_out

    grad_current = (
        (current.astype(jnp.float32) - target_rows.astype(jnp.float32)) / rows
    ).astype(BF16)
    grad_skips = {}
    weight_grads = jnp.zeros(((slot_count + 1) * channels, channels), F32)
    for stage in reversed(range(section_count)):
        is_decoder = stage >= half_count
        skip_in = skips[section_count - 1 - stage] if is_decoder else blank
        grad_skip = blank if is_decoder else grad_skips[section_count - 1 - stage]
        grad_current, e_out, weight_grads = stage_backward(
            flags_at(stage), section_inputs[stage], time_embed, all_weights, skip_in,
            grad_current, grad_skip, weight_grads, is_decoder, slot_count, channels,
        )
        if is_decoder:
            grad_skips[stage] = e_out

    return lax.psum_scatter(weight_grads, "rep", scatter_dimension=0, tiled=True)[None]


def solution(mesh):
    placed = (
        P(None, "rep", None),
        P(None, "rep", None),
        P("rep", None),
        P("section"),
        P("section", None, None),
    )
    return jax.shard_map(
        on_device, mesh=mesh, in_specs=placed, out_specs=P("section", "rep", None), check_vma=False
    )
```

```python
import functools
import math

import jax
import jax.numpy as jnp
from jax import lax
from jax.experimental import pallas as pl
from jax.experimental.pallas import tpu as pltpu
from jax.sharding import PartitionSpec as P

EPSILON = 1e-06
F32 = jnp.float32
BF16 = jnp.bfloat16


def noise_level(step_values):
    phase = (step_values.astype(jnp.float32) / 1000.0 + 0.008) / 1.008 * (math.pi / 2.0)
    return jnp.cos(phase) ** 2


def time_features(step_values, channels):
    half_width = channels // 2
    ladder = jnp.exp(-math.log(10000.0) * jnp.arange(half_width, dtype=jnp.float32) / half_width)
    angles = step_values.astype(jnp.float32)[..., None] * ladder
    return jnp.concatenate([jnp.sin(angles), jnp.cos(angles)], axis=-1)


def contract_rows(left, right):
    return lax.dot_general(left, right, (((0,), (0,)), ((), ())), preferred_element_type=F32)


def contract_cols(left, right):
    return lax.dot_general(left, right, (((1,), (1,)), ((), ())), preferred_element_type=F32)


def plain_product(left, right):
    return lax.dot_general(left, right, (((1,), (0,)), ((), ())), preferred_element_type=F32)


def sigmoid(value):
    return 1.0 / (1.0 + jnp.exp(-value))


def inverse_rms_of(hidden):
    return lax.rsqrt(jnp.mean(hidden * hidden, axis=-1, keepdims=True) + EPSILON)


def run_forward_slots(h_ref, te, w_ref, count, slot_count, channels, store_ref=None):
    for slot_index in range(slot_count):

        @pl.when(slot_index < count)
        def _():
            hidden = h_ref[...]
            if store_ref is not None:
                store_ref[slot_index] = hidden
            preact = hidden * inverse_rms_of(hidden) + te
            activated = (preact * sigmoid(preact)).astype(BF16)
            weight = w_ref[slot_index * channels : (slot_index + 1) * channels, :]
            h_ref[...] = hidden + plain_product(activated, weight)


def load_weights(own_hbm, fetched, w_ref, sems, core, shift):
    half_rows = w_ref.shape[0] // 2
    mine_at = pl.multiple_of(core * half_rows, 16)
    sibling_at = pl.multiple_of((1 - core) * half_rows, 16)

    @pl.when(shift == 0)
    def _():
        copy = pltpu.make_async_copy(own_hbm.at[0], w_ref, sems.at[0])
        copy.start()
        copy.wait()

    for index, (mine_hbm, sibling_hbm) in enumerate(fetched):

        @pl.when(shift == index + 1)
        def _():
            copies = [
                pltpu.make_async_copy(
                    mine_hbm.at[pl.ds(0, half_rows)], w_ref.at[pl.ds(mine_at, half_rows)],
                    sems.at[0],
                ),
                pltpu.make_async_copy(
                    sibling_hbm.at[pl.ds(0, half_rows)], w_ref.at[pl.ds(sibling_at, half_rows)],
                    sems.at[1],
                ),
            ]
            for copy in copies:
                copy.start()
            for copy in copies:
                copy.wait()


def split_weight_refs(refs, fetched_count):
    own_hbm = refs[0]
    fetched = [
        (refs[1 + 2 * index], refs[2 + 2 * index]) for index in range(fetched_count)
    ]
    return own_hbm, fetched, refs[1 + 2 * fetched_count :]


def read_table(table_ref, stage, section_count):
    section_index = table_ref[section_count]
    shift = lax.rem(section_index - stage + section_count, section_count)
    return table_ref[shift], section_index == stage, table_ref[section_count + 1], shift


def forward_kernel(
    table_ref, a_ref, te_ref, *refs, decoder, slot_count, channels, fetched_count, stage
):
    own_hbm, fetched, refs = split_weight_refs(refs, fetched_count)
    skip_ref, out_ref, skip_out_ref, h_ref, w_ref, w_sems = refs
    count, unused_owned, core, shift = read_table(table_ref, stage, fetched_count + 1)
    load_weights(own_hbm, fetched, w_ref, w_sems, core, shift)
    side = w_ref[slot_count * channels :, :]
    hidden = a_ref[...].astype(F32)
    if decoder:
        hidden = hidden + plain_product(skip_ref[...], side)
    h_ref[...] = hidden
    run_forward_slots(h_ref, te_ref[...], w_ref, count, slot_count, channels)
    section_out = h_ref[...].astype(BF16)
    out_ref[...] = section_out
    if not decoder:
        skip_out_ref[...] = plain_product(section_out, side).astype(BF16)


def backward_kernel(
    table_ref, a_ref, te_ref, *refs, decoder, slot_count, channels, fetched_count, stage
):
    own_hbm, fetched, refs = split_weight_refs(refs, fetched_count)
    (skip_ref, g_ref, e_ref, grads_acc_ref, gprev_ref, e_out_ref, grads_out_ref,
     h_ref, hs_ref, gh_ref, grads_scr, sem, w_ref, w_sems) = refs
    count, owned, core, shift = read_table(table_ref, stage, fetched_count + 1)
    load_weights(own_hbm, fetched, w_ref, w_sems, core, shift)
    side = w_ref[slot_count * channels :, :]
    te = te_ref[...]
    hidden = a_ref[...].astype(F32)
    if decoder:
        hidden = hidden + plain_product(skip_ref[...], side)
    h_ref[...] = hidden
    run_forward_slots(h_ref, te, w_ref, count, slot_count, channels, store_ref=hs_ref)
    grad_hidden = g_ref[...].astype(F32)
    if not decoder:
        grad_skip = e_ref[...]
        grad_hidden = grad_hidden + contract_cols(grad_skip, side)
        section_out = h_ref[...].astype(BF16)
        grads_scr[slot_count * channels :, :] = contract_rows(section_out, grad_skip)

    gh_ref[...] = grad_hidden
    for slot_index in reversed(range(slot_count)):
        rows = slice(slot_index * channels, (slot_index + 1) * channels)

        @pl.when(slot_index < count)
        def _():
            hidden = hs_ref[slot_index]
            inverse_rms = inverse_rms_of(hidden)
            normed = hidden * inverse_rms
            preact = normed + te
            sigmoid_val = sigmoid(preact)
            grad_hidden = gh_ref[...]
            grad_low = grad_hidden.astype(BF16)
            activated = (preact * sigmoid_val).astype(BF16)
            grads_scr[rows, :] = contract_rows(activated, grad_low)
            grad_act = contract_cols(grad_low, w_ref[rows, :])
            grad_pre = grad_act * sigmoid_val * (1.0 + preact * (1.0 - sigmoid_val))
            gh_ref[...] = grad_hidden + inverse_rms * (
                grad_pre - normed * jnp.mean(grad_pre * normed, axis=-1, keepdims=True)
            )

        @pl.when(slot_index >= count)
        def _():
            grads_scr[rows, :] = jnp.zeros((channels, channels), F32)

    grad_low = gh_ref[...].astype(BF16)
    gprev_ref[...] = grad_low
    if decoder:
        e_out_ref[...] = contract_cols(grad_low, side).astype(BF16)
        grads_scr[slot_count * channels :, :] = contract_rows(skip_ref[...], grad_low)

    @pl.when(owned)
    def _():
        grads_copy = pltpu.make_async_copy(grads_scr, grads_out_ref, sem)
        grads_copy.start()
        grads_copy.wait()


PARAMS = pltpu.CompilerParams(vmem_limit_bytes=48 * 1024 * 1024)


VMEM_SPEC = pl.BlockSpec(memory_space=pltpu.VMEM)
SMEM_SPEC = pl.BlockSpec(memory_space=pltpu.SMEM)
ANY_SPEC = pl.BlockSpec(memory_space=pl.ANY)


def weight_operands(weights):
    own, fetched = weights
    flat = [own]
    for pair in fetched:
        flat.extend(pair)
    return flat, len(fetched)


def stage_forward(flags, a, te, weights, skip_in, decoder, slot_count, channels, stage):
    rows = a.shape[0]
    flat, fetched_count = weight_operands(weights)
    kernel = functools.partial(
        forward_kernel, decoder=decoder, slot_count=slot_count, channels=channels,
        fetched_count=fetched_count, stage=stage,
    )
    return pl.pallas_call(
        kernel,
        out_shape=(
            jax.ShapeDtypeStruct((rows, channels), BF16),
            jax.ShapeDtypeStruct((rows, channels), BF16),
        ),
        in_specs=[SMEM_SPEC, VMEM_SPEC, VMEM_SPEC] + [ANY_SPEC] * len(flat) + [VMEM_SPEC],
        out_specs=(VMEM_SPEC, VMEM_SPEC),
        scratch_shapes=[
            pltpu.VMEM((rows, channels), F32),
            pltpu.VMEM(((slot_count + 1) * channels, channels), BF16),
            pltpu.SemaphoreType.DMA((2,)),
        ],
        compiler_params=PARAMS,
    )(flags, a, te, *flat, skip_in)


def stage_backward(
    flags, a, te, weights, skip_in, grad_out, grad_skip, grads_acc, decoder,
    slot_count, channels, stage
):
    rows = a.shape[0]
    flat, fetched_count = weight_operands(weights)
    kernel = functools.partial(
        backward_kernel, decoder=decoder, slot_count=slot_count, channels=channels,
        fetched_count=fetched_count, stage=stage,
    )
    return pl.pallas_call(
        kernel,
        out_shape=(
            jax.ShapeDtypeStruct((rows, channels), BF16),
            jax.ShapeDtypeStruct((rows, channels), BF16),
            jax.ShapeDtypeStruct(grads_acc.shape, F32),
        ),
        in_specs=[SMEM_SPEC, VMEM_SPEC, VMEM_SPEC] + [ANY_SPEC] * len(flat)
        + [VMEM_SPEC] * 3 + [ANY_SPEC],
        out_specs=(VMEM_SPEC, VMEM_SPEC, ANY_SPEC),
        scratch_shapes=[
            pltpu.VMEM((rows, channels), F32),
            pltpu.VMEM((slot_count, rows, channels), F32),
            pltpu.VMEM((rows, channels), F32),
            pltpu.VMEM(grads_acc.shape, F32),
            pltpu.SemaphoreType.DMA(()),
            pltpu.VMEM(((slot_count + 1) * channels, channels), BF16),
            pltpu.SemaphoreType.DMA((2,)),
        ],
        input_output_aliases={3 + len(flat) + 3: 2},
        compiler_params=PARAMS,
    )(flags, a, te, *flat, skip_in, grad_out, grad_skip, grads_acc)


def on_device(clean_latents, target_noise, timesteps, layer_counts, section_weights):
    section_count = lax.axis_size("section")
    half_count = section_count // 2
    section_index = lax.axis_index("section")
    micro_count, row_count, channels = clean_latents.shape
    rows = micro_count * row_count
    weights = section_weights[0]
    slot_count = weights.shape[0] // channels - 1
    step_values = timesteps[0]

    rep_count = lax.axis_size("rep")
    core_index = lax.axis_index("rep") % 2
    half_rows = weights.shape[0] // 2
    my_half = lax.dynamic_slice_in_dim(weights, core_index * half_rows, half_rows, 0)
    count_rows = jnp.broadcast_to(layer_counts[0].astype(BF16), (16, channels))
    block_rows = half_rows + 16

    def tiles_of(value):
        return value.reshape(block_rows // 16, 16, channels)

    def rows_of(value):
        return value.reshape(block_rows, channels)

    my_block = tiles_of(jnp.concatenate([my_half, count_rows]))
    chip_swap = [(i, i ^ 1) for i in range(rep_count)]
    fetched = []
    counts_by_shift = [layer_counts]
    for shift in range(1, section_count):
        pairs = [(i, (i + shift) % section_count) for i in range(section_count)]
        mine = lax.ppermute(my_block, "section", pairs)
        sibling = lax.ppermute(mine, "rep", chip_swap)
        fetched.append((rows_of(mine), rows_of(sibling)))
        counts_by_shift.append(lax.ppermute(layer_counts, "section", pairs))
    table = jnp.concatenate(
        counts_by_shift
        + [jnp.stack([section_index, core_index]).astype(jnp.int32)]
    )
    all_weights = (section_weights, fetched)

    signal_level = noise_level(step_values)[:, None, None]
    noisy_input = (
        jnp.sqrt(signal_level) * clean_latents.astype(jnp.float32)
        + jnp.sqrt(1.0 - signal_level) * target_noise.astype(jnp.float32)
    ).astype(BF16).reshape(rows, channels)
    target_rows = target_noise.reshape(rows, channels)
    time_embed = jnp.broadcast_to(
        time_features(step_values, channels)[:, None, :], (micro_count, row_count, channels)
    ).reshape(rows, channels)


    blank = jnp.zeros((rows, channels), BF16)
    current = noisy_input
    section_inputs = []
    skips = {}
    for stage in range(section_count):
        is_decoder = stage >= half_count
        section_inputs.append(current)
        skip_in = skips[section_count - 1 - stage] if is_decoder else blank
        current, skip_out = stage_forward(
            table, current, time_embed, all_weights, skip_in,
            is_decoder, slot_count, channels, stage,
        )
        if not is_decoder:
            skips[stage] = skip_out

    grad_current = (
        (current.astype(jnp.float32) - target_rows.astype(jnp.float32)) / rows
    ).astype(BF16)
    grad_skips = {}
    weight_grads = jnp.zeros(((slot_count + 1) * channels, channels), F32)
    for stage in reversed(range(section_count)):
        is_decoder = stage >= half_count
        skip_in = skips[section_count - 1 - stage] if is_decoder else blank
        grad_skip = blank if is_decoder else grad_skips[section_count - 1 - stage]
        grad_current, e_out, weight_grads = stage_backward(
            table, section_inputs[stage], time_embed, all_weights, skip_in,
            grad_current, grad_skip, weight_grads, is_decoder, slot_count, channels, stage,
        )
        if is_decoder:
            grad_skips[stage] = e_out

    return lax.psum_scatter(weight_grads, "rep", scatter_dimension=0, tiled=True)[None]


def solution(mesh):
    placed = (
        P(None, "rep", None),
        P(None, "rep", None),
        P("rep", None),
        P("section"),
        P("section", None, None),
    )
    return jax.shard_map(
        on_device, mesh=mesh, in_specs=placed, out_specs=P("section", "rep", None), check_vma=False
    )
```

```python
import functools
import math

import jax
import jax.numpy as jnp
from jax import lax
from jax.experimental import pallas as pl
from jax.experimental.pallas import tpu as pltpu
from jax.sharding import PartitionSpec as P

EPSILON = 1e-06
F32 = jnp.float32
BF16 = jnp.bfloat16


def noise_level(step_values):
    phase = (step_values.astype(jnp.float32) / 1000.0 + 0.008) / 1.008 * (math.pi / 2.0)
    return jnp.cos(phase) ** 2


def time_features(step_values, channels):
    half_width = channels // 2
    ladder = jnp.exp(-math.log(10000.0) * jnp.arange(half_width, dtype=jnp.float32) / half_width)
    angles = step_values.astype(jnp.float32)[..., None] * ladder
    return jnp.concatenate([jnp.sin(angles), jnp.cos(angles)], axis=-1)


def contract_rows(left, right):
    return lax.dot_general(left, right, (((0,), (0,)), ((), ())), preferred_element_type=F32)


def contract_cols(left, right):
    return lax.dot_general(left, right, (((1,), (1,)), ((), ())), preferred_element_type=F32)


def plain_product(left, right):
    return lax.dot_general(left, right, (((1,), (0,)), ((), ())), preferred_element_type=F32)


def sigmoid(value):
    return 1.0 / (1.0 + jnp.exp(-value))


def inverse_rms_of(hidden):
    return lax.rsqrt(jnp.mean(hidden * hidden, axis=-1, keepdims=True) + EPSILON)


def run_forward_slots(h_ref, te, w_ref, count, slot_count, channels, store_ref=None):
    for slot_index in range(slot_count):

        @pl.when(slot_index < count)
        def _():
            hidden = h_ref[...]
            if store_ref is not None:
                store_ref[slot_index] = hidden
            preact = hidden * inverse_rms_of(hidden) + te
            activated = (preact * sigmoid(preact)).astype(BF16)
            weight = w_ref[slot_index * channels : (slot_index + 1) * channels, :]
            h_ref[...] = hidden + plain_product(activated, weight)


def load_weights(own_hbm, fetched, w_ref, sems, core, shift):
    half_rows = w_ref.shape[0] // 2
    mine_at = pl.multiple_of(core * half_rows, 16)
    sibling_at = pl.multiple_of((1 - core) * half_rows, 16)

    @pl.when(shift == 0)
    def _():
        copy = pltpu.make_async_copy(own_hbm.at[0], w_ref, sems.at[0])
        copy.start()
        copy.wait()

    for index, (mine_hbm, sibling_hbm) in enumerate(fetched):

        @pl.when(shift == index + 1)
        def _():
            copies = [
                pltpu.make_async_copy(
                    mine_hbm.at[pl.ds(0, half_rows)], w_ref.at[pl.ds(mine_at, half_rows)],
                    sems.at[0],
                ),
                pltpu.make_async_copy(
                    sibling_hbm.at[pl.ds(0, half_rows)], w_ref.at[pl.ds(sibling_at, half_rows)],
                    sems.at[1],
                ),
            ]
            for copy in copies:
                copy.start()
            for copy in copies:
                copy.wait()


def split_weight_refs(refs, fetched_count):
    own_hbm = refs[0]
    fetched = [
        (refs[1 + 2 * index], refs[2 + 2 * index]) for index in range(fetched_count)
    ]
    return own_hbm, fetched, refs[1 + 2 * fetched_count :]


def read_table(table_refs, stage, section_count):
    section_index = table_refs[section_count][0]
    shift = lax.rem(section_index - stage + section_count, section_count)
    count = table_refs[0][0]
    for index in range(1, section_count):
        count = jnp.where(shift == index, table_refs[index][0], count)
    return count, section_index == stage, table_refs[section_count + 1][0], shift


def forward_kernel(*refs, decoder, slot_count, channels, fetched_count, stage):
    table_refs = refs[: fetched_count + 3]
    a_ref, te_ref = refs[fetched_count + 3 : fetched_count + 5]
    own_hbm, fetched, refs = split_weight_refs(refs[fetched_count + 5 :], fetched_count)
    skip_ref, out_ref, skip_out_ref, h_ref, w_ref, w_sems = refs
    count, unused_owned, core, shift = read_table(table_refs, stage, fetched_count + 1)
    load_weights(own_hbm, fetched, w_ref, w_sems, core, shift)
    side = w_ref[slot_count * channels :, :]
    hidden = a_ref[...].astype(F32)
    if decoder:
        hidden = hidden + plain_product(skip_ref[...], side)
    h_ref[...] = hidden
    run_forward_slots(h_ref, te_ref[...], w_ref, count, slot_count, channels)
    section_out = h_ref[...].astype(BF16)
    out_ref[...] = section_out
    if not decoder:
        skip_out_ref[...] = plain_product(section_out, side).astype(BF16)


def backward_kernel(*refs, decoder, slot_count, channels, fetched_count, stage, accumulate):
    table_refs = refs[: fetched_count + 3]
    a_ref, te_ref = refs[fetched_count + 3 : fetched_count + 5]
    own_hbm, fetched, refs = split_weight_refs(refs[fetched_count + 5 :], fetched_count)
    if not accumulate:
        refs = refs[:3] + (None,) + refs[3:]
    (skip_ref, g_ref, e_ref, grads_acc_ref, gprev_ref, e_out_ref, grads_out_ref,
     h_ref, hs_ref, gh_ref, grads_scr, sem, w_ref, w_sems) = refs
    count, owned, core, shift = read_table(table_refs, stage, fetched_count + 1)
    load_weights(own_hbm, fetched, w_ref, w_sems, core, shift)
    side = w_ref[slot_count * channels :, :]
    te = te_ref[...]
    hidden = a_ref[...].astype(F32)
    if decoder:
        hidden = hidden + plain_product(skip_ref[...], side)
    h_ref[...] = hidden
    run_forward_slots(h_ref, te, w_ref, count, slot_count, channels, store_ref=hs_ref)
    grad_hidden = g_ref[...].astype(F32)
    if not decoder:
        grad_skip = e_ref[...]
        grad_hidden = grad_hidden + contract_cols(grad_skip, side)
        section_out = h_ref[...].astype(BF16)
        grads_scr[slot_count * channels :, :] = contract_rows(section_out, grad_skip)

    gh_ref[...] = grad_hidden
    for slot_index in reversed(range(slot_count)):
        rows = slice(slot_index * channels, (slot_index + 1) * channels)

        @pl.when(slot_index < count)
        def _():
            hidden = hs_ref[slot_index]
            inverse_rms = inverse_rms_of(hidden)
            normed = hidden * inverse_rms
            preact = normed + te
            sigmoid_val = sigmoid(preact)
            grad_hidden = gh_ref[...]
            grad_low = grad_hidden.astype(BF16)
            activated = (preact * sigmoid_val).astype(BF16)
            grads_scr[rows, :] = contract_rows(activated, grad_low)
            grad_act = contract_cols(grad_low, w_ref[rows, :])
            grad_pre = grad_act * sigmoid_val * (1.0 + preact * (1.0 - sigmoid_val))
            gh_ref[...] = grad_hidden + inverse_rms * (
                grad_pre - normed * jnp.mean(grad_pre * normed, axis=-1, keepdims=True)
            )

        @pl.when(slot_index >= count)
        def _():
            grads_scr[rows, :] = jnp.zeros((channels, channels), F32)

    grad_low = gh_ref[...].astype(BF16)
    gprev_ref[...] = grad_low
    if decoder:
        e_out_ref[...] = contract_cols(grad_low, side).astype(BF16)
        grads_scr[slot_count * channels :, :] = contract_rows(skip_ref[...], grad_low)

    @pl.when(owned)
    def _():
        grads_copy = pltpu.make_async_copy(grads_scr, grads_out_ref, sem)
        grads_copy.start()
        grads_copy.wait()


PARAMS = pltpu.CompilerParams(vmem_limit_bytes=48 * 1024 * 1024)


VMEM_SPEC = pl.BlockSpec(memory_space=pltpu.VMEM)
SMEM_SPEC = pl.BlockSpec(memory_space=pltpu.SMEM)
ANY_SPEC = pl.BlockSpec(memory_space=pl.ANY)


def weight_operands(weights):
    own, fetched = weights
    flat = [own]
    for pair in fetched:
        flat.extend(pair)
    return flat, len(fetched)


def stage_forward(flags, a, te, weights, skip_in, decoder, slot_count, channels, stage):
    rows = a.shape[0]
    flat, fetched_count = weight_operands(weights)
    kernel = functools.partial(
        forward_kernel, decoder=decoder, slot_count=slot_count, channels=channels,
        fetched_count=fetched_count, stage=stage,
    )
    return pl.pallas_call(
        kernel,
        out_shape=(
            jax.ShapeDtypeStruct((rows, channels), BF16),
            jax.ShapeDtypeStruct((rows, channels), BF16),
        ),
        in_specs=[SMEM_SPEC] * len(flags) + [VMEM_SPEC, VMEM_SPEC] + [ANY_SPEC] * len(flat)
        + [VMEM_SPEC],
        out_specs=(VMEM_SPEC, VMEM_SPEC),
        scratch_shapes=[
            pltpu.VMEM((rows, channels), F32),
            pltpu.VMEM(((slot_count + 1) * channels, channels), BF16),
            pltpu.SemaphoreType.DMA((2,)),
        ],
        compiler_params=PARAMS,
    )(*flags, a, te, *flat, skip_in)


def stage_backward(
    flags, a, te, weights, skip_in, grad_out, grad_skip, grads_acc, decoder,
    slot_count, channels, stage
):
    rows = a.shape[0]
    flat, fetched_count = weight_operands(weights)
    kernel = functools.partial(
        backward_kernel, decoder=decoder, slot_count=slot_count, channels=channels,
        fetched_count=fetched_count, stage=stage, accumulate=grads_acc is not None,
    )
    grads_shape = ((slot_count + 1) * channels, channels)
    accumulated = [] if grads_acc is None else [grads_acc]
    leading = len(flags) + 2 + len(flat) + 3
    return pl.pallas_call(
        kernel,
        out_shape=(
            jax.ShapeDtypeStruct((rows, channels), BF16),
            jax.ShapeDtypeStruct((rows, channels), BF16),
            jax.ShapeDtypeStruct(grads_shape, F32),
        ),
        in_specs=[SMEM_SPEC] * len(flags) + [VMEM_SPEC, VMEM_SPEC] + [ANY_SPEC] * len(flat)
        + [VMEM_SPEC] * 3 + [ANY_SPEC] * len(accumulated),
        out_specs=(VMEM_SPEC, VMEM_SPEC, ANY_SPEC),
        scratch_shapes=[
            pltpu.VMEM((rows, channels), F32),
            pltpu.VMEM((slot_count, rows, channels), F32),
            pltpu.VMEM((rows, channels), F32),
            pltpu.VMEM(grads_shape, F32),
            pltpu.SemaphoreType.DMA(()),
            pltpu.VMEM(((slot_count + 1) * channels, channels), BF16),
            pltpu.SemaphoreType.DMA((2,)),
        ],
        input_output_aliases={leading: 2} if accumulated else {},
        compiler_params=PARAMS,
    )(*flags, a, te, *flat, skip_in, grad_out, grad_skip, *accumulated)


def on_device(clean_latents, target_noise, timesteps, layer_counts, section_weights):
    section_count = lax.axis_size("section")
    half_count = section_count // 2
    section_index = lax.axis_index("section")
    micro_count, row_count, channels = clean_latents.shape
    rows = micro_count * row_count
    weights = section_weights[0]
    slot_count = weights.shape[0] // channels - 1
    step_values = timesteps[0]

    rep_count = lax.axis_size("rep")
    core_index = lax.axis_index("rep") % 2
    half_rows = weights.shape[0] // 2
    my_half = lax.dynamic_slice_in_dim(weights, core_index * half_rows, half_rows, 0)
    count_rows = jnp.broadcast_to(layer_counts[0].astype(BF16), (16, channels))
    block_rows = half_rows + 16

    def tiles_of(value):
        return value.reshape(block_rows // 16, 16, channels)

    def rows_of(value):
        return value.reshape(block_rows, channels)

    my_block = tiles_of(jnp.concatenate([my_half, count_rows]))
    chip_swap = [(i, i ^ 1) for i in range(rep_count)]
    shift_pairs = [
        [(i, (i + shift) % section_count) for i in range(section_count)]
        for shift in range(1, section_count)
    ]
    counts_by_shift = [layer_counts] + [
        lax.ppermute(layer_counts, "section", pairs) for pairs in shift_pairs
    ]
    fetched = []
    for pairs in shift_pairs:
        mine = lax.ppermute(my_block, "section", pairs)
        sibling = lax.ppermute(mine, "rep", chip_swap)
        fetched.append((rows_of(mine), rows_of(sibling)))
    table = counts_by_shift + [
        section_index.astype(jnp.int32).reshape(1),
        core_index.astype(jnp.int32).reshape(1),
    ]
    all_weights = (section_weights, fetched)

    signal_level = noise_level(step_values)[:, None, None]
    noisy_input = (
        jnp.sqrt(signal_level) * clean_latents.astype(jnp.float32)
        + jnp.sqrt(1.0 - signal_level) * target_noise.astype(jnp.float32)
    ).astype(BF16).reshape(rows, channels)
    target_rows = target_noise.reshape(rows, channels)
    time_embed = jnp.broadcast_to(
        time_features(step_values, channels)[:, None, :], (micro_count, row_count, channels)
    ).reshape(rows, channels)


    blank = jnp.zeros((rows, channels), BF16)
    current = noisy_input
    section_inputs = []
    skips = {}
    for stage in range(section_count):
        is_decoder = stage >= half_count
        section_inputs.append(current)
        skip_in = skips[section_count - 1 - stage] if is_decoder else blank
        current, skip_out = stage_forward(
            table, current, time_embed, all_weights, skip_in,
            is_decoder, slot_count, channels, stage,
        )
        if not is_decoder:
            skips[stage] = skip_out

    grad_current = (
        (current.astype(jnp.float32) - target_rows.astype(jnp.float32)) / rows
    ).astype(BF16)
    grad_skips = {}
    weight_grads = None
    for stage in reversed(range(section_count)):
        is_decoder = stage >= half_count
        skip_in = skips[section_count - 1 - stage] if is_decoder else blank
        grad_skip = blank if is_decoder else grad_skips[section_count - 1 - stage]
        grad_current, e_out, weight_grads = stage_backward(
            table, section_inputs[stage], time_embed, all_weights, skip_in,
            grad_current, grad_skip, weight_grads, is_decoder, slot_count, channels, stage,
        )
        if is_decoder:
            grad_skips[stage] = e_out

    return lax.psum_scatter(weight_grads, "rep", scatter_dimension=0, tiled=True)[None]


def solution(mesh):
    placed = (
        P(None, "rep", None),
        P(None, "rep", None),
        P("rep", None),
        P("section"),
        P("section", None, None),
    )
    return jax.shard_map(
        on_device, mesh=mesh, in_specs=placed, out_specs=P("section", "rep", None), check_vma=False
    )
```

```python
import functools
import math

import jax
import jax.numpy as jnp
from jax import lax
from jax.experimental import pallas as pl
from jax.experimental.pallas import tpu as pltpu
from jax.sharding import PartitionSpec as P

EPSILON = 1e-06
F32 = jnp.float32
BF16 = jnp.bfloat16


def noise_level(step_values):
    phase = (step_values.astype(jnp.float32) / 1000.0 + 0.008) / 1.008 * (math.pi / 2.0)
    return jnp.cos(phase) ** 2


def time_features(step_values, channels):
    half_width = channels // 2
    ladder = jnp.exp(-math.log(10000.0) * jnp.arange(half_width, dtype=jnp.float32) / half_width)
    angles = step_values.astype(jnp.float32)[..., None] * ladder
    return jnp.concatenate([jnp.sin(angles), jnp.cos(angles)], axis=-1)


def contract_rows(left, right):
    return lax.dot_general(left, right, (((0,), (0,)), ((), ())), preferred_element_type=F32)


def contract_cols(left, right):
    return lax.dot_general(left, right, (((1,), (1,)), ((), ())), preferred_element_type=F32)


def plain_product(left, right):
    return lax.dot_general(left, right, (((1,), (0,)), ((), ())), preferred_element_type=F32)


def sigmoid(value):
    return 1.0 / (1.0 + jnp.exp(-value))


def inverse_rms_of(hidden):
    return lax.rsqrt(jnp.mean(hidden * hidden, axis=-1, keepdims=True) + EPSILON)


def slot_rows(slot_index, channels):
    return pl.ds(pl.multiple_of(slot_index * channels, 16), channels)


def run_forward_slots(h_ref, te, w_ref, count, slot_count, channels, store_ref=None):
    def body(slot_index, carry):
        hidden = h_ref[...]
        if store_ref is not None:
            store_ref[slot_index] = hidden
        preact = hidden * inverse_rms_of(hidden) + te
        activated = (preact * sigmoid(preact)).astype(BF16)
        weight = w_ref[slot_rows(slot_index, channels), :]
        h_ref[...] = hidden + plain_product(activated, weight)
        return carry

    lax.fori_loop(0, count, body, 0)


def load_weights(own_hbm, fetched, w_ref, sems, core, shift):
    half_rows = w_ref.shape[0] // 2
    mine_at = pl.multiple_of(core * half_rows, 16)
    sibling_at = pl.multiple_of((1 - core) * half_rows, 16)

    @pl.when(shift == 0)
    def _():
        copy = pltpu.make_async_copy(own_hbm.at[0], w_ref, sems.at[0])
        copy.start()
        copy.wait()

    for index, (mine_hbm, sibling_hbm) in enumerate(fetched):

        @pl.when(shift == index + 1)
        def _():
            copies = [
                pltpu.make_async_copy(
                    mine_hbm.at[pl.ds(0, half_rows)], w_ref.at[pl.ds(mine_at, half_rows)],
                    sems.at[0],
                ),
                pltpu.make_async_copy(
                    sibling_hbm.at[pl.ds(0, half_rows)], w_ref.at[pl.ds(sibling_at, half_rows)],
                    sems.at[1],
                ),
            ]
            for copy in copies:
                copy.start()
            for copy in copies:
                copy.wait()


def split_weight_refs(refs, fetched_count):
    own_hbm = refs[0]
    fetched = [
        (refs[1 + 2 * index], refs[2 + 2 * index]) for index in range(fetched_count)
    ]
    return own_hbm, fetched, refs[1 + 2 * fetched_count :]


def read_table(table_refs, stage, section_count):
    section_index = table_refs[section_count][0]
    shift = lax.rem(section_index - stage + section_count, section_count)
    count = table_refs[0][0]
    for index in range(1, section_count):
        count = jnp.where(shift == index, table_refs[index][0], count)
    return count, section_index == stage, table_refs[section_count + 1][0], shift


def forward_kernel(*refs, decoder, slot_count, channels, fetched_count, stage):
    table_refs = refs[: fetched_count + 3]
    a_ref, te_ref = refs[fetched_count + 3 : fetched_count + 5]
    own_hbm, fetched, refs = split_weight_refs(refs[fetched_count + 5 :], fetched_count)
    skip_ref, out_ref, skip_out_ref, h_ref, w_ref, w_sems = refs
    count, unused_owned, core, shift = read_table(table_refs, stage, fetched_count + 1)
    load_weights(own_hbm, fetched, w_ref, w_sems, core, shift)
    side = w_ref[slot_count * channels :, :]
    hidden = a_ref[...].astype(F32)
    if decoder:
        hidden = hidden + plain_product(skip_ref[...], side)
    h_ref[...] = hidden
    run_forward_slots(h_ref, te_ref[...], w_ref, count, slot_count, channels)
    section_out = h_ref[...].astype(BF16)
    out_ref[...] = section_out
    if not decoder:
        skip_out_ref[...] = plain_product(section_out, side).astype(BF16)


def backward_kernel(*refs, decoder, slot_count, channels, fetched_count, stage, accumulate):
    table_refs = refs[: fetched_count + 3]
    a_ref, te_ref = refs[fetched_count + 3 : fetched_count + 5]
    own_hbm, fetched, refs = split_weight_refs(refs[fetched_count + 5 :], fetched_count)
    if not accumulate:
        refs = refs[:3] + (None,) + refs[3:]
    (skip_ref, g_ref, e_ref, grads_acc_ref, gprev_ref, e_out_ref, grads_out_ref,
     h_ref, hs_ref, gh_ref, grads_scr, sem, w_ref, w_sems) = refs
    count, owned, core, shift = read_table(table_refs, stage, fetched_count + 1)
    load_weights(own_hbm, fetched, w_ref, w_sems, core, shift)
    side = w_ref[slot_count * channels :, :]
    te = te_ref[...]
    hidden = a_ref[...].astype(F32)
    if decoder:
        hidden = hidden + plain_product(skip_ref[...], side)
    h_ref[...] = hidden
    run_forward_slots(h_ref, te, w_ref, count, slot_count, channels, store_ref=hs_ref)
    grad_hidden = g_ref[...].astype(F32)
    if not decoder:
        grad_skip = e_ref[...]
        grad_hidden = grad_hidden + contract_cols(grad_skip, side)
        section_out = h_ref[...].astype(BF16)
        grads_scr[slot_count * channels :, :] = contract_rows(section_out, grad_skip)

    gh_ref[...] = grad_hidden

    def back_body(step, carry):
        slot_index = count - 1 - step
        rows = slot_rows(slot_index, channels)
        hidden = hs_ref[slot_index]
        inverse_rms = inverse_rms_of(hidden)
        normed = hidden * inverse_rms
        preact = normed + te
        sigmoid_val = sigmoid(preact)
        grad_hidden = gh_ref[...]
        grad_low = grad_hidden.astype(BF16)
        activated = (preact * sigmoid_val).astype(BF16)
        grads_scr[rows, :] = contract_rows(activated, grad_low)
        grad_act = contract_cols(grad_low, w_ref[rows, :])
        grad_pre = grad_act * sigmoid_val * (1.0 + preact * (1.0 - sigmoid_val))
        gh_ref[...] = grad_hidden + inverse_rms * (
            grad_pre - normed * jnp.mean(grad_pre * normed, axis=-1, keepdims=True)
        )
        return carry

    lax.fori_loop(0, count, back_body, 0)

    def zero_body(slot_index, carry):
        grads_scr[slot_rows(slot_index, channels), :] = jnp.zeros((channels, channels), F32)
        return carry

    lax.fori_loop(count, slot_count, zero_body, 0)

    grad_low = gh_ref[...].astype(BF16)
    gprev_ref[...] = grad_low
    if decoder:
        e_out_ref[...] = contract_cols(grad_low, side).astype(BF16)
        grads_scr[slot_count * channels :, :] = contract_rows(skip_ref[...], grad_low)

    @pl.when(owned)
    def _():
        grads_copy = pltpu.make_async_copy(grads_scr, grads_out_ref, sem)
        grads_copy.start()
        grads_copy.wait()


PARAMS = pltpu.CompilerParams(vmem_limit_bytes=48 * 1024 * 1024)


VMEM_SPEC = pl.BlockSpec(memory_space=pltpu.VMEM)
SMEM_SPEC = pl.BlockSpec(memory_space=pltpu.SMEM)
ANY_SPEC = pl.BlockSpec(memory_space=pl.ANY)


def weight_operands(weights):
    own, fetched = weights
    flat = [own]
    for pair in fetched:
        flat.extend(pair)
    return flat, len(fetched)


def stage_forward(flags, a, te, weights, skip_in, decoder, slot_count, channels, stage):
    rows = a.shape[0]
    flat, fetched_count = weight_operands(weights)
    kernel = functools.partial(
        forward_kernel, decoder=decoder, slot_count=slot_count, channels=channels,
        fetched_count=fetched_count, stage=stage,
    )
    return pl.pallas_call(
        kernel,
        out_shape=(
            jax.ShapeDtypeStruct((rows, channels), BF16),
            jax.ShapeDtypeStruct((rows, channels), BF16),
        ),
        in_specs=[SMEM_SPEC] * len(flags) + [VMEM_SPEC, VMEM_SPEC] + [ANY_SPEC] * len(flat)
        + [VMEM_SPEC],
        out_specs=(VMEM_SPEC, VMEM_SPEC),
        scratch_shapes=[
            pltpu.VMEM((rows, channels), F32),
            pltpu.VMEM(((slot_count + 1) * channels, channels), BF16),
            pltpu.SemaphoreType.DMA((2,)),
        ],
        compiler_params=PARAMS,
    )(*flags, a, te, *flat, skip_in)


def stage_backward(
    flags, a, te, weights, skip_in, grad_out, grad_skip, grads_acc, decoder,
    slot_count, channels, stage
):
    rows = a.shape[0]
    flat, fetched_count = weight_operands(weights)
    kernel = functools.partial(
        backward_kernel, decoder=decoder, slot_count=slot_count, channels=channels,
        fetched_count=fetched_count, stage=stage, accumulate=grads_acc is not None,
    )
    grads_shape = ((slot_count + 1) * channels, channels)
    accumulated = [] if grads_acc is None else [grads_acc]
    leading = len(flags) + 2 + len(flat) + 3
    return pl.pallas_call(
        kernel,
        out_shape=(
            jax.ShapeDtypeStruct((rows, channels), BF16),
            jax.ShapeDtypeStruct((rows, channels), BF16),
            jax.ShapeDtypeStruct(grads_shape, F32),
        ),
        in_specs=[SMEM_SPEC] * len(flags) + [VMEM_SPEC, VMEM_SPEC] + [ANY_SPEC] * len(flat)
        + [VMEM_SPEC] * 3 + [ANY_SPEC] * len(accumulated),
        out_specs=(VMEM_SPEC, VMEM_SPEC, ANY_SPEC),
        scratch_shapes=[
            pltpu.VMEM((rows, channels), F32),
            pltpu.VMEM((slot_count, rows, channels), F32),
            pltpu.VMEM((rows, channels), F32),
            pltpu.VMEM(grads_shape, F32),
            pltpu.SemaphoreType.DMA(()),
            pltpu.VMEM(((slot_count + 1) * channels, channels), BF16),
            pltpu.SemaphoreType.DMA((2,)),
        ],
        input_output_aliases={leading: 2} if accumulated else {},
        compiler_params=PARAMS,
    )(*flags, a, te, *flat, skip_in, grad_out, grad_skip, *accumulated)


def on_device(clean_latents, target_noise, timesteps, layer_counts, section_weights):
    section_count = lax.axis_size("section")
    half_count = section_count // 2
    section_index = lax.axis_index("section")
    micro_count, row_count, channels = clean_latents.shape
    rows = micro_count * row_count
    weights = section_weights[0]
    slot_count = weights.shape[0] // channels - 1
    step_values = timesteps[0]

    rep_count = lax.axis_size("rep")
    core_index = lax.axis_index("rep") % 2
    half_rows = weights.shape[0] // 2
    my_half = lax.dynamic_slice_in_dim(weights, core_index * half_rows, half_rows, 0)
    count_rows = jnp.broadcast_to(layer_counts[0].astype(BF16), (16, channels))
    block_rows = half_rows + 16

    def tiles_of(value):
        return value.reshape(block_rows // 16, 16, channels)

    def rows_of(value):
        return value.reshape(block_rows, channels)

    my_block = tiles_of(jnp.concatenate([my_half, count_rows]))
    chip_swap = [(i, i ^ 1) for i in range(rep_count)]
    shift_pairs = [
        [(i, (i + shift) % section_count) for i in range(section_count)]
        for shift in range(1, section_count)
    ]
    counts_by_shift = [layer_counts] + [
        lax.ppermute(layer_counts, "section", pairs) for pairs in shift_pairs
    ]
    fetched = []
    for pairs in shift_pairs:
        mine = lax.ppermute(my_block, "section", pairs)
        sibling = lax.ppermute(mine, "rep", chip_swap)
        fetched.append((rows_of(mine), rows_of(sibling)))
    table = counts_by_shift + [
        section_index.astype(jnp.int32).reshape(1),
        core_index.astype(jnp.int32).reshape(1),
    ]
    all_weights = (section_weights, fetched)

    signal_level = noise_level(step_values)[:, None, None]
    noisy_input = (
        jnp.sqrt(signal_level) * clean_latents.astype(jnp.float32)
        + jnp.sqrt(1.0 - signal_level) * target_noise.astype(jnp.float32)
    ).astype(BF16).reshape(rows, channels)
    target_rows = target_noise.reshape(rows, channels)
    time_embed = jnp.broadcast_to(
        time_features(step_values, channels)[:, None, :], (micro_count, row_count, channels)
    ).reshape(rows, channels)


    blank = jnp.zeros((rows, channels), BF16)
    current = noisy_input
    section_inputs = []
    skips = {}
    for stage in range(section_count):
        is_decoder = stage >= half_count
        section_inputs.append(current)
        skip_in = skips[section_count - 1 - stage] if is_decoder else blank
        current, skip_out = stage_forward(
            table, current, time_embed, all_weights, skip_in,
            is_decoder, slot_count, channels, stage,
        )
        if not is_decoder:
            skips[stage] = skip_out

    grad_current = (
        (current.astype(jnp.float32) - target_rows.astype(jnp.float32)) / rows
    ).astype(BF16)
    grad_skips = {}
    weight_grads = None
    for stage in reversed(range(section_count)):
        is_decoder = stage >= half_count
        skip_in = skips[section_count - 1 - stage] if is_decoder else blank
        grad_skip = blank if is_decoder else grad_skips[section_count - 1 - stage]
        grad_current, e_out, weight_grads = stage_backward(
            table, section_inputs[stage], time_embed, all_weights, skip_in,
            grad_current, grad_skip, weight_grads, is_decoder, slot_count, channels, stage,
        )
        if is_decoder:
            grad_skips[stage] = e_out

    return lax.psum_scatter(weight_grads, "rep", scatter_dimension=0, tiled=True)[None]


def solution(mesh):
    placed = (
        P(None, "rep", None),
        P(None, "rep", None),
        P("rep", None),
        P("section"),
        P("section", None, None),
    )
    return jax.shard_map(
        on_device, mesh=mesh, in_specs=placed, out_specs=P("section", "rep", None), check_vma=False
    )
```

```python
import functools
import math

import jax
import jax.numpy as jnp
from jax import lax
from jax.experimental import pallas as pl
from jax.experimental.pallas import tpu as pltpu
from jax.sharding import PartitionSpec as P

EPSILON = 1e-06
F32 = jnp.float32
BF16 = jnp.bfloat16


def noise_level(step_values):
    phase = (step_values.astype(jnp.float32) / 1000.0 + 0.008) / 1.008 * (math.pi / 2.0)
    return jnp.cos(phase) ** 2


def time_features(step_values, channels):
    half_width = channels // 2
    ladder = jnp.exp(-math.log(10000.0) * jnp.arange(half_width, dtype=jnp.float32) / half_width)
    angles = step_values.astype(jnp.float32)[..., None] * ladder
    return jnp.concatenate([jnp.sin(angles), jnp.cos(angles)], axis=-1)


def contract_rows(left, right):
    return lax.dot_general(left, right, (((0,), (0,)), ((), ())), preferred_element_type=F32)


def contract_cols(left, right):
    return lax.dot_general(left, right, (((1,), (1,)), ((), ())), preferred_element_type=F32)


def plain_product(left, right):
    return lax.dot_general(left, right, (((1,), (0,)), ((), ())), preferred_element_type=F32)


def sigmoid(value):
    return 1.0 / (1.0 + jnp.exp(-value))


def inverse_rms_of(hidden):
    return lax.rsqrt(jnp.mean(hidden * hidden, axis=-1, keepdims=True) + EPSILON)


def slot_rows(slot_index, channels):
    return pl.ds(pl.multiple_of(slot_index * channels, 16), channels)


def run_forward_slots(h_ref, te, w_ref, count, slot_count, channels, store_ref=None):
    def body(slot_index, carry):
        hidden = h_ref[...]
        if store_ref is not None:
            store_ref[slot_index] = hidden
        preact = hidden * inverse_rms_of(hidden) + te
        activated = (preact * sigmoid(preact)).astype(BF16)
        weight = w_ref[slot_rows(slot_index, channels), :]
        h_ref[...] = hidden + plain_product(activated, weight)
        return carry

    lax.fori_loop(0, count, body, 0)


def load_weights(own_hbm, fetched, w_ref, sems, core, shift):
    half_rows = w_ref.shape[0] // 2
    mine_at = pl.multiple_of(core * half_rows, 16)
    sibling_at = pl.multiple_of((1 - core) * half_rows, 16)

    @pl.when(shift == 0)
    def _():
        copy = pltpu.make_async_copy(own_hbm.at[0], w_ref, sems.at[0])
        copy.start()
        copy.wait()

    for index, (mine_hbm, sibling_hbm) in enumerate(fetched):

        @pl.when(shift == index + 1)
        def _():
            copies = [
                pltpu.make_async_copy(
                    mine_hbm.at[pl.ds(0, half_rows)], w_ref.at[pl.ds(mine_at, half_rows)],
                    sems.at[0],
                ),
                pltpu.make_async_copy(
                    sibling_hbm.at[pl.ds(0, half_rows)], w_ref.at[pl.ds(sibling_at, half_rows)],
                    sems.at[1],
                ),
            ]
            for copy in copies:
                copy.start()
            for copy in copies:
                copy.wait()


def split_weight_refs(refs, fetched_count):
    own_hbm = refs[0]
    fetched = [
        (refs[1 + 2 * index], refs[2 + 2 * index]) for index in range(fetched_count)
    ]
    return own_hbm, fetched, refs[1 + 2 * fetched_count :]


def read_table(table_refs, stage, section_count):
    section_index = table_refs[section_count][0]
    shift = lax.rem(section_index - stage + section_count, section_count)
    count = table_refs[0][0]
    for index in range(1, section_count):
        count = jnp.where(shift == index, table_refs[index][0], count)
    return count, section_index == stage, table_refs[section_count + 1][0], shift


def forward_kernel(*refs, decoder, slot_count, channels, fetched_count, stage):
    table_refs = refs[: fetched_count + 3]
    a_ref, te_ref = refs[fetched_count + 3 : fetched_count + 5]
    own_hbm, fetched, refs = split_weight_refs(refs[fetched_count + 5 :], fetched_count)
    skip_ref, out_ref, skip_out_ref, h_ref, w_ref, w_sems = refs
    count, unused_owned, core, shift = read_table(table_refs, stage, fetched_count + 1)
    load_weights(own_hbm, fetched, w_ref, w_sems, core, shift)
    side = w_ref[slot_count * channels :, :]
    hidden = a_ref[...].astype(F32)
    if decoder:
        hidden = hidden + plain_product(skip_ref[...], side)
    h_ref[...] = hidden
    run_forward_slots(h_ref, te_ref[...], w_ref, count, slot_count, channels)
    section_out = h_ref[...].astype(BF16)
    out_ref[...] = section_out
    if not decoder:
        skip_out_ref[...] = plain_product(section_out, side).astype(BF16)


def backward_kernel(*refs, decoder, slot_count, channels, fetched_count, stage, accumulate):
    table_refs = refs[: fetched_count + 3]
    a_ref, te_ref = refs[fetched_count + 3 : fetched_count + 5]
    own_hbm, fetched, refs = split_weight_refs(refs[fetched_count + 5 :], fetched_count)
    if not accumulate:
        refs = refs[:3] + (None,) + refs[3:]
    (skip_ref, g_ref, e_ref, grads_acc_ref, gprev_ref, e_out_ref, grads_out_ref,
     h_ref, hs_ref, gh_ref, grads_scr, sem, w_ref, w_sems) = refs
    count, owned, core, shift = read_table(table_refs, stage, fetched_count + 1)
    load_weights(own_hbm, fetched, w_ref, w_sems, core, shift)
    side = w_ref[slot_count * channels :, :]
    te = te_ref[...]
    hidden = a_ref[...].astype(F32)
    if decoder:
        hidden = hidden + plain_product(skip_ref[...], side)
    h_ref[...] = hidden
    run_forward_slots(h_ref, te, w_ref, count, slot_count, channels, store_ref=hs_ref)
    grad_hidden = g_ref[...].astype(F32)
    if not decoder:
        grad_skip = e_ref[...]
        grad_hidden = grad_hidden + contract_cols(grad_skip, side)
        section_out = h_ref[...].astype(BF16)
        grads_scr[slot_count * channels :, :] = contract_rows(section_out, grad_skip)

    gh_ref[...] = grad_hidden

    def back_body(step, carry):
        slot_index = count - 1 - step
        rows = slot_rows(slot_index, channels)
        hidden = hs_ref[slot_index]
        inverse_rms = inverse_rms_of(hidden)
        normed = hidden * inverse_rms
        preact = normed + te
        sigmoid_val = sigmoid(preact)
        grad_hidden = gh_ref[...]
        grad_low = grad_hidden.astype(BF16)

        @pl.when(owned)
        def _():
            activated = (preact * sigmoid_val).astype(BF16)
            grads_scr[rows, :] = contract_rows(activated, grad_low)

        grad_act = contract_cols(grad_low, w_ref[rows, :])
        grad_pre = grad_act * sigmoid_val * (1.0 + preact * (1.0 - sigmoid_val))
        gh_ref[...] = grad_hidden + inverse_rms * (
            grad_pre - normed * jnp.mean(grad_pre * normed, axis=-1, keepdims=True)
        )
        return carry

    lax.fori_loop(0, count, back_body, 0)

    def zero_body(slot_index, carry):
        grads_scr[slot_rows(slot_index, channels), :] = jnp.zeros((channels, channels), F32)
        return carry

    lax.fori_loop(count, slot_count, zero_body, 0)

    grad_low = gh_ref[...].astype(BF16)
    gprev_ref[...] = grad_low
    if decoder:
        e_out_ref[...] = contract_cols(grad_low, side).astype(BF16)
        grads_scr[slot_count * channels :, :] = contract_rows(skip_ref[...], grad_low)

    @pl.when(owned)
    def _():
        grads_copy = pltpu.make_async_copy(grads_scr, grads_out_ref, sem)
        grads_copy.start()
        grads_copy.wait()


PARAMS = pltpu.CompilerParams(vmem_limit_bytes=48 * 1024 * 1024)


VMEM_SPEC = pl.BlockSpec(memory_space=pltpu.VMEM)
SMEM_SPEC = pl.BlockSpec(memory_space=pltpu.SMEM)
ANY_SPEC = pl.BlockSpec(memory_space=pl.ANY)


def weight_operands(weights):
    own, fetched = weights
    flat = [own]
    for pair in fetched:
        flat.extend(pair)
    return flat, len(fetched)


def stage_forward(flags, a, te, weights, skip_in, decoder, slot_count, channels, stage):
    rows = a.shape[0]
    flat, fetched_count = weight_operands(weights)
    kernel = functools.partial(
        forward_kernel, decoder=decoder, slot_count=slot_count, channels=channels,
        fetched_count=fetched_count, stage=stage,
    )
    return pl.pallas_call(
        kernel,
        out_shape=(
            jax.ShapeDtypeStruct((rows, channels), BF16),
            jax.ShapeDtypeStruct((rows, channels), BF16),
        ),
        in_specs=[SMEM_SPEC] * len(flags) + [VMEM_SPEC, VMEM_SPEC] + [ANY_SPEC] * len(flat)
        + [VMEM_SPEC],
        out_specs=(VMEM_SPEC, VMEM_SPEC),
        scratch_shapes=[
            pltpu.VMEM((rows, channels), F32),
            pltpu.VMEM(((slot_count + 1) * channels, channels), BF16),
            pltpu.SemaphoreType.DMA((2,)),
        ],
        compiler_params=PARAMS,
    )(*flags, a, te, *flat, skip_in)


def stage_backward(
    flags, a, te, weights, skip_in, grad_out, grad_skip, grads_acc, decoder,
    slot_count, channels, stage
):
    rows = a.shape[0]
    flat, fetched_count = weight_operands(weights)
    kernel = functools.partial(
        backward_kernel, decoder=decoder, slot_count=slot_count, channels=channels,
        fetched_count=fetched_count, stage=stage, accumulate=grads_acc is not None,
    )
    grads_shape = ((slot_count + 1) * channels, channels)
    accumulated = [] if grads_acc is None else [grads_acc]
    leading = len(flags) + 2 + len(flat) + 3
    return pl.pallas_call(
        kernel,
        out_shape=(
            jax.ShapeDtypeStruct((rows, channels), BF16),
            jax.ShapeDtypeStruct((rows, channels), BF16),
            jax.ShapeDtypeStruct(grads_shape, F32),
        ),
        in_specs=[SMEM_SPEC] * len(flags) + [VMEM_SPEC, VMEM_SPEC] + [ANY_SPEC] * len(flat)
        + [VMEM_SPEC] * 3 + [ANY_SPEC] * len(accumulated),
        out_specs=(VMEM_SPEC, VMEM_SPEC, ANY_SPEC),
        scratch_shapes=[
            pltpu.VMEM((rows, channels), F32),
            pltpu.VMEM((slot_count, rows, channels), F32),
            pltpu.VMEM((rows, channels), F32),
            pltpu.VMEM(grads_shape, F32),
            pltpu.SemaphoreType.DMA(()),
            pltpu.VMEM(((slot_count + 1) * channels, channels), BF16),
            pltpu.SemaphoreType.DMA((2,)),
        ],
        input_output_aliases={leading: 2} if accumulated else {},
        compiler_params=PARAMS,
    )(*flags, a, te, *flat, skip_in, grad_out, grad_skip, *accumulated)


def on_device(clean_latents, target_noise, timesteps, layer_counts, section_weights):
    section_count = lax.axis_size("section")
    half_count = section_count // 2
    section_index = lax.axis_index("section")
    micro_count, row_count, channels = clean_latents.shape
    rows = micro_count * row_count
    weights = section_weights[0]
    slot_count = weights.shape[0] // channels - 1
    step_values = timesteps[0]

    rep_count = lax.axis_size("rep")
    core_index = lax.axis_index("rep") % 2
    half_rows = weights.shape[0] // 2
    my_half = lax.dynamic_slice_in_dim(weights, core_index * half_rows, half_rows, 0)
    count_rows = jnp.broadcast_to(layer_counts[0].astype(BF16), (16, channels))
    block_rows = half_rows + 16

    def tiles_of(value):
        return value.reshape(block_rows // 16, 16, channels)

    def rows_of(value):
        return value.reshape(block_rows, channels)

    my_block = tiles_of(jnp.concatenate([my_half, count_rows]))
    chip_swap = [(i, i ^ 1) for i in range(rep_count)]
    shift_pairs = [
        [(i, (i + shift) % section_count) for i in range(section_count)]
        for shift in range(1, section_count)
    ]
    counts_by_shift = [layer_counts] + [
        lax.ppermute(layer_counts, "section", pairs) for pairs in shift_pairs
    ]
    fetched = []
    for pairs in shift_pairs:
        mine = lax.ppermute(my_block, "section", pairs)
        sibling = lax.ppermute(mine, "rep", chip_swap)
        fetched.append((rows_of(mine), rows_of(sibling)))
    table = counts_by_shift + [
        section_index.astype(jnp.int32).reshape(1),
        core_index.astype(jnp.int32).reshape(1),
    ]
    all_weights = (section_weights, fetched)

    signal_level = noise_level(step_values)[:, None, None]
    noisy_input = (
        jnp.sqrt(signal_level) * clean_latents.astype(jnp.float32)
        + jnp.sqrt(1.0 - signal_level) * target_noise.astype(jnp.float32)
    ).astype(BF16).reshape(rows, channels)
    target_rows = target_noise.reshape(rows, channels)
    time_embed = jnp.broadcast_to(
        time_features(step_values, channels)[:, None, :], (micro_count, row_count, channels)
    ).reshape(rows, channels)


    blank = jnp.zeros((rows, channels), BF16)
    current = noisy_input
    section_inputs = []
    skips = {}
    for stage in range(section_count):
        is_decoder = stage >= half_count
        section_inputs.append(current)
        skip_in = skips[section_count - 1 - stage] if is_decoder else blank
        current, skip_out = stage_forward(
            table, current, time_embed, all_weights, skip_in,
            is_decoder, slot_count, channels, stage,
        )
        if not is_decoder:
            skips[stage] = skip_out

    grad_current = (
        (current.astype(jnp.float32) - target_rows.astype(jnp.float32)) / rows
    ).astype(BF16)
    grad_skips = {}
    weight_grads = None
    for stage in reversed(range(section_count)):
        is_decoder = stage >= half_count
        skip_in = skips[section_count - 1 - stage] if is_decoder else blank
        grad_skip = blank if is_decoder else grad_skips[section_count - 1 - stage]
        grad_current, e_out, weight_grads = stage_backward(
            table, section_inputs[stage], time_embed, all_weights, skip_in,
            grad_current, grad_skip, weight_grads, is_decoder, slot_count, channels, stage,
        )
        if is_decoder:
            grad_skips[stage] = e_out

    return lax.psum_scatter(weight_grads, "rep", scatter_dimension=0, tiled=True)[None]


def solution(mesh):
    placed = (
        P(None, "rep", None),
        P(None, "rep", None),
        P("rep", None),
        P("section"),
        P("section", None, None),
    )
    return jax.shard_map(
        on_device, mesh=mesh, in_specs=placed, out_specs=P("section", "rep", None), check_vma=False
    )
```

```python
import functools
import math

import jax
import jax.numpy as jnp
from jax import lax
from jax.experimental import pallas as pl
from jax.experimental.pallas import tpu as pltpu
from jax.sharding import PartitionSpec as P

EPSILON = 1e-06
F32 = jnp.float32
BF16 = jnp.bfloat16


def noise_level(step_values):
    phase = (step_values.astype(jnp.float32) / 1000.0 + 0.008) / 1.008 * (math.pi / 2.0)
    return jnp.cos(phase) ** 2


def time_features(step_values, channels):
    half_width = channels // 2
    ladder = jnp.exp(-math.log(10000.0) * jnp.arange(half_width, dtype=jnp.float32) / half_width)
    angles = step_values.astype(jnp.float32)[..., None] * ladder
    return jnp.concatenate([jnp.sin(angles), jnp.cos(angles)], axis=-1)


def contract_rows(left, right):
    return lax.dot_general(left, right, (((0,), (0,)), ((), ())), preferred_element_type=F32)


def contract_cols(left, right):
    return lax.dot_general(left, right, (((1,), (1,)), ((), ())), preferred_element_type=F32)


def plain_product(left, right):
    return lax.dot_general(left, right, (((1,), (0,)), ((), ())), preferred_element_type=F32)


def sigmoid(value):
    return 1.0 / (1.0 + jnp.exp(-value))


def inverse_rms_of(hidden):
    return lax.rsqrt(jnp.mean(hidden * hidden, axis=-1, keepdims=True) + EPSILON)


def slot_rows(slot_index, channels):
    return pl.ds(pl.multiple_of(slot_index * channels, 16), channels)


def run_forward_slots(h_ref, te, w_ref, count, slot_count, channels, store_ref=None):
    def body(slot_index, carry):
        hidden = h_ref[...]
        if store_ref is not None:
            store_ref[slot_index] = hidden
        preact = hidden * inverse_rms_of(hidden) + te
        activated = (preact * sigmoid(preact)).astype(BF16)
        weight = w_ref[slot_rows(slot_index, channels), :]
        h_ref[...] = hidden + plain_product(activated, weight)
        return carry

    lax.fori_loop(0, count, body, 0)


def load_weights(own_hbm, fetched, w_ref, sems, core, shift, waiting):
    half_rows = w_ref.shape[0] // 2
    mine_at = pl.multiple_of(core * half_rows, 16)
    sibling_at = pl.multiple_of((1 - core) * half_rows, 16)

    def act(copies):
        for copy in copies:
            if waiting:
                copy.wait()
            else:
                copy.start()

    @pl.when(shift == 0)
    def _():
        act([pltpu.make_async_copy(own_hbm.at[0], w_ref, sems.at[0])])

    for index, (mine_hbm, sibling_hbm) in enumerate(fetched):

        @pl.when(shift == index + 1)
        def _():
            act([
                pltpu.make_async_copy(
                    mine_hbm.at[pl.ds(0, half_rows)], w_ref.at[pl.ds(mine_at, half_rows)],
                    sems.at[0],
                ),
                pltpu.make_async_copy(
                    sibling_hbm.at[pl.ds(0, half_rows)], w_ref.at[pl.ds(sibling_at, half_rows)],
                    sems.at[1],
                ),
            ])


def split_weight_refs(refs, fetched_count):
    own_hbm = refs[0]
    fetched = [
        (refs[1 + 2 * index], refs[2 + 2 * index]) for index in range(fetched_count)
    ]
    return own_hbm, fetched, refs[1 + 2 * fetched_count :]


def read_table(table_refs, stage, section_count):
    section_index = table_refs[section_count][0]
    shift = lax.rem(section_index - stage + section_count, section_count)
    count = table_refs[0][0]
    for index in range(1, section_count):
        count = jnp.where(shift == index, table_refs[index][0], count)
    return count, section_index == stage, table_refs[section_count + 1][0], shift


def forward_kernel(*refs, decoder, slot_count, channels, fetched_count, stage):
    table_refs = refs[: fetched_count + 3]
    a_ref, te_ref = refs[fetched_count + 3 : fetched_count + 5]
    own_hbm, fetched, refs = split_weight_refs(refs[fetched_count + 5 :], fetched_count)
    skip_ref, out_ref, skip_out_ref, h_ref, w_ref, w_sems = refs
    count, unused_owned, core, shift = read_table(table_refs, stage, fetched_count + 1)
    load_weights(own_hbm, fetched, w_ref, w_sems, core, shift, False)
    hidden = a_ref[...].astype(F32)
    load_weights(own_hbm, fetched, w_ref, w_sems, core, shift, True)
    side = w_ref[slot_count * channels :, :]
    if decoder:
        hidden = hidden + plain_product(skip_ref[...], side)
    h_ref[...] = hidden
    run_forward_slots(h_ref, te_ref[...], w_ref, count, slot_count, channels)
    section_out = h_ref[...].astype(BF16)
    out_ref[...] = section_out
    if not decoder:
        skip_out_ref[...] = plain_product(section_out, side).astype(BF16)


def backward_kernel(*refs, decoder, slot_count, channels, fetched_count, stage, accumulate):
    table_refs = refs[: fetched_count + 3]
    a_ref, te_ref = refs[fetched_count + 3 : fetched_count + 5]
    own_hbm, fetched, refs = split_weight_refs(refs[fetched_count + 5 :], fetched_count)
    if not accumulate:
        refs = refs[:3] + (None,) + refs[3:]
    (skip_ref, g_ref, e_ref, grads_acc_ref, gprev_ref, e_out_ref, grads_out_ref,
     h_ref, hs_ref, gh_ref, grads_scr, sem, w_ref, w_sems) = refs
    count, owned, core, shift = read_table(table_refs, stage, fetched_count + 1)
    load_weights(own_hbm, fetched, w_ref, w_sems, core, shift, False)
    gh_ref[...] = g_ref[...].astype(F32)
    hidden = a_ref[...].astype(F32)
    load_weights(own_hbm, fetched, w_ref, w_sems, core, shift, True)
    side = w_ref[slot_count * channels :, :]
    te = te_ref[...]
    if decoder:
        hidden = hidden + plain_product(skip_ref[...], side)
    h_ref[...] = hidden
    run_forward_slots(h_ref, te, w_ref, count, slot_count, channels, store_ref=hs_ref)
    grad_hidden = gh_ref[...]
    if not decoder:
        grad_skip = e_ref[...]
        grad_hidden = grad_hidden + contract_cols(grad_skip, side)
        section_out = h_ref[...].astype(BF16)
        grads_scr[slot_count * channels :, :] = contract_rows(section_out, grad_skip)

    gh_ref[...] = grad_hidden

    def back_body(step, carry):
        slot_index = count - 1 - step
        rows = slot_rows(slot_index, channels)
        hidden = hs_ref[slot_index]
        inverse_rms = inverse_rms_of(hidden)
        normed = hidden * inverse_rms
        preact = normed + te
        sigmoid_val = sigmoid(preact)
        grad_hidden = gh_ref[...]
        grad_low = grad_hidden.astype(BF16)
        activated = (preact * sigmoid_val).astype(BF16)
        grads_scr[rows, :] = contract_rows(activated, grad_low)
        grad_act = contract_cols(grad_low, w_ref[rows, :])
        grad_pre = grad_act * sigmoid_val * (1.0 + preact * (1.0 - sigmoid_val))
        gh_ref[...] = grad_hidden + inverse_rms * (
            grad_pre - normed * jnp.mean(grad_pre * normed, axis=-1, keepdims=True)
        )
        return carry

    lax.fori_loop(0, count, back_body, 0)

    def zero_body(slot_index, carry):
        grads_scr[slot_rows(slot_index, channels), :] = jnp.zeros((channels, channels), F32)
        return carry

    lax.fori_loop(count, slot_count, zero_body, 0)

    grad_low = gh_ref[...].astype(BF16)
    gprev_ref[...] = grad_low
    if decoder:
        e_out_ref[...] = contract_cols(grad_low, side).astype(BF16)
        grads_scr[slot_count * channels :, :] = contract_rows(skip_ref[...], grad_low)

    @pl.when(owned)
    def _():
        grads_copy = pltpu.make_async_copy(grads_scr, grads_out_ref, sem)
        grads_copy.start()
        grads_copy.wait()


PARAMS = pltpu.CompilerParams(vmem_limit_bytes=48 * 1024 * 1024)


VMEM_SPEC = pl.BlockSpec(memory_space=pltpu.VMEM)
SMEM_SPEC = pl.BlockSpec(memory_space=pltpu.SMEM)
ANY_SPEC = pl.BlockSpec(memory_space=pl.ANY)


def weight_operands(weights):
    own, fetched = weights
    flat = [own]
    for pair in fetched:
        flat.extend(pair)
    return flat, len(fetched)


def stage_forward(flags, a, te, weights, skip_in, decoder, slot_count, channels, stage):
    rows = a.shape[0]
    flat, fetched_count = weight_operands(weights)
    kernel = functools.partial(
        forward_kernel, decoder=decoder, slot_count=slot_count, channels=channels,
        fetched_count=fetched_count, stage=stage,
    )
    return pl.pallas_call(
        kernel,
        out_shape=(
            jax.ShapeDtypeStruct((rows, channels), BF16),
            jax.ShapeDtypeStruct((rows, channels), BF16),
        ),
        in_specs=[SMEM_SPEC] * len(flags) + [VMEM_SPEC, VMEM_SPEC] + [ANY_SPEC] * len(flat)
        + [VMEM_SPEC],
        out_specs=(VMEM_SPEC, VMEM_SPEC),
        scratch_shapes=[
            pltpu.VMEM((rows, channels), F32),
            pltpu.VMEM(((slot_count + 1) * channels, channels), BF16),
            pltpu.SemaphoreType.DMA((2,)),
        ],
        compiler_params=PARAMS,
    )(*flags, a, te, *flat, skip_in)


def stage_backward(
    flags, a, te, weights, skip_in, grad_out, grad_skip, grads_acc, decoder,
    slot_count, channels, stage
):
    rows = a.shape[0]
    flat, fetched_count = weight_operands(weights)
    kernel = functools.partial(
        backward_kernel, decoder=decoder, slot_count=slot_count, channels=channels,
        fetched_count=fetched_count, stage=stage, accumulate=grads_acc is not None,
    )
    grads_shape = ((slot_count + 1) * channels, channels)
    accumulated = [] if grads_acc is None else [grads_acc]
    leading = len(flags) + 2 + len(flat) + 3
    return pl.pallas_call(
        kernel,
        out_shape=(
            jax.ShapeDtypeStruct((rows, channels), BF16),
            jax.ShapeDtypeStruct((rows, channels), BF16),
            jax.ShapeDtypeStruct(grads_shape, F32),
        ),
        in_specs=[SMEM_SPEC] * len(flags) + [VMEM_SPEC, VMEM_SPEC] + [ANY_SPEC] * len(flat)
        + [VMEM_SPEC] * 3 + [ANY_SPEC] * len(accumulated),
        out_specs=(VMEM_SPEC, VMEM_SPEC, ANY_SPEC),
        scratch_shapes=[
            pltpu.VMEM((rows, channels), F32),
            pltpu.VMEM((slot_count, rows, channels), F32),
            pltpu.VMEM((rows, channels), F32),
            pltpu.VMEM(grads_shape, F32),
            pltpu.SemaphoreType.DMA(()),
            pltpu.VMEM(((slot_count + 1) * channels, channels), BF16),
            pltpu.SemaphoreType.DMA((2,)),
        ],
        input_output_aliases={leading: 2} if accumulated else {},
        compiler_params=PARAMS,
    )(*flags, a, te, *flat, skip_in, grad_out, grad_skip, *accumulated)


def on_device(clean_latents, target_noise, timesteps, layer_counts, section_weights):
    section_count = lax.axis_size("section")
    half_count = section_count // 2
    section_index = lax.axis_index("section")
    micro_count, row_count, channels = clean_latents.shape
    rows = micro_count * row_count
    weights = section_weights[0]
    slot_count = weights.shape[0] // channels - 1
    step_values = timesteps[0]

    rep_count = lax.axis_size("rep")
    core_index = lax.axis_index("rep") % 2
    half_rows = weights.shape[0] // 2
    my_half = lax.dynamic_slice_in_dim(weights, core_index * half_rows, half_rows, 0)
    count_rows = jnp.broadcast_to(layer_counts[0].astype(BF16), (16, channels))
    block_rows = half_rows + 16

    def tiles_of(value):
        return value.reshape(block_rows // 16, 16, channels)

    def rows_of(value):
        return value.reshape(block_rows, channels)

    my_block = tiles_of(jnp.concatenate([my_half, count_rows]))
    chip_swap = [(i, i ^ 1) for i in range(rep_count)]
    shift_pairs = [
        [(i, (i + shift) % section_count) for i in range(section_count)]
        for shift in range(1, section_count)
    ]
    counts_by_shift = [layer_counts] + [
        lax.ppermute(layer_counts, "section", pairs) for pairs in shift_pairs
    ]
    fetched = []
    for pairs in shift_pairs:
        mine = lax.ppermute(my_block, "section", pairs)
        sibling = lax.ppermute(mine, "rep", chip_swap)
        fetched.append((rows_of(mine), rows_of(sibling)))
    table = counts_by_shift + [
        section_index.astype(jnp.int32).reshape(1),
        core_index.astype(jnp.int32).reshape(1),
    ]
    all_weights = (section_weights, fetched)

    signal_level = noise_level(step_values)[:, None, None]
    noisy_input = (
        jnp.sqrt(signal_level) * clean_latents.astype(jnp.float32)
        + jnp.sqrt(1.0 - signal_level) * target_noise.astype(jnp.float32)
    ).astype(BF16).reshape(rows, channels)
    target_rows = target_noise.reshape(rows, channels)
    time_embed = jnp.broadcast_to(
        time_features(step_values, channels)[:, None, :], (micro_count, row_count, channels)
    ).reshape(rows, channels)


    blank = jnp.zeros((rows, channels), BF16)
    current = noisy_input
    section_inputs = []
    skips = {}
    for stage in range(section_count):
        is_decoder = stage >= half_count
        section_inputs.append(current)
        skip_in = skips[section_count - 1 - stage] if is_decoder else blank
        current, skip_out = stage_forward(
            table, current, time_embed, all_weights, skip_in,
            is_decoder, slot_count, channels, stage,
        )
        if not is_decoder:
            skips[stage] = skip_out

    grad_current = (
        (current.astype(jnp.float32) - target_rows.astype(jnp.float32)) / rows
    ).astype(BF16)
    grad_skips = {}
    weight_grads = None
    for stage in reversed(range(section_count)):
        is_decoder = stage >= half_count
        skip_in = skips[section_count - 1 - stage] if is_decoder else blank
        grad_skip = blank if is_decoder else grad_skips[section_count - 1 - stage]
        grad_current, e_out, weight_grads = stage_backward(
            table, section_inputs[stage], time_embed, all_weights, skip_in,
            grad_current, grad_skip, weight_grads, is_decoder, slot_count, channels, stage,
        )
        if is_decoder:
            grad_skips[stage] = e_out

    return lax.psum_scatter(weight_grads, "rep", scatter_dimension=0, tiled=True)[None]


def solution(mesh):
    placed = (
        P(None, "rep", None),
        P(None, "rep", None),
        P("rep", None),
        P("section"),
        P("section", None, None),
    )
    return jax.shard_map(
        on_device, mesh=mesh, in_specs=placed, out_specs=P("section", "rep", None), check_vma=False
    )
```

```python
import functools
import math

import jax
import jax.numpy as jnp
from jax import lax
from jax.experimental import pallas as pl
from jax.experimental.pallas import tpu as pltpu
from jax.sharding import PartitionSpec as P

EPSILON = 1e-06
F32 = jnp.float32
BF16 = jnp.bfloat16


def noise_level(step_values):
    phase = (step_values.astype(jnp.float32) / 1000.0 + 0.008) / 1.008 * (math.pi / 2.0)
    return jnp.cos(phase) ** 2


def time_features(step_values, channels):
    half_width = channels // 2
    ladder = jnp.exp(-math.log(10000.0) * jnp.arange(half_width, dtype=jnp.float32) / half_width)
    angles = step_values.astype(jnp.float32)[..., None] * ladder
    return jnp.concatenate([jnp.sin(angles), jnp.cos(angles)], axis=-1)


def contract_rows(left, right):
    return lax.dot_general(left, right, (((0,), (0,)), ((), ())), preferred_element_type=F32)


def contract_cols(left, right):
    return lax.dot_general(left, right, (((1,), (1,)), ((), ())), preferred_element_type=F32)


def plain_product(left, right):
    return lax.dot_general(left, right, (((1,), (0,)), ((), ())), preferred_element_type=F32)


def sigmoid(value):
    return 1.0 / (1.0 + jnp.exp(-value))


def inverse_rms_of(hidden):
    return lax.rsqrt(jnp.mean(hidden * hidden, axis=-1, keepdims=True) + EPSILON)


def slot_rows(slot_index, channels):
    return pl.ds(pl.multiple_of(slot_index * channels, 16), channels)


def run_forward_slots(h_ref, te, w_ref, count, slot_count, channels, store_ref=None):
    def body(slot_index, carry):
        hidden = h_ref[...]
        if store_ref is not None:
            store_ref[slot_index] = hidden
        preact = hidden * inverse_rms_of(hidden) + te
        activated = (preact * sigmoid(preact)).astype(BF16)
        weight = w_ref[slot_rows(slot_index, channels), :]
        h_ref[...] = hidden + plain_product(activated, weight)
        return carry

    lax.fori_loop(0, count, body, 0)


def load_weights(own_hbm, fetched, w_ref, sems, core, shift):
    half_rows = w_ref.shape[0] // 2
    mine_at = pl.multiple_of(core * half_rows, 16)
    sibling_at = pl.multiple_of((1 - core) * half_rows, 16)

    @pl.when(shift == 0)
    def _():
        copy = pltpu.make_async_copy(own_hbm.at[0], w_ref, sems.at[0])
        copy.start()
        copy.wait()

    for index, (mine_hbm, sibling_hbm) in enumerate(fetched):

        @pl.when(shift == index + 1)
        def _():
            copies = [
                pltpu.make_async_copy(
                    mine_hbm.at[pl.ds(0, half_rows)], w_ref.at[pl.ds(mine_at, half_rows)],
                    sems.at[0],
                ),
                pltpu.make_async_copy(
                    sibling_hbm.at[pl.ds(0, half_rows)], w_ref.at[pl.ds(sibling_at, half_rows)],
                    sems.at[1],
                ),
            ]
            for copy in copies:
                copy.start()
            for copy in copies:
                copy.wait()


def split_weight_refs(refs, fetched_count):
    own_hbm = refs[0]
    fetched = [
        (refs[1 + 2 * index], refs[2 + 2 * index]) for index in range(fetched_count)
    ]
    return own_hbm, fetched, refs[1 + 2 * fetched_count :]


def read_table(table_refs, stage, section_count):
    section_index = table_refs[section_count][0]
    shift = lax.rem(section_index - stage + section_count, section_count)
    count = table_refs[0][0]
    for index in range(1, section_count):
        count = jnp.where(shift == index, table_refs[index][0], count)
    return count, section_index == stage, table_refs[section_count + 1][0], shift


def forward_kernel(*refs, decoder, slot_count, channels, fetched_count, stage):
    table_refs = refs[: fetched_count + 3]
    a_ref, te_ref = refs[fetched_count + 3 : fetched_count + 5]
    own_hbm, fetched, refs = split_weight_refs(refs[fetched_count + 5 :], fetched_count)
    skip_ref, out_ref, skip_out_ref, h_ref, w_ref, w_sems = refs
    count, unused_owned, core, shift = read_table(table_refs, stage, fetched_count + 1)
    load_weights(own_hbm, fetched, w_ref, w_sems, core, shift)
    side = w_ref[slot_count * channels :, :]
    hidden = a_ref[...].astype(F32)
    if decoder:
        hidden = hidden + plain_product(skip_ref[...], side)
    h_ref[...] = hidden
    run_forward_slots(h_ref, te_ref[...], w_ref, count, slot_count, channels)
    section_out = h_ref[...].astype(BF16)
    out_ref[...] = section_out
    if not decoder:
        skip_out_ref[...] = plain_product(section_out, side).astype(BF16)


def backward_kernel(*refs, decoder, slot_count, channels, fetched_count, stage, accumulate):
    table_refs = refs[: fetched_count + 3]
    a_ref, te_ref = refs[fetched_count + 3 : fetched_count + 5]
    own_hbm, fetched, refs = split_weight_refs(refs[fetched_count + 5 :], fetched_count)
    if not accumulate:
        refs = refs[:3] + (None,) + refs[3:]
    (skip_ref, g_ref, e_ref, grads_acc_ref, gprev_ref, e_out_ref, grads_out_ref,
     h_ref, hs_ref, gh_ref, grads_scr, sem, w_ref, w_sems) = refs
    count, owned, core, shift = read_table(table_refs, stage, fetched_count + 1)
    load_weights(own_hbm, fetched, w_ref, w_sems, core, shift)
    side = w_ref[slot_count * channels :, :]
    te = te_ref[...]
    hidden = a_ref[...].astype(F32)
    if decoder:
        hidden = hidden + plain_product(skip_ref[...], side)
    h_ref[...] = hidden
    run_forward_slots(h_ref, te, w_ref, count, slot_count, channels, store_ref=hs_ref)
    grad_hidden = g_ref[...].astype(F32)
    if not decoder:
        grad_skip = e_ref[...]
        grad_hidden = grad_hidden + contract_cols(grad_skip, side)
        section_out = h_ref[...].astype(BF16)
        grads_scr[slot_count * channels :, :] = contract_rows(section_out, grad_skip)

    gh_ref[...] = grad_hidden

    def back_body(step, carry):
        slot_index = count - 1 - step
        rows = slot_rows(slot_index, channels)
        hidden = hs_ref[slot_index]
        inverse_rms = inverse_rms_of(hidden)
        normed = hidden * inverse_rms
        preact = normed + te
        sigmoid_val = sigmoid(preact)
        grad_hidden = gh_ref[...]
        grad_low = grad_hidden.astype(BF16)
        activated = (preact * sigmoid_val).astype(BF16)
        grads_scr[rows, :] = contract_rows(activated, grad_low)
        grad_act = contract_cols(grad_low, w_ref[rows, :])
        grad_pre = grad_act * sigmoid_val * (1.0 + preact * (1.0 - sigmoid_val))
        gh_ref[...] = grad_hidden + inverse_rms * (
            grad_pre - normed * jnp.mean(grad_pre * normed, axis=-1, keepdims=True)
        )
        return carry

    lax.fori_loop(0, count, back_body, 0)

    def zero_body(slot_index, carry):
        grads_scr[slot_rows(slot_index, channels), :] = jnp.zeros((channels, channels), F32)
        return carry

    lax.fori_loop(count, slot_count, zero_body, 0)

    grad_low = gh_ref[...].astype(BF16)
    gprev_ref[...] = grad_low
    if decoder:
        e_out_ref[...] = contract_cols(grad_low, side).astype(BF16)
        grads_scr[slot_count * channels :, :] = contract_rows(skip_ref[...], grad_low)

    @pl.when(owned)
    def _():
        grads_copy = pltpu.make_async_copy(grads_scr, grads_out_ref, sem)
        grads_copy.start()
        grads_copy.wait()


PARAMS = pltpu.CompilerParams(vmem_limit_bytes=48 * 1024 * 1024)


VMEM_SPEC = pl.BlockSpec(memory_space=pltpu.VMEM)
SMEM_SPEC = pl.BlockSpec(memory_space=pltpu.SMEM)
ANY_SPEC = pl.BlockSpec(memory_space=pl.ANY)


def weight_operands(weights):
    own, fetched = weights
    flat = [own]
    for pair in fetched:
        flat.extend(pair)
    return flat, len(fetched)


def stage_forward(flags, a, te, weights, skip_in, decoder, slot_count, channels, stage):
    rows = a.shape[0]
    flat, fetched_count = weight_operands(weights)
    kernel = functools.partial(
        forward_kernel, decoder=decoder, slot_count=slot_count, channels=channels,
        fetched_count=fetched_count, stage=stage,
    )
    return pl.pallas_call(
        kernel,
        out_shape=(
            jax.ShapeDtypeStruct((rows, channels), BF16),
            jax.ShapeDtypeStruct((rows, channels), BF16),
        ),
        in_specs=[SMEM_SPEC] * len(flags) + [VMEM_SPEC, VMEM_SPEC] + [ANY_SPEC] * len(flat)
        + [VMEM_SPEC],
        out_specs=(VMEM_SPEC, VMEM_SPEC),
        scratch_shapes=[
            pltpu.VMEM((rows, channels), F32),
            pltpu.VMEM(((slot_count + 1) * channels, channels), BF16),
            pltpu.SemaphoreType.DMA((2,)),
        ],
        compiler_params=PARAMS,
    )(*flags, a, te, *flat, skip_in)


def stage_backward(
    flags, a, te, weights, skip_in, grad_out, grad_skip, grads_acc, decoder,
    slot_count, channels, stage
):
    rows = a.shape[0]
    flat, fetched_count = weight_operands(weights)
    kernel = functools.partial(
        backward_kernel, decoder=decoder, slot_count=slot_count, channels=channels,
        fetched_count=fetched_count, stage=stage, accumulate=grads_acc is not None,
    )
    grads_shape = ((slot_count + 1) * channels, channels)
    accumulated = [] if grads_acc is None else [grads_acc]
    leading = len(flags) + 2 + len(flat) + 3
    return pl.pallas_call(
        kernel,
        out_shape=(
            jax.ShapeDtypeStruct((rows, channels), BF16),
            jax.ShapeDtypeStruct((rows, channels), BF16),
            jax.ShapeDtypeStruct(grads_shape, F32),
        ),
        in_specs=[SMEM_SPEC] * len(flags) + [VMEM_SPEC, VMEM_SPEC] + [ANY_SPEC] * len(flat)
        + [VMEM_SPEC] * 3 + [ANY_SPEC] * len(accumulated),
        out_specs=(VMEM_SPEC, VMEM_SPEC, ANY_SPEC),
        scratch_shapes=[
            pltpu.VMEM((rows, channels), F32),
            pltpu.VMEM((slot_count, rows, channels), F32),
            pltpu.VMEM((rows, channels), F32),
            pltpu.VMEM(grads_shape, F32),
            pltpu.SemaphoreType.DMA(()),
            pltpu.VMEM(((slot_count + 1) * channels, channels), BF16),
            pltpu.SemaphoreType.DMA((2,)),
        ],
        input_output_aliases={leading: 2} if accumulated else {},
        compiler_params=PARAMS,
    )(*flags, a, te, *flat, skip_in, grad_out, grad_skip, *accumulated)


def on_device(clean_latents, target_noise, timesteps, layer_counts, section_weights):
    section_count = lax.axis_size("section")
    half_count = section_count // 2
    section_index = lax.axis_index("section")
    micro_count, row_count, channels = clean_latents.shape
    rows = micro_count * row_count
    weights = section_weights[0]
    slot_count = weights.shape[0] // channels - 1
    step_values = timesteps[0]

    rep_count = lax.axis_size("rep")
    core_index = lax.axis_index("rep") % 2
    half_rows = weights.shape[0] // 2
    my_half = lax.dynamic_slice_in_dim(weights, core_index * half_rows, half_rows, 0)
    count_rows = jnp.broadcast_to(layer_counts[0].astype(BF16), (16, channels))
    block_rows = half_rows + 16

    def tiles_of(value):
        return value.reshape(block_rows // 16, 16, channels)

    def rows_of(value):
        return value.reshape(block_rows, channels)

    my_block = tiles_of(jnp.concatenate([my_half, count_rows]))
    chip_swap = [(i, i ^ 1) for i in range(rep_count)]
    shift_pairs = [
        [(i, (i + shift) % section_count) for i in range(section_count)]
        for shift in range(1, section_count)
    ]
    counts_by_shift = [layer_counts] + [
        lax.ppermute(layer_counts, "section", pairs) for pairs in shift_pairs
    ]
    fetched = []
    for pairs in shift_pairs:
        mine = lax.ppermute(my_block, "section", pairs)
        sibling = lax.ppermute(mine, "rep", chip_swap)
        fetched.append((rows_of(mine), rows_of(sibling)))
    table = counts_by_shift + [
        section_index.astype(jnp.int32).reshape(1),
        core_index.astype(jnp.int32).reshape(1),
    ]
    all_weights = (section_weights, fetched)

    signal_level = noise_level(step_values)[:, None, None]
    noisy_input = (
        jnp.sqrt(signal_level) * clean_latents.astype(jnp.float32)
        + jnp.sqrt(1.0 - signal_level) * target_noise.astype(jnp.float32)
    ).astype(BF16).reshape(rows, channels)
    target_rows = target_noise.reshape(rows, channels)
    time_embed = jnp.broadcast_to(
        time_features(step_values, channels)[:, None, :], (micro_count, row_count, channels)
    ).reshape(rows, channels)


    blank = jnp.zeros((rows, channels), BF16)
    current = noisy_input
    section_inputs = []
    skips = {}
    for stage in range(section_count):
        is_decoder = stage >= half_count
        section_inputs.append(current)
        skip_in = skips[section_count - 1 - stage] if is_decoder else blank
        current, skip_out = stage_forward(
            table, current, time_embed, all_weights, skip_in,
            is_decoder, slot_count, channels, stage,
        )
        if not is_decoder:
            skips[stage] = skip_out

    grad_current = (
        (current.astype(jnp.float32) - target_rows.astype(jnp.float32)) / rows
    ).astype(BF16)
    grad_skips = {}
    weight_grads = None
    for stage in reversed(range(section_count)):
        is_decoder = stage >= half_count
        skip_in = skips[section_count - 1 - stage] if is_decoder else blank
        grad_skip = blank if is_decoder else grad_skips[section_count - 1 - stage]
        grad_current, e_out, weight_grads = stage_backward(
            table, section_inputs[stage], time_embed, all_weights, skip_in,
            grad_current, grad_skip, weight_grads, is_decoder, slot_count, channels, stage,
        )
        if is_decoder:
            grad_skips[stage] = e_out

    return halving_scatter(weight_grads)[None]


def halving_scatter(grads):
    rep_count = lax.axis_size("rep")
    bits = rep_count.bit_length() - 1
    channels = grads.shape[1]
    chunk = grads.shape[0] // rep_count
    ordered = grads.reshape([2] * bits + [chunk, channels])
    ordered = ordered.transpose(list(reversed(range(bits))) + [bits, bits + 1])
    current = ordered.reshape(grads.shape)
    rep_index = lax.axis_index("rep")
    for bit in range(bits):
        half = current.shape[0] // 2
        my_bit = (rep_index >> bit) & 1
        keep = lax.dynamic_slice_in_dim(current, my_bit * half, half, 0)
        give = lax.dynamic_slice_in_dim(current, (1 - my_bit) * half, half, 0)
        pairs = [(i, i ^ (1 << bit)) for i in range(rep_count)]
        got = lax.ppermute(give.reshape(half // 8, 8, channels), "rep", pairs)
        current = keep + got.reshape(half, channels)
    return current


def solution(mesh):
    placed = (
        P(None, "rep", None),
        P(None, "rep", None),
        P("rep", None),
        P("section"),
        P("section", None, None),
    )
    return jax.shard_map(
        on_device, mesh=mesh, in_specs=placed, out_specs=P("section", "rep", None), check_vma=False
    )
```

```python
import functools
import math

import jax
import jax.numpy as jnp
from jax import lax
from jax.experimental import pallas as pl
from jax.experimental.pallas import tpu as pltpu
from jax.sharding import PartitionSpec as P

EPSILON = 1e-06
F32 = jnp.float32
BF16 = jnp.bfloat16


def noise_level(step_values):
    phase = (step_values.astype(jnp.float32) / 1000.0 + 0.008) / 1.008 * (math.pi / 2.0)
    return jnp.cos(phase) ** 2


def time_features(step_values, channels):
    half_width = channels // 2
    ladder = jnp.exp(-math.log(10000.0) * jnp.arange(half_width, dtype=jnp.float32) / half_width)
    angles = step_values.astype(jnp.float32)[..., None] * ladder
    return jnp.concatenate([jnp.sin(angles), jnp.cos(angles)], axis=-1)


def contract_rows(left, right):
    return lax.dot_general(left, right, (((0,), (0,)), ((), ())), preferred_element_type=F32)


def contract_cols(left, right):
    return lax.dot_general(left, right, (((1,), (1,)), ((), ())), preferred_element_type=F32)


def plain_product(left, right):
    return lax.dot_general(left, right, (((1,), (0,)), ((), ())), preferred_element_type=F32)


def sigmoid(value):
    return 1.0 / (1.0 + jnp.exp(-value))


def inverse_rms_of(hidden):
    return lax.rsqrt(jnp.mean(hidden * hidden, axis=-1, keepdims=True) + EPSILON)


def slot_rows(slot_index, channels):
    return pl.ds(pl.multiple_of(slot_index * channels, 16), channels)


def run_forward_slots(h_ref, te, w_ref, count, slot_count, channels, store_ref=None):
    def body(slot_index, carry):
        hidden = h_ref[...]
        if store_ref is not None:
            store_ref[slot_index] = hidden
        preact = hidden * inverse_rms_of(hidden) + te
        activated = (preact * sigmoid(preact)).astype(BF16)
        weight = w_ref[slot_rows(slot_index, channels), :]
        h_ref[...] = hidden + plain_product(activated, weight)
        return carry

    lax.fori_loop(0, count, body, 0)


def load_weights(own_hbm, fetched, w_ref, sems, core, shift):
    half_rows = w_ref.shape[0] // 2
    mine_at = pl.multiple_of(core * half_rows, 16)
    sibling_at = pl.multiple_of((1 - core) * half_rows, 16)

    @pl.when(shift == 0)
    def _():
        copy = pltpu.make_async_copy(own_hbm.at[0], w_ref, sems.at[0])
        copy.start()
        copy.wait()

    for index, (mine_hbm, sibling_hbm) in enumerate(fetched):

        @pl.when(shift == index + 1)
        def _():
            copies = [
                pltpu.make_async_copy(
                    mine_hbm.at[pl.ds(0, half_rows)], w_ref.at[pl.ds(mine_at, half_rows)],
                    sems.at[0],
                ),
                pltpu.make_async_copy(
                    sibling_hbm.at[pl.ds(0, half_rows)], w_ref.at[pl.ds(sibling_at, half_rows)],
                    sems.at[1],
                ),
            ]
            for copy in copies:
                copy.start()
            for copy in copies:
                copy.wait()


def split_weight_refs(refs, fetched_count):
    own_hbm = refs[0]
    fetched = [
        (refs[1 + 2 * index], refs[2 + 2 * index]) for index in range(fetched_count)
    ]
    return own_hbm, fetched, refs[1 + 2 * fetched_count :]


def read_table(table_refs, stage, section_count):
    section_index = table_refs[section_count][0]
    shift = lax.rem(section_index - stage + section_count, section_count)
    count = table_refs[0][0]
    for index in range(1, section_count):
        count = jnp.where(shift == index, table_refs[index][0], count)
    return count, section_index == stage, table_refs[section_count + 1][0], shift


def forward_kernel(*refs, decoder, slot_count, channels, fetched_count, stage):
    table_refs = refs[: fetched_count + 3]
    a_ref, te_ref = refs[fetched_count + 3 : fetched_count + 5]
    own_hbm, fetched, refs = split_weight_refs(refs[fetched_count + 5 :], fetched_count)
    skip_ref, out_ref, skip_out_ref, h_ref, w_ref, w_sems = refs
    count, unused_owned, core, shift = read_table(table_refs, stage, fetched_count + 1)
    load_weights(own_hbm, fetched, w_ref, w_sems, core, shift)
    side = w_ref[slot_count * channels :, :]
    hidden = a_ref[...].astype(F32)
    if decoder:
        hidden = hidden + plain_product(skip_ref[...], side)
    h_ref[...] = hidden
    run_forward_slots(h_ref, te_ref[...], w_ref, count, slot_count, channels)
    section_out = h_ref[...].astype(BF16)
    out_ref[...] = section_out
    if not decoder:
        skip_out_ref[...] = plain_product(section_out, side).astype(BF16)


def backward_kernel(*refs, decoder, slot_count, channels, fetched_count, stage, accumulate):
    table_refs = refs[: fetched_count + 3]
    a_ref, te_ref = refs[fetched_count + 3 : fetched_count + 5]
    own_hbm, fetched, refs = split_weight_refs(refs[fetched_count + 5 :], fetched_count)
    if not accumulate:
        refs = refs[:3] + (None,) + refs[3:]
    (skip_ref, g_ref, e_ref, grads_acc_ref, gprev_ref, e_out_ref, grads_out_ref,
     h_ref, hs_ref, gh_ref, grads_scr, sem, w_ref, w_sems) = refs
    count, owned, core, shift = read_table(table_refs, stage, fetched_count + 1)
    load_weights(own_hbm, fetched, w_ref, w_sems, core, shift)
    side = w_ref[slot_count * channels :, :]
    te = te_ref[...]
    hidden = a_ref[...].astype(F32)
    if decoder:
        hidden = hidden + plain_product(skip_ref[...], side)
    h_ref[...] = hidden
    run_forward_slots(h_ref, te, w_ref, count, slot_count, channels, store_ref=hs_ref)
    grad_hidden = g_ref[...].astype(F32)
    if not decoder:
        grad_skip = e_ref[...]
        grad_hidden = grad_hidden + contract_cols(grad_skip, side)
        section_out = h_ref[...].astype(BF16)
        grads_scr[slot_count * channels :, :] = contract_rows(section_out, grad_skip)

    gh_ref[...] = grad_hidden

    def back_body(step, carry):
        slot_index = count - 1 - step
        rows = slot_rows(slot_index, channels)
        hidden = hs_ref[slot_index]
        inverse_rms = inverse_rms_of(hidden)
        normed = hidden * inverse_rms
        preact = normed + te
        sigmoid_val = sigmoid(preact)
        grad_hidden = gh_ref[...]
        grad_low = grad_hidden.astype(BF16)
        activated = (preact * sigmoid_val).astype(BF16)
        grads_scr[rows, :] = contract_rows(activated, grad_low)
        grad_act = contract_cols(grad_low, w_ref[rows, :])
        grad_pre = grad_act * sigmoid_val * (1.0 + preact * (1.0 - sigmoid_val))
        gh_ref[...] = grad_hidden + inverse_rms * (
            grad_pre - normed * jnp.mean(grad_pre * normed, axis=-1, keepdims=True)
        )
        return carry

    lax.fori_loop(0, count, back_body, 0)

    def zero_body(slot_index, carry):
        grads_scr[slot_rows(slot_index, channels), :] = jnp.zeros((channels, channels), F32)
        return carry

    lax.fori_loop(count, slot_count, zero_body, 0)

    grad_low = gh_ref[...].astype(BF16)
    gprev_ref[...] = grad_low
    if decoder:
        e_out_ref[...] = contract_cols(grad_low, side).astype(BF16)
        grads_scr[slot_count * channels :, :] = contract_rows(skip_ref[...], grad_low)

    @pl.when(owned)
    def _():
        grads_copy = pltpu.make_async_copy(grads_scr, grads_out_ref, sem)
        grads_copy.start()
        grads_copy.wait()


PARAMS = pltpu.CompilerParams(vmem_limit_bytes=48 * 1024 * 1024)


VMEM_SPEC = pl.BlockSpec(memory_space=pltpu.VMEM)
SMEM_SPEC = pl.BlockSpec(memory_space=pltpu.SMEM)
ANY_SPEC = pl.BlockSpec(memory_space=pl.ANY)


def weight_operands(weights):
    own, fetched = weights
    flat = [own]
    for pair in fetched:
        flat.extend(pair)
    return flat, len(fetched)


def stage_forward(flags, a, te, weights, skip_in, decoder, slot_count, channels, stage):
    rows = a.shape[0]
    flat, fetched_count = weight_operands(weights)
    kernel = functools.partial(
        forward_kernel, decoder=decoder, slot_count=slot_count, channels=channels,
        fetched_count=fetched_count, stage=stage,
    )
    return pl.pallas_call(
        kernel,
        out_shape=(
            jax.ShapeDtypeStruct((rows, channels), BF16),
            jax.ShapeDtypeStruct((rows, channels), BF16),
        ),
        in_specs=[SMEM_SPEC] * len(flags) + [VMEM_SPEC, VMEM_SPEC] + [ANY_SPEC] * len(flat)
        + [VMEM_SPEC],
        out_specs=(VMEM_SPEC, VMEM_SPEC),
        scratch_shapes=[
            pltpu.VMEM((rows, channels), F32),
            pltpu.VMEM(((slot_count + 1) * channels, channels), BF16),
            pltpu.SemaphoreType.DMA((2,)),
        ],
        compiler_params=PARAMS,
    )(*flags, a, te, *flat, skip_in)


def stage_backward(
    flags, a, te, weights, skip_in, grad_out, grad_skip, grads_acc, decoder,
    slot_count, channels, stage
):
    rows = a.shape[0]
    flat, fetched_count = weight_operands(weights)
    kernel = functools.partial(
        backward_kernel, decoder=decoder, slot_count=slot_count, channels=channels,
        fetched_count=fetched_count, stage=stage, accumulate=grads_acc is not None,
    )
    grads_shape = ((slot_count + 1) * channels, channels)
    accumulated = [] if grads_acc is None else [grads_acc]
    leading = len(flags) + 2 + len(flat) + 3
    return pl.pallas_call(
        kernel,
        out_shape=(
            jax.ShapeDtypeStruct((rows, channels), BF16),
            jax.ShapeDtypeStruct((rows, channels), BF16),
            jax.ShapeDtypeStruct(grads_shape, F32),
        ),
        in_specs=[SMEM_SPEC] * len(flags) + [VMEM_SPEC, VMEM_SPEC] + [ANY_SPEC] * len(flat)
        + [VMEM_SPEC] * 3 + [ANY_SPEC] * len(accumulated),
        out_specs=(VMEM_SPEC, VMEM_SPEC, ANY_SPEC),
        scratch_shapes=[
            pltpu.VMEM((rows, channels), F32),
            pltpu.VMEM((slot_count, rows, channels), F32),
            pltpu.VMEM((rows, channels), F32),
            pltpu.VMEM(grads_shape, F32),
            pltpu.SemaphoreType.DMA(()),
            pltpu.VMEM(((slot_count + 1) * channels, channels), BF16),
            pltpu.SemaphoreType.DMA((2,)),
        ],
        input_output_aliases={leading: 2} if accumulated else {},
        compiler_params=PARAMS,
    )(*flags, a, te, *flat, skip_in, grad_out, grad_skip, *accumulated)


def on_device(clean_latents, target_noise, timesteps, layer_counts, section_weights):
    section_count = lax.axis_size("section")
    half_count = section_count // 2
    section_index = lax.axis_index("section")
    micro_count, row_count, channels = clean_latents.shape
    rows = micro_count * row_count
    weights = section_weights[0]
    slot_count = weights.shape[0] // channels - 1
    step_values = timesteps[0]

    rep_count = lax.axis_size("rep")
    core_index = lax.axis_index("rep") % 2
    half_rows = weights.shape[0] // 2
    my_half = lax.dynamic_slice_in_dim(weights, core_index * half_rows, half_rows, 0)
    count_rows = jnp.broadcast_to(layer_counts[0].astype(BF16), (16, channels))
    block_rows = half_rows + 16

    def tiles_of(value):
        return value.reshape(block_rows // 16, 16, channels)

    def rows_of(value):
        return value.reshape(block_rows, channels)

    my_block = tiles_of(jnp.concatenate([my_half, count_rows]))
    chip_swap = [(i, i ^ 1) for i in range(rep_count)]
    shift_pairs = [
        [(i, (i + shift) % section_count) for i in range(section_count)]
        for shift in range(1, section_count)
    ]
    counts_by_shift = [layer_counts] + [
        lax.ppermute(layer_counts, "section", pairs) for pairs in shift_pairs
    ]
    fetched = []
    for pairs in shift_pairs:
        mine = lax.ppermute(my_block, "section", pairs)
        sibling = lax.ppermute(mine, "rep", chip_swap)
        fetched.append((rows_of(mine), rows_of(sibling)))
    table = counts_by_shift + [
        section_index.astype(jnp.int32).reshape(1),
        core_index.astype(jnp.int32).reshape(1),
    ]
    all_weights = (section_weights, fetched)

    signal_level = noise_level(step_values)[:, None, None]
    noisy_input = (
        jnp.sqrt(signal_level) * clean_latents.astype(jnp.float32)
        + jnp.sqrt(1.0 - signal_level) * target_noise.astype(jnp.float32)
    ).astype(BF16).reshape(rows, channels)
    target_rows = target_noise.reshape(rows, channels)
    time_embed = jnp.broadcast_to(
        time_features(step_values, channels)[:, None, :], (micro_count, row_count, channels)
    ).reshape(rows, channels)


    blank = jnp.zeros((rows, channels), BF16)
    current = noisy_input
    section_inputs = []
    skips = {}
    for stage in range(section_count):
        is_decoder = stage >= half_count
        section_inputs.append(current)
        skip_in = skips[section_count - 1 - stage] if is_decoder else blank
        current, skip_out = stage_forward(
            table, current, time_embed, all_weights, skip_in,
            is_decoder, slot_count, channels, stage,
        )
        if not is_decoder:
            skips[stage] = skip_out

    grad_current = (
        (current.astype(jnp.float32) - target_rows.astype(jnp.float32)) / rows
    ).astype(BF16)
    grad_skips = {}
    weight_grads = None
    for stage in reversed(range(section_count)):
        is_decoder = stage >= half_count
        skip_in = skips[section_count - 1 - stage] if is_decoder else blank
        grad_skip = blank if is_decoder else grad_skips[section_count - 1 - stage]
        grad_current, e_out, weight_grads = stage_backward(
            table, section_inputs[stage], time_embed, all_weights, skip_in,
            grad_current, grad_skip, weight_grads, is_decoder, slot_count, channels, stage,
        )
        if is_decoder:
            grad_skips[stage] = e_out

    return halving_scatter(weight_grads)[None]


def halving_scatter(grads):
    rep_count = lax.axis_size("rep")
    group_count = rep_count // 2
    channels = grads.shape[1]
    chunk = grads.shape[0] // rep_count
    ordered = (
        grads.reshape(group_count, 2, chunk, channels).transpose(1, 0, 2, 3).reshape(grads.shape)
    )
    rep_index = lax.axis_index("rep")
    core = rep_index % 2
    group = rep_index // 2
    half = grads.shape[0] // 2
    keep = lax.dynamic_slice_in_dim(ordered, core * half, half, 0)
    give = lax.dynamic_slice_in_dim(ordered, (1 - core) * half, half, 0)
    chip_swap = [(i, i ^ 1) for i in range(rep_count)]
    got = lax.ppermute(give.reshape(half // 8, 8, channels), "rep", chip_swap)
    current = keep + got.reshape(half, channels)
    total = lax.dynamic_slice_in_dim(current, group * chunk, chunk, 0)
    for shift in range(1, group_count):
        target = (group + shift) % group_count
        sent = lax.dynamic_slice_in_dim(current, target * chunk, chunk, 0)
        pairs = [
            (i, 2 * ((i // 2 + shift) % group_count) + i % 2) for i in range(rep_count)
        ]
        arrived = lax.ppermute(sent.reshape(chunk // 8, 8, channels), "rep", pairs)
        total = total + arrived.reshape(chunk, channels)
    return total


def solution(mesh):
    placed = (
        P(None, "rep", None),
        P(None, "rep", None),
        P("rep", None),
        P("section"),
        P("section", None, None),
    )
    return jax.shard_map(
        on_device, mesh=mesh, in_specs=placed, out_specs=P("section", "rep", None), check_vma=False
    )
```

```python
import functools
import math

import jax
import jax.numpy as jnp
from jax import lax
from jax.experimental import pallas as pl
from jax.experimental.pallas import tpu as pltpu
from jax.sharding import PartitionSpec as P

EPSILON = 1e-06
F32 = jnp.float32
BF16 = jnp.bfloat16


def noise_level(step_values):
    phase = (step_values.astype(jnp.float32) / 1000.0 + 0.008) / 1.008 * (math.pi / 2.0)
    return jnp.cos(phase) ** 2


def time_features(step_values, channels):
    half_width = channels // 2
    ladder = jnp.exp(-math.log(10000.0) * jnp.arange(half_width, dtype=jnp.float32) / half_width)
    angles = step_values.astype(jnp.float32)[..., None] * ladder
    return jnp.concatenate([jnp.sin(angles), jnp.cos(angles)], axis=-1)


def contract_rows(left, right):
    return lax.dot_general(left, right, (((0,), (0,)), ((), ())), preferred_element_type=F32)


def contract_cols(left, right):
    return lax.dot_general(left, right, (((1,), (1,)), ((), ())), preferred_element_type=F32)


def plain_product(left, right):
    return lax.dot_general(left, right, (((1,), (0,)), ((), ())), preferred_element_type=F32)


def sigmoid(value):
    return 1.0 / (1.0 + jnp.exp(-value))


def inverse_rms_of(hidden):
    return lax.rsqrt(jnp.mean(hidden * hidden, axis=-1, keepdims=True) + EPSILON)


def slot_rows(slot_index, channels):
    return pl.ds(pl.multiple_of(slot_index * channels, 16), channels)


def run_forward_slots(h_ref, te, w_ref, count, slot_count, channels, store_ref=None):
    def body(slot_index, carry):
        hidden = h_ref[...]
        if store_ref is not None:
            store_ref[slot_index] = hidden
        preact = hidden * inverse_rms_of(hidden) + te
        activated = (preact * sigmoid(preact)).astype(BF16)
        weight = w_ref[slot_rows(slot_index, channels), :]
        h_ref[...] = hidden + plain_product(activated, weight)
        return carry

    lax.fori_loop(0, count, body, 0)


def load_weights(own_hbm, fetched, w_ref, sems, core, shift):
    half_rows = w_ref.shape[0] // 2
    mine_at = pl.multiple_of(core * half_rows, 16)
    sibling_at = pl.multiple_of((1 - core) * half_rows, 16)

    @pl.when(shift == 0)
    def _():
        copy = pltpu.make_async_copy(own_hbm.at[0], w_ref, sems.at[0])
        copy.start()
        copy.wait()

    for index, (mine_hbm, sibling_hbm) in enumerate(fetched):

        @pl.when(shift == index + 1)
        def _():
            copies = [
                pltpu.make_async_copy(
                    mine_hbm.at[pl.ds(0, half_rows)], w_ref.at[pl.ds(mine_at, half_rows)],
                    sems.at[0],
                ),
                pltpu.make_async_copy(
                    sibling_hbm.at[pl.ds(0, half_rows)], w_ref.at[pl.ds(sibling_at, half_rows)],
                    sems.at[1],
                ),
            ]
            for copy in copies:
                copy.start()
            for copy in copies:
                copy.wait()


def split_weight_refs(refs, fetched_count):
    own_hbm = refs[0]
    fetched = [
        (refs[1 + 2 * index], refs[2 + 2 * index]) for index in range(fetched_count)
    ]
    return own_hbm, fetched, refs[1 + 2 * fetched_count :]


def read_table(table_refs, stage, section_count):
    section_index = table_refs[section_count][0]
    shift = lax.rem(section_index - stage + section_count, section_count)
    count = table_refs[0][0]
    for index in range(1, section_count):
        count = jnp.where(shift == index, table_refs[index][0], count)
    return count, section_index == stage, table_refs[section_count + 1][0], shift


def forward_kernel(*refs, decoder, slot_count, channels, fetched_count, stage):
    table_refs = refs[: fetched_count + 3]
    a_ref, te_ref = refs[fetched_count + 3 : fetched_count + 5]
    own_hbm, fetched, refs = split_weight_refs(refs[fetched_count + 5 :], fetched_count)
    skip_ref, out_ref, skip_out_ref, h_ref, w_ref, w_sems = refs
    count, unused_owned, core, shift = read_table(table_refs, stage, fetched_count + 1)
    load_weights(own_hbm, fetched, w_ref, w_sems, core, shift)
    side = w_ref[slot_count * channels :, :]
    hidden = a_ref[...].astype(F32)
    if decoder:
        hidden = hidden + plain_product(skip_ref[...], side)
    h_ref[...] = hidden
    run_forward_slots(h_ref, te_ref[...], w_ref, count, slot_count, channels)
    section_out = h_ref[...].astype(BF16)
    out_ref[...] = section_out
    if not decoder:
        skip_out_ref[...] = plain_product(section_out, side).astype(BF16)


def backward_kernel(
    *refs, decoder, slot_count, channels, fetched_count, stage, accumulate, block_order
):
    table_refs = refs[: fetched_count + 3]
    a_ref, te_ref = refs[fetched_count + 3 : fetched_count + 5]
    own_hbm, fetched, refs = split_weight_refs(refs[fetched_count + 5 :], fetched_count)
    if not accumulate:
        refs = refs[:3] + (None,) + refs[3:]
    (skip_ref, g_ref, e_ref, grads_acc_ref, gprev_ref, e_out_ref, grads_out_ref,
     h_ref, hs_ref, gh_ref, grads_scr, sem, w_ref, w_sems) = refs
    count, owned, core, shift = read_table(table_refs, stage, fetched_count + 1)
    load_weights(own_hbm, fetched, w_ref, w_sems, core, shift)
    side = w_ref[slot_count * channels :, :]
    te = te_ref[...]
    hidden = a_ref[...].astype(F32)
    if decoder:
        hidden = hidden + plain_product(skip_ref[...], side)
    h_ref[...] = hidden
    run_forward_slots(h_ref, te, w_ref, count, slot_count, channels, store_ref=hs_ref)
    grad_hidden = g_ref[...].astype(F32)
    if not decoder:
        grad_skip = e_ref[...]
        grad_hidden = grad_hidden + contract_cols(grad_skip, side)
        section_out = h_ref[...].astype(BF16)
        grads_scr[slot_count * channels :, :] = contract_rows(section_out, grad_skip)

    gh_ref[...] = grad_hidden

    def back_body(step, carry):
        slot_index = count - 1 - step
        rows = slot_rows(slot_index, channels)
        hidden = hs_ref[slot_index]
        inverse_rms = inverse_rms_of(hidden)
        normed = hidden * inverse_rms
        preact = normed + te
        sigmoid_val = sigmoid(preact)
        grad_hidden = gh_ref[...]
        grad_low = grad_hidden.astype(BF16)
        activated = (preact * sigmoid_val).astype(BF16)
        grads_scr[rows, :] = contract_rows(activated, grad_low)
        grad_act = contract_cols(grad_low, w_ref[rows, :])
        grad_pre = grad_act * sigmoid_val * (1.0 + preact * (1.0 - sigmoid_val))
        gh_ref[...] = grad_hidden + inverse_rms * (
            grad_pre - normed * jnp.mean(grad_pre * normed, axis=-1, keepdims=True)
        )
        return carry

    lax.fori_loop(0, count, back_body, 0)

    def zero_body(slot_index, carry):
        grads_scr[slot_rows(slot_index, channels), :] = jnp.zeros((channels, channels), F32)
        return carry

    lax.fori_loop(count, slot_count, zero_body, 0)

    grad_low = gh_ref[...].astype(BF16)
    gprev_ref[...] = grad_low
    if decoder:
        e_out_ref[...] = contract_cols(grad_low, side).astype(BF16)
        grads_scr[slot_count * channels :, :] = contract_rows(skip_ref[...], grad_low)

    @pl.when(owned)
    def _():
        if block_order is None:
            copies = [pltpu.make_async_copy(grads_scr, grads_out_ref, sem.at[0])]
        else:
            copies = [
                pltpu.make_async_copy(
                    grads_scr.at[pl.ds(source * channels, channels)],
                    grads_out_ref.at[pl.ds(target * channels, channels)],
                    sem.at[source],
                )
                for source, target in enumerate(block_order)
            ]
        for copy in copies:
            copy.start()
        for copy in copies:
            copy.wait()


PARAMS = pltpu.CompilerParams(vmem_limit_bytes=48 * 1024 * 1024)


VMEM_SPEC = pl.BlockSpec(memory_space=pltpu.VMEM)
SMEM_SPEC = pl.BlockSpec(memory_space=pltpu.SMEM)
ANY_SPEC = pl.BlockSpec(memory_space=pl.ANY)


def weight_operands(weights):
    own, fetched = weights
    flat = [own]
    for pair in fetched:
        flat.extend(pair)
    return flat, len(fetched)


def stage_forward(flags, a, te, weights, skip_in, decoder, slot_count, channels, stage):
    rows = a.shape[0]
    flat, fetched_count = weight_operands(weights)
    kernel = functools.partial(
        forward_kernel, decoder=decoder, slot_count=slot_count, channels=channels,
        fetched_count=fetched_count, stage=stage,
    )
    return pl.pallas_call(
        kernel,
        out_shape=(
            jax.ShapeDtypeStruct((rows, channels), BF16),
            jax.ShapeDtypeStruct((rows, channels), BF16),
        ),
        in_specs=[SMEM_SPEC] * len(flags) + [VMEM_SPEC, VMEM_SPEC] + [ANY_SPEC] * len(flat)
        + [VMEM_SPEC],
        out_specs=(VMEM_SPEC, VMEM_SPEC),
        scratch_shapes=[
            pltpu.VMEM((rows, channels), F32),
            pltpu.VMEM(((slot_count + 1) * channels, channels), BF16),
            pltpu.SemaphoreType.DMA((2,)),
        ],
        compiler_params=PARAMS,
    )(*flags, a, te, *flat, skip_in)


def stage_backward(
    flags, a, te, weights, skip_in, grad_out, grad_skip, grads_acc, decoder,
    slot_count, channels, stage, block_order
):
    rows = a.shape[0]
    flat, fetched_count = weight_operands(weights)
    kernel = functools.partial(
        backward_kernel, decoder=decoder, slot_count=slot_count, channels=channels,
        fetched_count=fetched_count, stage=stage, accumulate=grads_acc is not None,
        block_order=block_order,
    )
    grads_shape = ((slot_count + 1) * channels, channels)
    accumulated = [] if grads_acc is None else [grads_acc]
    leading = len(flags) + 2 + len(flat) + 3
    return pl.pallas_call(
        kernel,
        out_shape=(
            jax.ShapeDtypeStruct((rows, channels), BF16),
            jax.ShapeDtypeStruct((rows, channels), BF16),
            jax.ShapeDtypeStruct(grads_shape, F32),
        ),
        in_specs=[SMEM_SPEC] * len(flags) + [VMEM_SPEC, VMEM_SPEC] + [ANY_SPEC] * len(flat)
        + [VMEM_SPEC] * 3 + [ANY_SPEC] * len(accumulated),
        out_specs=(VMEM_SPEC, VMEM_SPEC, ANY_SPEC),
        scratch_shapes=[
            pltpu.VMEM((rows, channels), F32),
            pltpu.VMEM((slot_count, rows, channels), F32),
            pltpu.VMEM((rows, channels), F32),
            pltpu.VMEM(grads_shape, F32),
            pltpu.SemaphoreType.DMA((slot_count + 1,)),
            pltpu.VMEM(((slot_count + 1) * channels, channels), BF16),
            pltpu.SemaphoreType.DMA((2,)),
        ],
        input_output_aliases={leading: 2} if accumulated else {},
        compiler_params=PARAMS,
    )(*flags, a, te, *flat, skip_in, grad_out, grad_skip, *accumulated)


def on_device(clean_latents, target_noise, timesteps, layer_counts, section_weights):
    section_count = lax.axis_size("section")
    half_count = section_count // 2
    section_index = lax.axis_index("section")
    micro_count, row_count, channels = clean_latents.shape
    rows = micro_count * row_count
    weights = section_weights[0]
    slot_count = weights.shape[0] // channels - 1
    step_values = timesteps[0]

    rep_count = lax.axis_size("rep")
    core_index = lax.axis_index("rep") % 2
    half_rows = weights.shape[0] // 2
    my_half = lax.dynamic_slice_in_dim(weights, core_index * half_rows, half_rows, 0)
    count_rows = jnp.broadcast_to(layer_counts[0].astype(BF16), (16, channels))
    block_rows = half_rows + 16

    def tiles_of(value):
        return value.reshape(block_rows // 16, 16, channels)

    def rows_of(value):
        return value.reshape(block_rows, channels)

    my_block = tiles_of(jnp.concatenate([my_half, count_rows]))
    chip_swap = [(i, i ^ 1) for i in range(rep_count)]
    shift_pairs = [
        [(i, (i + shift) % section_count) for i in range(section_count)]
        for shift in range(1, section_count)
    ]
    counts_by_shift = [layer_counts] + [
        lax.ppermute(layer_counts, "section", pairs) for pairs in shift_pairs
    ]
    fetched = []
    for pairs in shift_pairs:
        mine = lax.ppermute(my_block, "section", pairs)
        sibling = lax.ppermute(mine, "rep", chip_swap)
        fetched.append((rows_of(mine), rows_of(sibling)))
    table = counts_by_shift + [
        section_index.astype(jnp.int32).reshape(1),
        core_index.astype(jnp.int32).reshape(1),
    ]
    all_weights = (section_weights, fetched)

    signal_level = noise_level(step_values)[:, None, None]
    noisy_input = (
        jnp.sqrt(signal_level) * clean_latents.astype(jnp.float32)
        + jnp.sqrt(1.0 - signal_level) * target_noise.astype(jnp.float32)
    ).astype(BF16).reshape(rows, channels)
    target_rows = target_noise.reshape(rows, channels)
    time_embed = jnp.broadcast_to(
        time_features(step_values, channels)[:, None, :], (micro_count, row_count, channels)
    ).reshape(rows, channels)


    blank = jnp.zeros((rows, channels), BF16)
    current = noisy_input
    section_inputs = []
    skips = {}
    for stage in range(section_count):
        is_decoder = stage >= half_count
        section_inputs.append(current)
        skip_in = skips[section_count - 1 - stage] if is_decoder else blank
        current, skip_out = stage_forward(
            table, current, time_embed, all_weights, skip_in,
            is_decoder, slot_count, channels, stage,
        )
        if not is_decoder:
            skips[stage] = skip_out

    grad_current = (
        (current.astype(jnp.float32) - target_rows.astype(jnp.float32)) / rows
    ).astype(BF16)
    grad_skips = {}
    weight_grads = None
    rep_count = lax.axis_size("rep")
    block_order = None
    if rep_count == slot_count + 1 and rep_count % 2 == 0:
        block_order = tuple((j % 2) * (rep_count // 2) + j // 2 for j in range(rep_count))
    for stage in reversed(range(section_count)):
        is_decoder = stage >= half_count
        skip_in = skips[section_count - 1 - stage] if is_decoder else blank
        grad_skip = blank if is_decoder else grad_skips[section_count - 1 - stage]
        grad_current, e_out, weight_grads = stage_backward(
            table, section_inputs[stage], time_embed, all_weights, skip_in,
            grad_current, grad_skip, weight_grads, is_decoder, slot_count, channels, stage,
            block_order,
        )
        if is_decoder:
            grad_skips[stage] = e_out

    return halving_scatter(weight_grads, block_order is not None)[None]


def halving_scatter(grads, pre_ordered):
    rep_count = lax.axis_size("rep")
    group_count = rep_count // 2
    channels = grads.shape[1]
    chunk = grads.shape[0] // rep_count
    ordered = grads
    if not pre_ordered:
        ordered = (
            grads.reshape(group_count, 2, chunk, channels)
            .transpose(1, 0, 2, 3)
            .reshape(grads.shape)
        )
    rep_index = lax.axis_index("rep")
    core = rep_index % 2
    group = rep_index // 2
    half = grads.shape[0] // 2
    keep = lax.dynamic_slice_in_dim(ordered, core * half, half, 0)
    give = lax.dynamic_slice_in_dim(ordered, (1 - core) * half, half, 0)
    chip_swap = [(i, i ^ 1) for i in range(rep_count)]
    got = lax.ppermute(give.reshape(half // 8, 8, channels), "rep", chip_swap)
    current = keep + got.reshape(half, channels)
    total = lax.dynamic_slice_in_dim(current, group * chunk, chunk, 0)
    for shift in range(1, group_count):
        target = (group + shift) % group_count
        sent = lax.dynamic_slice_in_dim(current, target * chunk, chunk, 0)
        pairs = [
            (i, 2 * ((i // 2 + shift) % group_count) + i % 2) for i in range(rep_count)
        ]
        arrived = lax.ppermute(sent.reshape(chunk // 8, 8, channels), "rep", pairs)
        total = total + arrived.reshape(chunk, channels)
    return total


def solution(mesh):
    placed = (
        P(None, "rep", None),
        P(None, "rep", None),
        P("rep", None),
        P("section"),
        P("section", None, None),
    )
    return jax.shard_map(
        on_device, mesh=mesh, in_specs=placed, out_specs=P("section", "rep", None), check_vma=False
    )
```

```python
import functools
import math

import jax
import jax.numpy as jnp
from jax import lax
from jax.experimental import pallas as pl
from jax.experimental.pallas import tpu as pltpu
from jax.sharding import PartitionSpec as P

EPSILON = 1e-06
F32 = jnp.float32
BF16 = jnp.bfloat16


def noise_level(step_values):
    phase = (step_values.astype(jnp.float32) / 1000.0 + 0.008) / 1.008 * (math.pi / 2.0)
    return jnp.cos(phase) ** 2


def time_features(step_values, channels):
    half_width = channels // 2
    ladder = jnp.exp(-math.log(10000.0) * jnp.arange(half_width, dtype=jnp.float32) / half_width)
    angles = step_values.astype(jnp.float32)[..., None] * ladder
    return jnp.concatenate([jnp.sin(angles), jnp.cos(angles)], axis=-1)


def contract_rows(left, right):
    return lax.dot_general(left, right, (((0,), (0,)), ((), ())), preferred_element_type=F32)


def contract_cols(left, right):
    return lax.dot_general(left, right, (((1,), (1,)), ((), ())), preferred_element_type=F32)


def plain_product(left, right):
    return lax.dot_general(left, right, (((1,), (0,)), ((), ())), preferred_element_type=F32)


def sigmoid(value):
    return 1.0 / (1.0 + jnp.exp(-value))


def inverse_rms_of(hidden):
    return lax.rsqrt(jnp.mean(hidden * hidden, axis=-1, keepdims=True) + EPSILON)


def slot_rows(slot_index, channels):
    return pl.ds(pl.multiple_of(slot_index * channels, 16), channels)


def run_forward_slots(h_ref, te, w_ref, count, slot_count, channels, store_ref=None):
    def body(slot_index, carry):
        hidden = h_ref[...]
        if store_ref is not None:
            store_ref[slot_index] = hidden
        preact = hidden * inverse_rms_of(hidden) + te
        activated = (preact * sigmoid(preact)).astype(BF16)
        weight = w_ref[slot_rows(slot_index, channels), :]
        h_ref[...] = hidden + plain_product(activated, weight)
        return carry

    lax.fori_loop(0, count, body, 0)


def load_weights(own_hbm, fetched, w_ref, sems, core, shift):
    half_rows = w_ref.shape[0] // 2
    mine_at = pl.multiple_of(core * half_rows, 16)
    sibling_at = pl.multiple_of((1 - core) * half_rows, 16)

    @pl.when(shift == 0)
    def _():
        copy = pltpu.make_async_copy(own_hbm.at[0], w_ref, sems.at[0])
        copy.start()
        copy.wait()

    for index, (mine_hbm, sibling_hbm) in enumerate(fetched):

        @pl.when(shift == index + 1)
        def _():
            copies = [
                pltpu.make_async_copy(
                    mine_hbm.at[pl.ds(0, half_rows)], w_ref.at[pl.ds(mine_at, half_rows)],
                    sems.at[0],
                ),
                pltpu.make_async_copy(
                    sibling_hbm.at[pl.ds(0, half_rows)], w_ref.at[pl.ds(sibling_at, half_rows)],
                    sems.at[1],
                ),
            ]
            for copy in copies:
                copy.start()
            for copy in copies:
                copy.wait()


def split_weight_refs(refs, fetched_count):
    own_hbm = refs[0]
    fetched = [
        (refs[1 + 2 * index], refs[2 + 2 * index]) for index in range(fetched_count)
    ]
    return own_hbm, fetched, refs[1 + 2 * fetched_count :]


def read_table(table_refs, stage, section_count):
    section_index = table_refs[section_count][0]
    shift = lax.rem(section_index - stage + section_count, section_count)
    count = table_refs[0][0]
    for index in range(1, section_count):
        count = jnp.where(shift == index, table_refs[index][0], count)
    return count, section_index == stage, table_refs[section_count + 1][0], shift


def forward_kernel(*refs, decoder, slot_count, channels, fetched_count, stage):
    table_refs = refs[: fetched_count + 3]
    a_ref, te_ref = refs[fetched_count + 3 : fetched_count + 5]
    own_hbm, fetched, refs = split_weight_refs(refs[fetched_count + 5 :], fetched_count)
    skip_ref, out_ref, skip_out_ref, h_ref, w_ref, w_sems = refs
    count, unused_owned, core, shift = read_table(table_refs, stage, fetched_count + 1)
    load_weights(own_hbm, fetched, w_ref, w_sems, core, shift)
    side = w_ref[slot_count * channels :, :]
    hidden = a_ref[...].astype(F32)
    if decoder:
        hidden = hidden + plain_product(skip_ref[...], side)
    h_ref[...] = hidden
    run_forward_slots(h_ref, te_ref[...], w_ref, count, slot_count, channels)
    section_out = h_ref[...].astype(BF16)
    out_ref[...] = section_out
    if not decoder:
        skip_out_ref[...] = plain_product(section_out, side).astype(BF16)


def backward_kernel(*refs, decoder, slot_count, channels, fetched_count, stage, accumulate):
    table_refs = refs[: fetched_count + 3]
    a_ref, te_ref = refs[fetched_count + 3 : fetched_count + 5]
    own_hbm, fetched, refs = split_weight_refs(refs[fetched_count + 5 :], fetched_count)
    if not accumulate:
        refs = refs[:3] + (None,) + refs[3:]
    (skip_ref, g_ref, e_ref, grads_acc_ref, gprev_ref, e_out_ref, grads_out_ref,
     h_ref, hs_ref, gh_ref, grads_scr, sem, w_ref, w_sems) = refs
    count, owned, core, shift = read_table(table_refs, stage, fetched_count + 1)
    load_weights(own_hbm, fetched, w_ref, w_sems, core, shift)
    side = w_ref[slot_count * channels :, :]
    te = te_ref[...]
    hidden = a_ref[...].astype(F32)
    if decoder:
        hidden = hidden + plain_product(skip_ref[...], side)
    h_ref[...] = hidden
    run_forward_slots(h_ref, te, w_ref, count, slot_count, channels, store_ref=hs_ref)
    grad_hidden = g_ref[...].astype(F32)
    if not decoder:
        grad_skip = e_ref[...]
        grad_hidden = grad_hidden + contract_cols(grad_skip, side)
        section_out = h_ref[...].astype(BF16)
        grads_scr[slot_count * channels :, :] = contract_rows(section_out, grad_skip)

    gh_ref[...] = grad_hidden

    def back_body(step, carry):
        slot_index = count - 1 - step
        rows = slot_rows(slot_index, channels)
        hidden = hs_ref[slot_index]
        inverse_rms = inverse_rms_of(hidden)
        normed = hidden * inverse_rms
        preact = normed + te
        sigmoid_val = sigmoid(preact)
        grad_hidden = gh_ref[...]
        grad_low = grad_hidden.astype(BF16)
        activated = (preact * sigmoid_val).astype(BF16)
        grads_scr[rows, :] = contract_rows(activated, grad_low)
        grad_act = contract_cols(grad_low, w_ref[rows, :])
        grad_pre = grad_act * sigmoid_val * (1.0 + preact * (1.0 - sigmoid_val))
        gh_ref[...] = grad_hidden + inverse_rms * (
            grad_pre - normed * jnp.mean(grad_pre * normed, axis=-1, keepdims=True)
        )
        return carry

    lax.fori_loop(0, count, back_body, 0)

    def zero_body(slot_index, carry):
        grads_scr[slot_rows(slot_index, channels), :] = jnp.zeros((channels, channels), F32)
        return carry

    lax.fori_loop(count, slot_count, zero_body, 0)

    grad_low = gh_ref[...].astype(BF16)
    gprev_ref[...] = grad_low
    if decoder:
        e_out_ref[...] = contract_cols(grad_low, side).astype(BF16)
        grads_scr[slot_count * channels :, :] = contract_rows(skip_ref[...], grad_low)

    @pl.when(owned)
    def _():
        grads_copy = pltpu.make_async_copy(grads_scr, grads_out_ref, sem)
        grads_copy.start()
        grads_copy.wait()


PARAMS = pltpu.CompilerParams(vmem_limit_bytes=48 * 1024 * 1024)


VMEM_SPEC = pl.BlockSpec(memory_space=pltpu.VMEM)
SMEM_SPEC = pl.BlockSpec(memory_space=pltpu.SMEM)
ANY_SPEC = pl.BlockSpec(memory_space=pl.ANY)


def weight_operands(weights):
    own, fetched = weights
    flat = [own]
    for pair in fetched:
        flat.extend(pair)
    return flat, len(fetched)


def stage_forward(flags, a, te, weights, skip_in, decoder, slot_count, channels, stage):
    rows = a.shape[0]
    flat, fetched_count = weight_operands(weights)
    kernel = functools.partial(
        forward_kernel, decoder=decoder, slot_count=slot_count, channels=channels,
        fetched_count=fetched_count, stage=stage,
    )
    return pl.pallas_call(
        kernel,
        out_shape=(
            jax.ShapeDtypeStruct((rows, channels), BF16),
            jax.ShapeDtypeStruct((rows, channels), BF16),
        ),
        in_specs=[SMEM_SPEC] * len(flags) + [VMEM_SPEC, VMEM_SPEC] + [ANY_SPEC] * len(flat)
        + [VMEM_SPEC],
        out_specs=(VMEM_SPEC, VMEM_SPEC),
        scratch_shapes=[
            pltpu.VMEM((rows, channels), F32),
            pltpu.VMEM(((slot_count + 1) * channels, channels), BF16),
            pltpu.SemaphoreType.DMA((2,)),
        ],
        compiler_params=PARAMS,
    )(*flags, a, te, *flat, skip_in)


def stage_backward(
    flags, a, te, weights, skip_in, grad_out, grad_skip, grads_acc, decoder,
    slot_count, channels, stage
):
    rows = a.shape[0]
    flat, fetched_count = weight_operands(weights)
    kernel = functools.partial(
        backward_kernel, decoder=decoder, slot_count=slot_count, channels=channels,
        fetched_count=fetched_count, stage=stage, accumulate=grads_acc is not None,
    )
    grads_shape = ((slot_count + 1) * channels, channels)
    accumulated = [] if grads_acc is None else [grads_acc]
    leading = len(flags) + 2 + len(flat) + 3
    return pl.pallas_call(
        kernel,
        out_shape=(
            jax.ShapeDtypeStruct((rows, channels), BF16),
            jax.ShapeDtypeStruct((rows, channels), BF16),
            jax.ShapeDtypeStruct(grads_shape, F32),
        ),
        in_specs=[SMEM_SPEC] * len(flags) + [VMEM_SPEC, VMEM_SPEC] + [ANY_SPEC] * len(flat)
        + [VMEM_SPEC] * 3 + [ANY_SPEC] * len(accumulated),
        out_specs=(VMEM_SPEC, VMEM_SPEC, ANY_SPEC),
        scratch_shapes=[
            pltpu.VMEM((rows, channels), F32),
            pltpu.VMEM((slot_count, rows, channels), F32),
            pltpu.VMEM((rows, channels), F32),
            pltpu.VMEM(grads_shape, F32),
            pltpu.SemaphoreType.DMA(()),
            pltpu.VMEM(((slot_count + 1) * channels, channels), BF16),
            pltpu.SemaphoreType.DMA((2,)),
        ],
        input_output_aliases={leading: 2} if accumulated else {},
        compiler_params=PARAMS,
    )(*flags, a, te, *flat, skip_in, grad_out, grad_skip, *accumulated)


def on_device(clean_latents, target_noise, timesteps, layer_counts, section_weights):
    section_count = lax.axis_size("section")
    half_count = section_count // 2
    section_index = lax.axis_index("section")
    micro_count, row_count, channels = clean_latents.shape
    rows = micro_count * row_count
    weights = section_weights[0]
    slot_count = weights.shape[0] // channels - 1
    step_values = timesteps[0]

    rep_count = lax.axis_size("rep")
    core_index = lax.axis_index("rep") % 2
    half_rows = weights.shape[0] // 2
    my_half = lax.dynamic_slice_in_dim(weights, core_index * half_rows, half_rows, 0)
    count_rows = jnp.broadcast_to(layer_counts[0].astype(BF16), (16, channels))
    block_rows = half_rows + 16

    def tiles_of(value):
        return value.reshape(block_rows // 16, 16, channels)

    def rows_of(value):
        return value.reshape(block_rows, channels)

    my_block = tiles_of(jnp.concatenate([my_half, count_rows]))
    chip_swap = [(i, i ^ 1) for i in range(rep_count)]
    shift_pairs = [
        [(i, (i + shift) % section_count) for i in range(section_count)]
        for shift in range(1, section_count)
    ]
    counts_by_shift = [layer_counts] + [
        lax.ppermute(layer_counts, "section", pairs) for pairs in shift_pairs
    ]
    fetched = []
    for pairs in shift_pairs:
        mine = lax.ppermute(my_block, "section", pairs)
        sibling = lax.ppermute(mine, "rep", chip_swap)
        fetched.append((rows_of(mine), rows_of(sibling)))
    table = counts_by_shift + [
        section_index.astype(jnp.int32).reshape(1),
        core_index.astype(jnp.int32).reshape(1),
    ]
    all_weights = (section_weights, fetched)

    signal_level = noise_level(step_values)[:, None, None]
    noisy_input = (
        jnp.sqrt(signal_level) * clean_latents.astype(jnp.float32)
        + jnp.sqrt(1.0 - signal_level) * target_noise.astype(jnp.float32)
    ).astype(BF16).reshape(rows, channels)
    target_rows = target_noise.reshape(rows, channels)
    time_embed = jnp.broadcast_to(
        time_features(step_values, channels)[:, None, :], (micro_count, row_count, channels)
    ).reshape(rows, channels)


    blank = jnp.zeros((rows, channels), BF16)
    current = noisy_input
    section_inputs = []
    skips = {}
    for stage in range(section_count):
        is_decoder = stage >= half_count
        section_inputs.append(current)
        skip_in = skips[section_count - 1 - stage] if is_decoder else blank
        current, skip_out = stage_forward(
            table, current, time_embed, all_weights, skip_in,
            is_decoder, slot_count, channels, stage,
        )
        if not is_decoder:
            skips[stage] = skip_out

    grad_current = (
        (current.astype(jnp.float32) - target_rows.astype(jnp.float32)) / rows
    ).astype(BF16)
    grad_skips = {}
    weight_grads = None
    for stage in reversed(range(section_count)):
        is_decoder = stage >= half_count
        skip_in = skips[section_count - 1 - stage] if is_decoder else blank
        grad_skip = blank if is_decoder else grad_skips[section_count - 1 - stage]
        grad_current, e_out, weight_grads = stage_backward(
            table, section_inputs[stage], time_embed, all_weights, skip_in,
            grad_current, grad_skip, weight_grads, is_decoder, slot_count, channels, stage,
        )
        if is_decoder:
            grad_skips[stage] = e_out

    return halving_scatter(weight_grads)[None]


def halving_scatter(grads):
    rep_count = lax.axis_size("rep")
    channels = grads.shape[1]
    chunk = grads.shape[0] // rep_count
    rep_index = lax.axis_index("rep")
    total = lax.dynamic_slice_in_dim(grads, rep_index * chunk, chunk, 0)
    for shift in range(1, rep_count):
        target = (rep_index + shift) % rep_count
        sent = lax.dynamic_slice_in_dim(grads, target * chunk, chunk, 0)
        pairs = [(i, (i + shift) % rep_count) for i in range(rep_count)]
        arrived = lax.ppermute(sent.reshape(chunk // 8, 8, channels), "rep", pairs)
        total = total + arrived.reshape(chunk, channels)
    return total


def solution(mesh):
    placed = (
        P(None, "rep", None),
        P(None, "rep", None),
        P("rep", None),
        P("section"),
        P("section", None, None),
    )
    return jax.shard_map(
        on_device, mesh=mesh, in_specs=placed, out_specs=P("section", "rep", None), check_vma=False
    )
```
